32 devices in a mesh: groups: 2 (over x), seq: 8 (over z, y), rep: 2 (over core).
Axes of the slice: x: 2, y: 2, z: 4, core: 2. Of those that a mesh axis runs over, the one named last changes fastest.
Arguments:
- inputs: bfloat16 [4, 4096, 1536], P(('groups', 'rep'), 'seq'), parts along dimension 0, may hold values from -6 to 6
- lengths: int32 [4], P(('groups', 'rep')), parts along dimension 0, may hold values from 2049 to 4096, as said below
- conv_weight: bfloat16 [3, 48, 1536], replicated, may hold values from -0.5 to 0.5
- point_weight: bfloat16 [1536, 1536], replicated, may hold values from -0.15625 to 0.15625
- cotangent: bfloat16 [4, 4096, 1536], P(('groups', 'rep'), 'seq'), parts along dimension 0, may hold values from -6 to 6
Outputs:
- output: bfloat16 [4, 4096, 1536], P(('groups', 'rep'), 'seq'), parts along dimension 0
- grad_inputs: bfloat16 [4, 4096, 1536], P(('groups', 'rep'), 'seq'), parts along dimension 0
- grad_point: float32 [3072, 1536], P(('groups', 'seq', 'rep')), parts along dimension 0
- grad_conv: float32 [6, 48, 1536], P('groups'), parts along dimension 0
The draws below stay inside these ranges and needn't reach their ends.
There are 2 independent parts, one for each index of `groups`. The reference program is written for one: setup_inputs(seed, part) draws one part's arguments, and reference() takes and returns one part's arrays. A program takes and returns all parts, laid end to end along the dimension named above; an argument that names none is the same for every part. Nothing has to cross between parts.
Inputs may be any that keep to these rules, and one draw needn't show every extreme that they name: `lengths`: one sample in each draw has all 4096 bins valid.
All inputs are finite; a program needn't handle non-finite values.
Results may differ from the reference program's by a relative error of at most 0.0031.
Values may be sent and summed in bfloat16 or wider, within the bound.
No kernel may reach another device: no remote copies, remote signals or barrier semaphores. Data moves between devices by JAX's collectives and lax.ppermute only.
A program may use at most 128 MiB of HBM per device.

```python
import math
import jax
import jax.numpy as jnp

C = 1536
GROUP_CHANNELS = 48
DILATION_STEP = 64
BINS = 4096
SAMPLES = 2


def draw_lengths(key, part):
    key_cut, key_full = jax.random.split(jax.random.fold_in(key, 7))
    cut = jax.random.randint(key_cut, (SAMPLES,), 0, BINS // 2)
    full = jax.random.randint(key_full, (), 0, SAMPLES)
    return jnp.where(jnp.arange(SAMPLES) == full, BINS, BINS - cut).astype(jnp.int32)


def level_of(rng, dims, shards, smallest, top_value):
    factor_of = 1.0
    for dim, blocks in shards:
        steps = jax.random.uniform(jax.random.fold_in(jax.random.fold_in(rng, 6), dim), (blocks,), jnp.float32, smallest / len(shards), top_value / len(shards))
        factor_of = factor_of * jnp.repeat(jnp.exp(steps), dims[dim] // blocks).reshape((-1,) + (1,) * (len(dims) - 1 - dim))
    return factor_of


def gaussian(own_key, dims, scale, bound, cuts=(), held_as=jnp.bfloat16):
    gain = level_of(own_key, dims, cuts, -0.22, 0.18) if cuts else 1.0
    entries = jax.random.normal(own_key, dims, jnp.float32) * scale * gain
    return jnp.minimum(jnp.maximum(entries, -bound), bound).astype(held_as)


def setup_inputs(seed: int = 0, part: int = 0) -> dict:
    seeds = jax.random.split(jax.random.key(seed), 6)
    part_splits = jax.random.split(jax.random.fold_in(seeds[5], part), 6)
    return {
        "inputs": gaussian(part_splits[0], (SAMPLES, BINS, C), 1.0, 6.0, ((0, 2), (1, 8))),
        "lengths": draw_lengths(jax.random.fold_in(jax.random.fold_in(seeds[5], part), 71), part),
        "conv_weight": gaussian(seeds[2], (3, GROUP_CHANNELS, C), (3 * GROUP_CHANNELS) ** -0.5, 0.5),
        "point_weight": gaussian(seeds[3], (C, C), C ** -0.5, 0.15625),
        "cotangent": gaussian(part_splits[4], (SAMPLES, BINS, C), 1.0, 6.0, ((0, 2), (1, 8))),
    }


def gelu_pair(pre):
    cdf = 0.5 * (1.0 + jax.scipy.special.erf(pre * 0.7071067811865476))
    dens = jnp.exp(-0.5 * pre * pre) * 0.3989422804014327
    return (pre * cdf, cdf + pre * dens)

def conv_taps(padded_input, weight, sequence_length):
    group_count = weight.shape[2] // GROUP_CHANNELS
    total = jnp.zeros((padded_input.shape[0], sequence_length, group_count, GROUP_CHANNELS), jnp.float32)
    for kernel_offset in range(3):
        segment_window = padded_input[:, kernel_offset * DILATION_STEP:kernel_offset * DILATION_STEP + sequence_length].reshape(padded_input.shape[0], sequence_length, group_count, GROUP_CHANNELS).astype(jnp.float32)
        wk = weight[kernel_offset].reshape(GROUP_CHANNELS, group_count, GROUP_CHANNELS).astype(jnp.float32)
        total = total + jnp.einsum('slgi,igj->slgj', segment_window, wk)
    return total.reshape(padded_input.shape[0], sequence_length, group_count * GROUP_CHANNELS)

def transpose_taps(padded_input, weight, sequence_length):
    group_count = weight.shape[2] // GROUP_CHANNELS
    total = jnp.zeros((padded_input.shape[0], sequence_length, group_count, GROUP_CHANNELS), jnp.float32)
    for kernel_offset in range(3):
        segment_window = padded_input[:, (2 - kernel_offset) * DILATION_STEP:(2 - kernel_offset) * DILATION_STEP + sequence_length].reshape(padded_input.shape[0], sequence_length, group_count, GROUP_CHANNELS).astype(jnp.float32)
        wk = weight[kernel_offset].reshape(GROUP_CHANNELS, group_count, GROUP_CHANNELS).astype(jnp.float32)
        total = total + jnp.einsum('slgj,igj->slgi', segment_window, wk)
    return total.reshape(padded_input.shape[0], sequence_length, group_count * GROUP_CHANNELS)

def weight_taps(input_padded, output_gradient, sequence_length):
    group_count = output_gradient.shape[2] // GROUP_CHANNELS
    gr = output_gradient.reshape(output_gradient.shape[0], sequence_length, group_count, GROUP_CHANNELS).astype(jnp.float32)
    taps = []
    for kernel_offset in range(3):
        segment_window = input_padded[:, kernel_offset * DILATION_STEP:kernel_offset * DILATION_STEP + sequence_length].reshape(output_gradient.shape[0], sequence_length, group_count, GROUP_CHANNELS).astype(jnp.float32)
        taps.append(jnp.einsum('slgi,slgj->igj', segment_window, gr).reshape(GROUP_CHANNELS, group_count * GROUP_CHANNELS))
    return jnp.stack(taps)

def reference(inputs, lengths, conv_weight, point_weight, cotangent):
    samples, bins, chans = inputs.shape
    mask = (jnp.arange(bins, dtype=jnp.int32)[None, :] < lengths[:, None]).astype(jnp.float32)
    mask3 = mask[:, :, None]
    masked_input = (inputs.astype(jnp.float32) * mask3).astype(jnp.bfloat16)
    input_padded = jnp.pad(masked_input, ((0, 0), (DILATION_STEP, DILATION_STEP), (0, 0)))
    pre = conv_taps(input_padded, conv_weight, bins)
    act_val, slope = gelu_pair(pre)
    act = (act_val * mask3).astype(jnp.bfloat16)
    act2 = act.reshape(samples * bins, chans)
    cot2 = cotangent.reshape(samples * bins, chans)
    proj = jnp.dot(act2, point_weight, preferred_element_type=jnp.float32).reshape(samples, bins, chans)
    output = (inputs.astype(jnp.float32) + proj).astype(jnp.bfloat16)
    back = jnp.dot(cot2, point_weight.T, preferred_element_type=jnp.float32).reshape(samples, bins, chans)
    preactivation_gradient = (back * slope * mask3).astype(jnp.bfloat16)
    gradient_padded = jnp.pad(preactivation_gradient, ((0, 0), (DILATION_STEP, DILATION_STEP), (0, 0)))
    spread = transpose_taps(gradient_padded, conv_weight, bins)
    grad_inputs = (cotangent.astype(jnp.float32) + mask3 * spread).astype(jnp.bfloat16)
    scale = 1.0 / math.sqrt(samples * bins)
    grad_point = jnp.dot(act2.T, cot2, preferred_element_type=jnp.float32) * scale
    grad_conv = weight_taps(input_padded, preactivation_gradient, bins) * scale
    return (output, grad_inputs, grad_point, grad_conv)
```

```python
import math

import jax
import jax.numpy as jnp
from jax import lax
from jax.sharding import PartitionSpec as P

GROUP_CHANNELS = 48
DILATION_STEP = 64


def with_halo(cells, sides, width):
    for axis, dim in sides:
        count = lax.axis_size(axis)
        ends = count - 1
        head = lax.slice_in_dim(cells, 0, width, axis=dim)
        tail = lax.slice_in_dim(cells, cells.shape[dim] - width, cells.shape[dim], axis=dim)
        cells = jnp.concatenate(
            [
                lax.ppermute(tail, axis, [(i, (i + 1) % count) for i in range(ends)]),
                cells,
                lax.ppermute(head, axis, [((i + 1) % count, i) for i in range(ends)]),
            ],
            axis=dim,
        )
    return cells


def gelu_pair(pre):
    cdf = 0.5 * (1.0 + jax.scipy.special.erf(pre * 0.7071067811865476))
    dens = jnp.exp(-0.5 * pre * pre) * 0.3989422804014327
    return (pre * cdf, cdf + pre * dens)


def conv_taps(padded_input, weight, sequence_length):
    group_count = weight.shape[2] // GROUP_CHANNELS
    total = jnp.zeros(
        (padded_input.shape[0], sequence_length, group_count, GROUP_CHANNELS), jnp.float32
    )
    for kernel_offset in range(3):
        segment_window = padded_input[
            :, kernel_offset * DILATION_STEP : kernel_offset * DILATION_STEP + sequence_length
        ].reshape(padded_input.shape[0], sequence_length, group_count, GROUP_CHANNELS)
        wk = weight[kernel_offset].reshape(GROUP_CHANNELS, group_count, GROUP_CHANNELS)
        total = total + jnp.einsum(
            "slgi,igj->slgj", segment_window, wk, preferred_element_type=jnp.float32
        )
    return total.reshape(padded_input.shape[0], sequence_length, group_count * GROUP_CHANNELS)


def transpose_taps(padded_input, weight, sequence_length):
    group_count = weight.shape[2] // GROUP_CHANNELS
    total = jnp.zeros(
        (padded_input.shape[0], sequence_length, group_count, GROUP_CHANNELS), jnp.float32
    )
    for kernel_offset in range(3):
        segment_window = padded_input[
            :,
            (2 - kernel_offset) * DILATION_STEP : (2 - kernel_offset) * DILATION_STEP
            + sequence_length,
        ].reshape(padded_input.shape[0], sequence_length, group_count, GROUP_CHANNELS)
        wk = weight[kernel_offset].reshape(GROUP_CHANNELS, group_count, GROUP_CHANNELS)
        total = total + jnp.einsum(
            "slgj,igj->slgi", segment_window, wk, preferred_element_type=jnp.float32
        )
    return total.reshape(padded_input.shape[0], sequence_length, group_count * GROUP_CHANNELS)


def weight_taps(input_padded, output_gradient, sequence_length):
    group_count = output_gradient.shape[2] // GROUP_CHANNELS
    grouped = output_gradient.reshape(
        output_gradient.shape[0], sequence_length, group_count, GROUP_CHANNELS
    )
    taps = []
    for kernel_offset in range(3):
        segment_window = input_padded[
            :, kernel_offset * DILATION_STEP : kernel_offset * DILATION_STEP + sequence_length
        ].reshape(output_gradient.shape[0], sequence_length, group_count, GROUP_CHANNELS)
        taps.append(
            jnp.einsum(
                "slgi,slgj->igj", segment_window, grouped, preferred_element_type=jnp.float32
            ).reshape(GROUP_CHANNELS, group_count * GROUP_CHANNELS)
        )
    return jnp.stack(taps)


def swap(value, axis, distance):
    count = lax.axis_size(axis)
    return lax.ppermute(value, axis, [(i, i ^ distance) for i in range(count)])


def tree_sum(value):
    for axis in ("rep", "seq"):
        count = lax.axis_size(axis)
        if count & (count - 1):
            value = lax.psum(value, axis)
            continue
        distance = 1
        while distance < count:
            value = value + swap(value, axis, distance)
            distance *= 2
    return value


def point_gradient(act_rows, cot_rows, seq_count, rep_count):
    chans = act_rows.shape[1]
    block = chans // (seq_count * rep_count)
    blocks = act_rows.reshape(act_rows.shape[0], seq_count, rep_count, block)
    rep_index = lax.axis_index("rep")

    def rows_of(owner):
        cols = lax.dynamic_index_in_dim(blocks, owner, axis=2, keepdims=False)
        cols = cols.reshape(act_rows.shape[0], seq_count * block)
        return lax.dot_general(
            cols, cot_rows, (((0,), (0,)), ((), ())), preferred_element_type=jnp.float32
        )

    if rep_count == 2:
        mine = rows_of(rep_index) + swap(rows_of(1 - rep_index), "rep", 1)
    else:
        full = lax.dot_general(
            act_rows, cot_rows, (((0,), (0,)), ((), ())), preferred_element_type=jnp.float32
        ).reshape(seq_count, rep_count, block, chans)
        mine = lax.psum_scatter(full, "rep", scatter_dimension=1, tiled=True)
        mine = mine.reshape(seq_count * block, chans)
    return lax.psum_scatter(mine, "seq", scatter_dimension=0, tiled=True)

def on_device(inputs, lengths, conv_weight, point_weight, cotangent):
    local_bins = inputs.shape[1]
    chans = inputs.shape[2]
    seq_count = lax.axis_size("seq")
    rep_count = lax.axis_size("rep")
    seq_index = lax.axis_index("seq")
    positions = seq_index * local_bins + jnp.arange(local_bins, dtype=jnp.int32)
    mask = (positions[None, :] < lengths[:, None]).astype(jnp.float32)
    mask3 = mask[:, :, None]
    masked_input = (inputs.astype(jnp.float32) * mask3).astype(jnp.bfloat16)
    scale = 1.0 / math.sqrt(rep_count * seq_count * local_bins)
    padded_input = with_halo(masked_input, (("seq", 1),), DILATION_STEP)
    pre = conv_taps(padded_input, conv_weight, local_bins)
    act_val, slope = gelu_pair(pre)
    act = (act_val * mask3).astype(jnp.bfloat16)
    act_rows = act.reshape(local_bins, chans)
    cot_rows = cotangent.reshape(local_bins, chans)
    proj = jnp.dot(act_rows, point_weight, preferred_element_type=jnp.float32).reshape(inputs.shape)
    output = (inputs.astype(jnp.float32) + proj).astype(jnp.bfloat16)
    back = lax.dot_general(
        cot_rows, point_weight, (((1,), (1,)), ((), ())), preferred_element_type=jnp.float32
    )
    preactivation_gradient = (back.reshape(inputs.shape) * slope * mask3).astype(jnp.bfloat16)
    padded_gradient = with_halo(preactivation_gradient, (("seq", 1),), DILATION_STEP)
    spread = transpose_taps(padded_gradient, conv_weight, local_bins)
    conv_local = weight_taps(padded_input, preactivation_gradient, local_bins)
    grad_conv = tree_sum(conv_local) * scale
    grad_inputs = (cotangent.astype(jnp.float32) + mask3 * spread).astype(jnp.bfloat16)
    grad_point = point_gradient(act_rows, cot_rows, seq_count, rep_count) * scale
    return (output, grad_inputs, grad_point, grad_conv)


def solution(mesh):
    return jax.shard_map(
        on_device,
        mesh=mesh,
        in_specs=(
            P(("groups", "rep"), "seq", None),
            P(("groups", "rep")),
            P(),
            P(),
            P(("groups", "rep"), "seq", None),
        ),
        out_specs=(
            P(("groups", "rep"), "seq", None),
            P(("groups", "rep"), "seq", None),
            P(("groups", "seq", "rep"), None),
            P("groups", None, None),
        ),
        check_vma=False,
    )
```

```python
import math

import jax
import jax.numpy as jnp
from jax import lax
from jax.sharding import PartitionSpec as P

GROUP_CHANNELS = 48
DILATION_STEP = 64


def with_halo(cells, sides, width):
    for axis, dim in sides:
        count = lax.axis_size(axis)
        ends = count - 1
        head = lax.slice_in_dim(cells, 0, width, axis=dim)
        tail = lax.slice_in_dim(cells, cells.shape[dim] - width, cells.shape[dim], axis=dim)
        cells = jnp.concatenate(
            [
                lax.ppermute(tail, axis, [(i, (i + 1) % count) for i in range(ends)]),
                cells,
                lax.ppermute(head, axis, [((i + 1) % count, i) for i in range(ends)]),
            ],
            axis=dim,
        )
    return cells


def gelu_pair(pre):
    cdf = 0.5 * (1.0 + jax.scipy.special.erf(pre * 0.7071067811865476))
    dens = jnp.exp(-0.5 * pre * pre) * 0.3989422804014327
    return (pre * cdf, cdf + pre * dens)


CHUNK = 384


def dense_weight(weight):
    taps, width, chans = weight.shape
    chunks = chans // CHUNK
    groups = CHUNK // width
    cells = weight.reshape(taps, width, chunks, groups, width).transpose(0, 2, 1, 3, 4)
    eye = jnp.eye(groups, dtype=weight.dtype)
    dense = cells[:, :, None, :, :, :] * eye[None, None, :, None, :, None]
    return dense.reshape(taps, chunks, CHUNK, CHUNK)


def conv_taps(padded_input, dense, sequence_length, transpose=False):
    rows = padded_input[0]
    parts = []
    for c in range(dense.shape[1]):
        total = None
        for k in range(3):
            start = (2 - k if transpose else k) * DILATION_STEP
            window = rows[start : start + sequence_length, c * CHUNK : (c + 1) * CHUNK]
            dims = (((1,), (1,)), ((), ())) if transpose else (((1,), (0,)), ((), ()))
            term = lax.dot_general(window, dense[k, c], dims, preferred_element_type=jnp.float32)
            total = term if total is None else total + term
        parts.append(total)
    return jnp.concatenate(parts, axis=1)[None]


def weight_taps(input_padded, output_gradient, sequence_length):
    rows = input_padded[0]
    grads = output_gradient[0]
    chans = grads.shape[1]
    chunks = chans // CHUNK
    groups = CHUNK // GROUP_CHANNELS
    eye = jnp.eye(groups, dtype=jnp.float32)
    taps = []
    for k in range(3):
        window = rows[k * DILATION_STEP : k * DILATION_STEP + sequence_length].reshape(
            sequence_length, chunks, CHUNK
        )
        full = jnp.einsum(
            "tci,tcj->cij", window, grads.reshape(sequence_length, chunks, CHUNK),
            preferred_element_type=jnp.float32,
        ).reshape(chunks, groups, GROUP_CHANNELS, groups, GROUP_CHANNELS)
        diag = jnp.einsum("caibj,ab->icbj", full, eye)
        taps.append(diag.reshape(GROUP_CHANNELS, chans))
    return jnp.stack(taps)


def swap(value, axis, distance):
    count = lax.axis_size(axis)
    return lax.ppermute(value, axis, [(i, i ^ distance) for i in range(count)])


def tree_sum(value):
    for axis in ("rep", "seq"):
        count = lax.axis_size(axis)
        if count & (count - 1):
            value = lax.psum(value, axis)
            continue
        distance = 1
        while distance < count:
            value = value + swap(value, axis, distance)
            distance *= 2
    return value


def point_gradient(act_rows, cot_rows, seq_count, rep_count):
    chans = act_rows.shape[1]
    block = chans // (seq_count * rep_count)
    blocks = act_rows.reshape(act_rows.shape[0], seq_count, rep_count, block)
    rep_index = lax.axis_index("rep")

    def rows_of(owner):
        cols = lax.dynamic_index_in_dim(blocks, owner, axis=2, keepdims=False)
        cols = cols.reshape(act_rows.shape[0], seq_count * block)
        return lax.dot_general(
            cols, cot_rows, (((0,), (0,)), ((), ())), preferred_element_type=jnp.float32
        )

    if rep_count == 2:
        mine = rows_of(rep_index) + swap(rows_of(1 - rep_index), "rep", 1)
    else:
        full = lax.dot_general(
            act_rows, cot_rows, (((0,), (0,)), ((), ())), preferred_element_type=jnp.float32
        ).reshape(seq_count, rep_count, block, chans)
        mine = lax.psum_scatter(full, "rep", scatter_dimension=1, tiled=True)
        mine = mine.reshape(seq_count * block, chans)
    return lax.psum_scatter(mine, "seq", scatter_dimension=0, tiled=True)

def on_device(inputs, lengths, conv_weight, point_weight, cotangent):
    local_bins = inputs.shape[1]
    chans = inputs.shape[2]
    seq_count = lax.axis_size("seq")
    rep_count = lax.axis_size("rep")
    seq_index = lax.axis_index("seq")
    positions = seq_index * local_bins + jnp.arange(local_bins, dtype=jnp.int32)
    mask = (positions[None, :] < lengths[:, None]).astype(jnp.float32)
    mask3 = mask[:, :, None]
    masked_input = (inputs.astype(jnp.float32) * mask3).astype(jnp.bfloat16)
    scale = 1.0 / math.sqrt(rep_count * seq_count * local_bins)
    padded_input = with_halo(masked_input, (("seq", 1),), DILATION_STEP)
    dense = dense_weight(conv_weight)
    pre = conv_taps(padded_input, dense, local_bins)
    act_val, slope = gelu_pair(pre)
    act = (act_val * mask3).astype(jnp.bfloat16)
    act_rows = act.reshape(local_bins, chans)
    cot_rows = cotangent.reshape(local_bins, chans)
    proj = jnp.dot(act_rows, point_weight, preferred_element_type=jnp.float32).reshape(inputs.shape)
    output = (inputs.astype(jnp.float32) + proj).astype(jnp.bfloat16)
    back = lax.dot_general(
        cot_rows, point_weight, (((1,), (1,)), ((), ())), preferred_element_type=jnp.float32
    )
    preactivation_gradient = (back.reshape(inputs.shape) * slope * mask3).astype(jnp.bfloat16)
    padded_gradient = with_halo(preactivation_gradient, (("seq", 1),), DILATION_STEP)
    spread = conv_taps(padded_gradient, dense, local_bins, transpose=True)
    conv_local = weight_taps(padded_input, preactivation_gradient, local_bins)
    grad_conv = tree_sum(conv_local) * scale
    grad_inputs = (cotangent.astype(jnp.float32) + mask3 * spread).astype(jnp.bfloat16)
    grad_point = point_gradient(act_rows, cot_rows, seq_count, rep_count) * scale
    return (output, grad_inputs, grad_point, grad_conv)


def solution(mesh):
    return jax.shard_map(
        on_device,
        mesh=mesh,
        in_specs=(
            P(("groups", "rep"), "seq", None),
            P(("groups", "rep")),
            P(),
            P(),
            P(("groups", "rep"), "seq", None),
        ),
        out_specs=(
            P(("groups", "rep"), "seq", None),
            P(("groups", "rep"), "seq", None),
            P(("groups", "seq", "rep"), None),
            P("groups", None, None),
        ),
        check_vma=False,
    )
```

```python
import math

import jax
import jax.numpy as jnp
from jax import lax
from jax.sharding import PartitionSpec as P

GROUP_CHANNELS = 48
DILATION_STEP = 64


def with_halo(cells, sides, width):
    for axis, dim in sides:
        count = lax.axis_size(axis)
        ends = count - 1
        head = lax.slice_in_dim(cells, 0, width, axis=dim)
        tail = lax.slice_in_dim(cells, cells.shape[dim] - width, cells.shape[dim], axis=dim)
        cells = jnp.concatenate(
            [
                lax.ppermute(tail, axis, [(i, (i + 1) % count) for i in range(ends)]),
                cells,
                lax.ppermute(head, axis, [((i + 1) % count, i) for i in range(ends)]),
            ],
            axis=dim,
        )
    return cells


def gelu_pair(pre):
    cdf = 0.5 * (1.0 + jax.scipy.special.erf(pre * 0.7071067811865476))
    dens = jnp.exp(-0.5 * pre * pre) * 0.3989422804014327
    return (pre * cdf, cdf + pre * dens)


CHUNK = 384


def group_mask(rows, chans, dtype):
    row_group = lax.broadcasted_iota(jnp.int32, (rows, chans), 0) // GROUP_CHANNELS
    col_group = (lax.broadcasted_iota(jnp.int32, (rows, chans), 1) % CHUNK) // GROUP_CHANNELS
    return (row_group == col_group).astype(dtype)


def dense_weight(weight):
    taps, width, chans = weight.shape
    groups = CHUNK // width
    tiled = jnp.tile(weight, (1, groups, 1))
    return tiled * group_mask(CHUNK, chans, weight.dtype)[None]


def conv_taps(padded_input, dense, sequence_length, transpose=False):
    rows = padded_input[0]
    chunks = dense.shape[2] // CHUNK
    parts = []
    for c in range(chunks):
        cols = slice(c * CHUNK, (c + 1) * CHUNK)
        total = None
        for k in range(3):
            start = (2 - k if transpose else k) * DILATION_STEP
            window = rows[start : start + sequence_length, cols]
            dims = (((1,), (1,)), ((), ())) if transpose else (((1,), (0,)), ((), ()))
            term = lax.dot_general(
                window, dense[k, :, cols], dims, preferred_element_type=jnp.float32
            )
            total = term if total is None else total + term
        parts.append(total)
    return jnp.concatenate(parts, axis=1)[None]


def weight_taps(input_padded, output_gradient, sequence_length):
    rows = input_padded[0]
    grads = output_gradient[0]
    chans = grads.shape[1]
    chunks = chans // CHUNK
    groups = CHUNK // GROUP_CHANNELS
    mask = group_mask(CHUNK, CHUNK, jnp.float32).reshape(groups, GROUP_CHANNELS, CHUNK)
    taps = []
    for k in range(3):
        parts = []
        for c in range(chunks):
            cols = slice(c * CHUNK, (c + 1) * CHUNK)
            window = rows[k * DILATION_STEP : k * DILATION_STEP + sequence_length, cols]
            full = lax.dot_general(
                window, grads[:, cols], (((0,), (0,)), ((), ())),
                preferred_element_type=jnp.float32,
            ).reshape(groups, GROUP_CHANNELS, CHUNK)
            parts.append(jnp.sum(full * mask, axis=0))
        taps.append(jnp.concatenate(parts, axis=1))
    return jnp.stack(taps)


def swap(value, axis, distance):
    count = lax.axis_size(axis)
    return lax.ppermute(value, axis, [(i, i ^ distance) for i in range(count)])


def tree_sum(value):
    for axis in ("rep", "seq"):
        count = lax.axis_size(axis)
        if count & (count - 1):
            value = lax.psum(value, axis)
            continue
        distance = 1
        while distance < count:
            value = value + swap(value, axis, distance)
            distance *= 2
    return value


def point_gradient(act_rows, cot_rows, seq_count, rep_count):
    chans = act_rows.shape[1]
    block = chans // (seq_count * rep_count)
    blocks = act_rows.reshape(act_rows.shape[0], seq_count, rep_count, block)
    rep_index = lax.axis_index("rep")

    def rows_of(owner):
        cols = lax.dynamic_index_in_dim(blocks, owner, axis=2, keepdims=False)
        cols = cols.reshape(act_rows.shape[0], seq_count * block)
        return lax.dot_general(
            cols, cot_rows, (((0,), (0,)), ((), ())), preferred_element_type=jnp.float32
        )

    if rep_count == 2:
        mine = rows_of(rep_index) + swap(rows_of(1 - rep_index), "rep", 1)
    else:
        full = lax.dot_general(
            act_rows, cot_rows, (((0,), (0,)), ((), ())), preferred_element_type=jnp.float32
        ).reshape(seq_count, rep_count, block, chans)
        mine = lax.psum_scatter(full, "rep", scatter_dimension=1, tiled=True)
        mine = mine.reshape(seq_count * block, chans)
    return lax.psum_scatter(mine, "seq", scatter_dimension=0, tiled=True)

def on_device(inputs, lengths, conv_weight, point_weight, cotangent):
    local_bins = inputs.shape[1]
    chans = inputs.shape[2]
    seq_count = lax.axis_size("seq")
    rep_count = lax.axis_size("rep")
    seq_index = lax.axis_index("seq")
    positions = seq_index * local_bins + jnp.arange(local_bins, dtype=jnp.int32)
    mask = (positions[None, :] < lengths[:, None]).astype(jnp.float32)
    mask3 = mask[:, :, None]
    masked_input = (inputs.astype(jnp.float32) * mask3).astype(jnp.bfloat16)
    scale = 1.0 / math.sqrt(rep_count * seq_count * local_bins)
    padded_input = with_halo(masked_input, (("seq", 1),), DILATION_STEP)
    dense = dense_weight(conv_weight)
    pre = conv_taps(padded_input, dense, local_bins)
    act_val, slope = gelu_pair(pre)
    act = (act_val * mask3).astype(jnp.bfloat16)
    act_rows = act.reshape(local_bins, chans)
    cot_rows = cotangent.reshape(local_bins, chans)
    proj = jnp.dot(act_rows, point_weight, preferred_element_type=jnp.float32).reshape(inputs.shape)
    output = (inputs.astype(jnp.float32) + proj).astype(jnp.bfloat16)
    back = lax.dot_general(
        cot_rows, point_weight, (((1,), (1,)), ((), ())), preferred_element_type=jnp.float32
    )
    preactivation_gradient = (back.reshape(inputs.shape) * slope * mask3).astype(jnp.bfloat16)
    padded_gradient = with_halo(preactivation_gradient, (("seq", 1),), DILATION_STEP)
    spread = conv_taps(padded_gradient, dense, local_bins, transpose=True)
    conv_local = weight_taps(padded_input, preactivation_gradient, local_bins)
    grad_conv = tree_sum(conv_local) * scale
    grad_inputs = (cotangent.astype(jnp.float32) + mask3 * spread).astype(jnp.bfloat16)
    grad_point = point_gradient(act_rows, cot_rows, seq_count, rep_count) * scale
    return (output, grad_inputs, grad_point, grad_conv)


def solution(mesh):
    return jax.shard_map(
        on_device,
        mesh=mesh,
        in_specs=(
            P(("groups", "rep"), "seq", None),
            P(("groups", "rep")),
            P(),
            P(),
            P(("groups", "rep"), "seq", None),
        ),
        out_specs=(
            P(("groups", "rep"), "seq", None),
            P(("groups", "rep"), "seq", None),
            P(("groups", "seq", "rep"), None),
            P("groups", None, None),
        ),
        check_vma=False,
    )
```

```python
import functools
import math

import jax
import jax.numpy as jnp
from jax import lax
from jax.sharding import PartitionSpec as P

GROUP_CHANNELS = 48
DILATION_STEP = 64


def with_halo(cells, sides, width):
    for axis, dim in sides:
        count = lax.axis_size(axis)
        ends = count - 1
        head = lax.slice_in_dim(cells, 0, width, axis=dim)
        tail = lax.slice_in_dim(cells, cells.shape[dim] - width, cells.shape[dim], axis=dim)
        cells = jnp.concatenate(
            [
                lax.ppermute(tail, axis, [(i, (i + 1) % count) for i in range(ends)]),
                cells,
                lax.ppermute(head, axis, [((i + 1) % count, i) for i in range(ends)]),
            ],
            axis=dim,
        )
    return cells


def gelu_pair(pre):
    cdf = 0.5 * (1.0 + jax.scipy.special.erf(pre * 0.7071067811865476))
    dens = jnp.exp(-0.5 * pre * pre) * 0.3989422804014327
    return (pre * cdf, cdf + pre * dens)


CHUNK = 384


def group_mask(rows, chans, dtype):
    row_group = lax.broadcasted_iota(jnp.int32, (rows, chans), 0) // GROUP_CHANNELS
    col_group = (lax.broadcasted_iota(jnp.int32, (rows, chans), 1) % CHUNK) // GROUP_CHANNELS
    return (row_group == col_group).astype(dtype)


def dense_weight(weight):
    taps, width, chans = weight.shape
    groups = CHUNK // width
    tiled = jnp.tile(weight, (1, groups, 1))
    return tiled * group_mask(CHUNK, chans, weight.dtype)[None]


def conv_taps(padded_input, dense, sequence_length, transpose=False):
    rows = padded_input[0]
    chunks = dense.shape[2] // CHUNK
    parts = []
    for c in range(chunks):
        cols = slice(c * CHUNK, (c + 1) * CHUNK)
        total = None
        for k in range(3):
            start = (2 - k if transpose else k) * DILATION_STEP
            window = rows[start : start + sequence_length, cols]
            dims = (((1,), (1,)), ((), ())) if transpose else (((1,), (0,)), ((), ()))
            term = lax.dot_general(
                window, dense[k, :, cols], dims, preferred_element_type=jnp.float32
            )
            total = term if total is None else total + term
        parts.append(total)
    return jnp.concatenate(parts, axis=1)[None]


def weight_taps(input_padded, output_gradient, sequence_length):
    rows = input_padded[0]
    grads = output_gradient[0]
    chans = grads.shape[1]
    chunks = chans // CHUNK
    groups = CHUNK // GROUP_CHANNELS
    mask = group_mask(CHUNK, CHUNK, jnp.float32).reshape(groups, GROUP_CHANNELS, CHUNK)
    taps = []
    for k in range(3):
        parts = []
        for c in range(chunks):
            cols = slice(c * CHUNK, (c + 1) * CHUNK)
            window = rows[k * DILATION_STEP : k * DILATION_STEP + sequence_length, cols]
            full = lax.dot_general(
                window, grads[:, cols], (((0,), (0,)), ((), ())),
                preferred_element_type=jnp.float32,
            ).reshape(groups, GROUP_CHANNELS, CHUNK)
            parts.append(jnp.sum(full * mask, axis=0))
        taps.append(jnp.concatenate(parts, axis=1))
    return jnp.stack(taps)


def swap(value, axis, distance):
    count = lax.axis_size(axis)
    return lax.ppermute(value, axis, [(i, i ^ distance) for i in range(count)])


def ring_order(mesh):
    count = mesh.shape["seq"]
    names = mesh.axis_names
    index = [0] * len(names)
    cells = []
    for s in range(count):
        index[names.index("seq")] = s
        device = mesh.devices[tuple(index)]
        coords = getattr(device, "coords", None)
        if coords is None:
            return list(range(count))
        cells.append((tuple(coords), s))
    cells.sort(key=lambda cell: (cell[0][1], cell[0][2] if cell[0][1] % 2 == 0 else -cell[0][2]))
    return [s for _, s in cells]


def ring_reduce_scatter(blocks, ring):
    count = blocks.shape[0]
    if count == 1:
        return blocks[0]
    position = [0] * count
    for p, s in enumerate(ring):
        position[s] = p
    ring_table = jnp.array(ring, jnp.int32)
    here = jnp.array(position, jnp.int32)[lax.axis_index("seq")]
    half = blocks.shape[2] // 2
    forward = [(ring[i], ring[(i + 1) % count]) for i in range(count)]
    backward = [(ring[i], ring[(i - 1) % count]) for i in range(count)]

    def block(offset, low):
        owner = ring_table[(here + offset) % count]
        rows = lax.dynamic_index_in_dim(blocks, owner, axis=0, keepdims=False)
        return rows[:, :half] if low else rows[:, half:]

    ahead = block(-1, True)
    behind = block(1, False)
    for step in range(count - 1):
        ahead = lax.ppermute(ahead, "seq", forward) + block(-2 - step, True)
        behind = lax.ppermute(behind, "seq", backward) + block(2 + step, False)
    return jnp.concatenate([ahead, behind], axis=1)


def reduce_gradients(act_rows, cot_rows, conv_local, seq_count, rep_count, ring):
    chans = act_rows.shape[1]
    devices = seq_count * rep_count
    block = chans // devices
    blocks = act_rows.reshape(act_rows.shape[0], seq_count, rep_count, block)
    conv_rows = conv_local.reshape(-1, chans)
    conv_count = conv_rows.shape[0]
    share = -(-conv_count // devices)
    conv_rows = jnp.pad(conv_rows, ((0, share * devices - conv_count), (0, 0)))
    conv_cells = conv_rows.reshape(seq_count, rep_count, share, chans)

    def rows_of(owner):
        cols = lax.dynamic_index_in_dim(blocks, owner, axis=2, keepdims=False)
        cols = cols.reshape(act_rows.shape[0], seq_count * block)
        point = lax.dot_general(
            cols, cot_rows, (((0,), (0,)), ((), ())), preferred_element_type=jnp.float32
        ).reshape(seq_count, block, chans)
        conv = lax.dynamic_index_in_dim(conv_cells, owner, axis=1, keepdims=False)
        return jnp.concatenate([point, conv], axis=1)

    rep_index = lax.axis_index("rep")
    if rep_count == 2:
        mine = rows_of(rep_index) + swap(rows_of(1 - rep_index), "rep", 1)
    else:
        mine = rows_of(0)
        for other in range(1, rep_count):
            mine = mine + lax.ppermute(
                rows_of((rep_index + other) % rep_count), "rep",
                [(i, (i + other) % rep_count) for i in range(rep_count)],
            )
    summed = ring_reduce_scatter(mine, ring)
    point = summed[:block]
    conv = lax.all_gather(summed[block:], ("seq", "rep"), axis=0, tiled=True)
    return point, conv[:conv_count].reshape(conv_local.shape)


def on_device(ring, inputs, lengths, conv_weight, point_weight, cotangent):
    local_bins = inputs.shape[1]
    chans = inputs.shape[2]
    seq_count = lax.axis_size("seq")
    rep_count = lax.axis_size("rep")
    seq_index = lax.axis_index("seq")
    positions = seq_index * local_bins + jnp.arange(local_bins, dtype=jnp.int32)
    mask = (positions[None, :] < lengths[:, None]).astype(jnp.float32)
    mask3 = mask[:, :, None]
    masked_input = (inputs.astype(jnp.float32) * mask3).astype(jnp.bfloat16)
    scale = 1.0 / math.sqrt(rep_count * seq_count * local_bins)
    padded_input = with_halo(masked_input, (("seq", 1),), DILATION_STEP)
    dense = dense_weight(conv_weight)
    pre = conv_taps(padded_input, dense, local_bins)
    act_val, slope = gelu_pair(pre)
    act = (act_val * mask3).astype(jnp.bfloat16)
    act_rows = act.reshape(local_bins, chans)
    cot_rows = cotangent.reshape(local_bins, chans)
    proj = jnp.dot(act_rows, point_weight, preferred_element_type=jnp.float32).reshape(inputs.shape)
    output = (inputs.astype(jnp.float32) + proj).astype(jnp.bfloat16)
    back = lax.dot_general(
        cot_rows, point_weight, (((1,), (1,)), ((), ())), preferred_element_type=jnp.float32
    )
    preactivation_gradient = (back.reshape(inputs.shape) * slope * mask3).astype(jnp.bfloat16)
    padded_gradient = with_halo(preactivation_gradient, (("seq", 1),), DILATION_STEP)
    spread = conv_taps(padded_gradient, dense, local_bins, transpose=True)
    conv_local = weight_taps(padded_input, preactivation_gradient, local_bins)
    grad_inputs = (cotangent.astype(jnp.float32) + mask3 * spread).astype(jnp.bfloat16)
    grad_point, grad_conv = reduce_gradients(
        act_rows, cot_rows, conv_local, seq_count, rep_count, ring
    )
    grad_point = grad_point * scale
    grad_conv = grad_conv * scale
    return (output, grad_inputs, grad_point, grad_conv)


def solution(mesh):
    return jax.shard_map(
        functools.partial(on_device, ring_order(mesh)),
        mesh=mesh,
        in_specs=(
            P(("groups", "rep"), "seq", None),
            P(("groups", "rep")),
            P(),
            P(),
            P(("groups", "rep"), "seq", None),
        ),
        out_specs=(
            P(("groups", "rep"), "seq", None),
            P(("groups", "rep"), "seq", None),
            P(("groups", "seq", "rep"), None),
            P("groups", None, None),
        ),
        check_vma=False,
    )
```

```python
import math

import jax
import jax.numpy as jnp
from jax import lax
from jax.sharding import PartitionSpec as P

GROUP_CHANNELS = 48
DILATION_STEP = 64


def with_halo(cells, sides, width):
    for axis, dim in sides:
        count = lax.axis_size(axis)
        ends = count - 1
        head = lax.slice_in_dim(cells, 0, width, axis=dim)
        tail = lax.slice_in_dim(cells, cells.shape[dim] - width, cells.shape[dim], axis=dim)
        cells = jnp.concatenate(
            [
                lax.ppermute(tail, axis, [(i, (i + 1) % count) for i in range(ends)]),
                cells,
                lax.ppermute(head, axis, [((i + 1) % count, i) for i in range(ends)]),
            ],
            axis=dim,
        )
    return cells


def gelu_pair(pre):
    cdf = 0.5 * (1.0 + jax.scipy.special.erf(pre * 0.7071067811865476))
    dens = jnp.exp(-0.5 * pre * pre) * 0.3989422804014327
    return (pre * cdf, cdf + pre * dens)


CHUNK = 384


def group_mask(rows, chans, dtype):
    row_group = lax.broadcasted_iota(jnp.int32, (rows, chans), 0) // GROUP_CHANNELS
    col_group = (lax.broadcasted_iota(jnp.int32, (rows, chans), 1) % CHUNK) // GROUP_CHANNELS
    return (row_group == col_group).astype(dtype)


def dense_weight(weight):
    taps, width, chans = weight.shape
    groups = CHUNK // width
    tiled = jnp.tile(weight, (1, groups, 1))
    return tiled * group_mask(CHUNK, chans, weight.dtype)[None]


def conv_taps(padded_input, dense, sequence_length, transpose=False):
    rows = padded_input[0]
    chunks = dense.shape[2] // CHUNK
    parts = []
    for c in range(chunks):
        cols = slice(c * CHUNK, (c + 1) * CHUNK)
        total = None
        for k in range(3):
            start = (2 - k if transpose else k) * DILATION_STEP
            window = rows[start : start + sequence_length, cols]
            dims = (((1,), (1,)), ((), ())) if transpose else (((1,), (0,)), ((), ()))
            term = lax.dot_general(
                window, dense[k, :, cols], dims, preferred_element_type=jnp.float32
            )
            total = term if total is None else total + term
        parts.append(total)
    return jnp.concatenate(parts, axis=1)[None]


def weight_taps(input_padded, output_gradient, sequence_length):
    rows = input_padded[0]
    grads = output_gradient[0]
    chans = grads.shape[1]
    chunks = chans // CHUNK
    groups = CHUNK // GROUP_CHANNELS
    mask = group_mask(CHUNK, CHUNK, jnp.float32).reshape(groups, GROUP_CHANNELS, CHUNK)
    taps = []
    for k in range(3):
        parts = []
        for c in range(chunks):
            cols = slice(c * CHUNK, (c + 1) * CHUNK)
            window = rows[k * DILATION_STEP : k * DILATION_STEP + sequence_length, cols]
            full = lax.dot_general(
                window, grads[:, cols], (((0,), (0,)), ((), ())),
                preferred_element_type=jnp.float32,
            ).reshape(groups, GROUP_CHANNELS, CHUNK)
            parts.append(jnp.sum(full * mask, axis=0))
        taps.append(jnp.concatenate(parts, axis=1))
    return jnp.stack(taps)


def swap(value, axis, distance):
    count = lax.axis_size(axis)
    return lax.ppermute(value, axis, [(i, i ^ distance) for i in range(count)])


def halving_plan(rows, cols, steps):
    plan = []
    for _ in range(steps):
        if cols % 256 == 0:
            plan.append(1)
            cols //= 2
        else:
            plan.append(0)
            rows //= 2
    return plan


def tree_sum(value):
    shape = value.shape
    cells = value.reshape(-1, shape[-1])
    stages = []
    for axis in ("rep", "seq"):
        distance = 1
        while distance < lax.axis_size(axis):
            stages.append((axis, distance))
            distance *= 2
    plan = halving_plan(cells.shape[0], cells.shape[1], len(stages))
    held = cells
    for (axis, distance), dim in zip(stages, plan):
        bit = (lax.axis_index(axis) // distance) % 2
        size = held.shape[dim] // 2
        keep = lax.dynamic_slice_in_dim(held, bit * size, size, axis=dim)
        give = lax.dynamic_slice_in_dim(held, (1 - bit) * size, size, axis=dim)
        held = keep + swap(give, axis, distance)
    for (axis, distance), dim in reversed(list(zip(stages, plan))):
        bit = (lax.axis_index(axis) // distance) % 2
        size = held.shape[dim]
        other = swap(held, axis, distance)
        full = jnp.concatenate([held, held], axis=dim)
        full = lax.dynamic_update_slice_in_dim(full, held, bit * size, axis=dim)
        held = lax.dynamic_update_slice_in_dim(full, other, (1 - bit) * size, axis=dim)
    return held.reshape(shape)


def point_gradient(act_rows, cot_rows, seq_count, rep_count):
    chans = act_rows.shape[1]
    block = chans // (seq_count * rep_count)
    blocks = act_rows.reshape(act_rows.shape[0], seq_count, rep_count, block)
    rep_index = lax.axis_index("rep")

    def rows_of(owner):
        cols = lax.dynamic_index_in_dim(blocks, owner, axis=2, keepdims=False)
        cols = cols.reshape(act_rows.shape[0], seq_count * block)
        return lax.dot_general(
            cols, cot_rows, (((0,), (0,)), ((), ())), preferred_element_type=jnp.float32
        )

    if rep_count == 2:
        mine = rows_of(rep_index) + swap(rows_of(1 - rep_index), "rep", 1)
    else:
        full = lax.dot_general(
            act_rows, cot_rows, (((0,), (0,)), ((), ())), preferred_element_type=jnp.float32
        ).reshape(seq_count, rep_count, block, chans)
        mine = lax.psum_scatter(full, "rep", scatter_dimension=1, tiled=True)
        mine = mine.reshape(seq_count * block, chans)
    return lax.psum_scatter(mine, "seq", scatter_dimension=0, tiled=True)

def on_device(inputs, lengths, conv_weight, point_weight, cotangent):
    local_bins = inputs.shape[1]
    chans = inputs.shape[2]
    seq_count = lax.axis_size("seq")
    rep_count = lax.axis_size("rep")
    seq_index = lax.axis_index("seq")
    positions = seq_index * local_bins + jnp.arange(local_bins, dtype=jnp.int32)
    mask = (positions[None, :] < lengths[:, None]).astype(jnp.float32)
    mask3 = mask[:, :, None]
    masked_input = (inputs.astype(jnp.float32) * mask3).astype(jnp.bfloat16)
    scale = 1.0 / math.sqrt(rep_count * seq_count * local_bins)
    padded_input = with_halo(masked_input, (("seq", 1),), DILATION_STEP)
    dense = dense_weight(conv_weight)
    pre = conv_taps(padded_input, dense, local_bins)
    act_val, slope = gelu_pair(pre)
    act = (act_val * mask3).astype(jnp.bfloat16)
    act_rows = act.reshape(local_bins, chans)
    cot_rows = cotangent.reshape(local_bins, chans)
    proj = jnp.dot(act_rows, point_weight, preferred_element_type=jnp.float32).reshape(inputs.shape)
    output = (inputs.astype(jnp.float32) + proj).astype(jnp.bfloat16)
    back = lax.dot_general(
        cot_rows, point_weight, (((1,), (1,)), ((), ())), preferred_element_type=jnp.float32
    )
    preactivation_gradient = (back.reshape(inputs.shape) * slope * mask3).astype(jnp.bfloat16)
    padded_gradient = with_halo(preactivation_gradient, (("seq", 1),), DILATION_STEP)
    spread = conv_taps(padded_gradient, dense, local_bins, transpose=True)
    conv_local = weight_taps(padded_input, preactivation_gradient, local_bins)
    grad_conv = tree_sum(conv_local) * scale
    grad_inputs = (cotangent.astype(jnp.float32) + mask3 * spread).astype(jnp.bfloat16)
    grad_point = point_gradient(act_rows, cot_rows, seq_count, rep_count) * scale
    return (output, grad_inputs, grad_point, grad_conv)


def solution(mesh):
    return jax.shard_map(
        on_device,
        mesh=mesh,
        in_specs=(
            P(("groups", "rep"), "seq", None),
            P(("groups", "rep")),
            P(),
            P(),
            P(("groups", "rep"), "seq", None),
        ),
        out_specs=(
            P(("groups", "rep"), "seq", None),
            P(("groups", "rep"), "seq", None),
            P(("groups", "seq", "rep"), None),
            P("groups", None, None),
        ),
        check_vma=False,
    )
```

```python
import math

import jax
import jax.numpy as jnp
from jax import lax
from jax.sharding import PartitionSpec as P

GROUP_CHANNELS = 48
DILATION_STEP = 64


def with_halo(cells, sides, width):
    for axis, dim in sides:
        count = lax.axis_size(axis)
        ends = count - 1
        head = lax.slice_in_dim(cells, 0, width, axis=dim)
        tail = lax.slice_in_dim(cells, cells.shape[dim] - width, cells.shape[dim], axis=dim)
        cells = jnp.concatenate(
            [
                lax.ppermute(tail, axis, [(i, (i + 1) % count) for i in range(ends)]),
                cells,
                lax.ppermute(head, axis, [((i + 1) % count, i) for i in range(ends)]),
            ],
            axis=dim,
        )
    return cells


def gelu_pair(pre):
    cdf = 0.5 * (1.0 + jax.scipy.special.erf(pre * 0.7071067811865476))
    dens = jnp.exp(-0.5 * pre * pre) * 0.3989422804014327
    return (pre * cdf, cdf + pre * dens)


CHUNK = 384


def group_mask(rows, chans, dtype):
    row_group = lax.broadcasted_iota(jnp.int32, (rows, chans), 0) // GROUP_CHANNELS
    col_group = (lax.broadcasted_iota(jnp.int32, (rows, chans), 1) % CHUNK) // GROUP_CHANNELS
    return (row_group == col_group).astype(dtype)


def dense_weight(weight):
    taps, width, chans = weight.shape
    groups = CHUNK // width
    tiled = jnp.tile(weight, (1, groups, 1))
    return tiled * group_mask(CHUNK, chans, weight.dtype)[None]


def conv_taps(padded_input, dense, sequence_length, transpose=False):
    rows = padded_input[0]
    chunks = dense.shape[2] // CHUNK
    parts = []
    for c in range(chunks):
        cols = slice(c * CHUNK, (c + 1) * CHUNK)
        total = None
        for k in range(3):
            start = (2 - k if transpose else k) * DILATION_STEP
            window = rows[start : start + sequence_length, cols]
            dims = (((1,), (1,)), ((), ())) if transpose else (((1,), (0,)), ((), ()))
            term = lax.dot_general(
                window, dense[k, :, cols], dims, preferred_element_type=jnp.float32
            )
            total = term if total is None else total + term
        parts.append(total)
    return jnp.concatenate(parts, axis=1)[None]


def weight_taps(input_padded, output_gradient, sequence_length):
    rows = input_padded[0]
    grads = output_gradient[0]
    chans = grads.shape[1]
    chunks = chans // CHUNK
    groups = CHUNK // GROUP_CHANNELS
    mask = group_mask(CHUNK, CHUNK, jnp.float32).reshape(groups, GROUP_CHANNELS, CHUNK)
    taps = []
    for k in range(3):
        parts = []
        for c in range(chunks):
            cols = slice(c * CHUNK, (c + 1) * CHUNK)
            window = rows[k * DILATION_STEP : k * DILATION_STEP + sequence_length, cols]
            full = lax.dot_general(
                window, grads[:, cols], (((0,), (0,)), ((), ())),
                preferred_element_type=jnp.float32,
            ).reshape(groups, GROUP_CHANNELS, CHUNK)
            parts.append(jnp.sum(full * mask, axis=0))
        taps.append(jnp.concatenate(parts, axis=1))
    return jnp.stack(taps)


def swap(value, axis, distance):
    count = lax.axis_size(axis)
    return lax.ppermute(value, axis, [(i, i ^ distance) for i in range(count)])


def halving_plan(rows, cols, steps):
    plan = []
    for _ in range(steps):
        if cols % 256 == 0:
            plan.append(1)
            cols //= 2
        else:
            plan.append(0)
            rows //= 2
    return plan


def tree_sum(value):
    shape = value.shape
    cells = value.reshape(-1, shape[-1])
    stages = []
    for axis in ("rep", "seq"):
        distance = 1
        while distance < lax.axis_size(axis):
            stages.append((axis, distance))
            distance *= 2
    plan = halving_plan(cells.shape[0], cells.shape[1], len(stages))
    held = cells
    for (axis, distance), dim in zip(stages, plan):
        bit = (lax.axis_index(axis) // distance) % 2
        size = held.shape[dim] // 2
        keep = lax.dynamic_slice_in_dim(held, bit * size, size, axis=dim)
        give = lax.dynamic_slice_in_dim(held, (1 - bit) * size, size, axis=dim)
        held = keep + swap(give, axis, distance)
    for (axis, distance), dim in reversed(list(zip(stages, plan))):
        bit = (lax.axis_index(axis) // distance) % 2
        size = held.shape[dim]
        other = swap(held, axis, distance)
        full = jnp.concatenate([held, held], axis=dim)
        full = lax.dynamic_update_slice_in_dim(full, held, bit * size, axis=dim)
        held = lax.dynamic_update_slice_in_dim(full, other, (1 - bit) * size, axis=dim)
    return held.reshape(shape)


def point_gradient(act_rows, cot_rows):
    return lax.dot_general(
        act_rows, cot_rows, (((0,), (0,)), ((), ())), preferred_element_type=jnp.float32
    )


def on_device(inputs, lengths, conv_weight, point_weight, cotangent):
    local_bins = inputs.shape[1]
    chans = inputs.shape[2]
    seq_count = lax.axis_size("seq")
    rep_count = lax.axis_size("rep")
    seq_index = lax.axis_index("seq")
    positions = seq_index * local_bins + jnp.arange(local_bins, dtype=jnp.int32)
    mask = (positions[None, :] < lengths[:, None]).astype(jnp.float32)
    mask3 = mask[:, :, None]
    masked_input = (inputs.astype(jnp.float32) * mask3).astype(jnp.bfloat16)
    scale = 1.0 / math.sqrt(rep_count * seq_count * local_bins)
    padded_input = with_halo(masked_input, (("seq", 1),), DILATION_STEP)
    dense = dense_weight(conv_weight)
    pre = conv_taps(padded_input, dense, local_bins)
    act_val, slope = gelu_pair(pre)
    act = (act_val * mask3).astype(jnp.bfloat16)
    act_rows = act.reshape(local_bins, chans)
    cot_rows = cotangent.reshape(local_bins, chans)
    proj = jnp.dot(act_rows, point_weight, preferred_element_type=jnp.float32).reshape(inputs.shape)
    output = (inputs.astype(jnp.float32) + proj).astype(jnp.bfloat16)
    point_partial = point_gradient(act_rows, cot_rows)
    point_partial, cot_rows = lax.optimization_barrier((point_partial, cot_rows))
    grad_point = lax.psum_scatter(
        point_partial, ("seq", "rep"), scatter_dimension=0, tiled=True
    )
    back = lax.dot_general(
        cot_rows, point_weight, (((1,), (1,)), ((), ())), preferred_element_type=jnp.float32
    )
    preactivation_gradient = (back.reshape(inputs.shape) * slope * mask3).astype(jnp.bfloat16)
    padded_gradient = with_halo(preactivation_gradient, (("seq", 1),), DILATION_STEP)
    spread = conv_taps(padded_gradient, dense, local_bins, transpose=True)
    conv_local = weight_taps(padded_input, preactivation_gradient, local_bins)
    grad_conv = tree_sum(conv_local) * scale
    grad_inputs = (cotangent.astype(jnp.float32) + mask3 * spread).astype(jnp.bfloat16)
    grad_point = grad_point * scale
    return (output, grad_inputs, grad_point, grad_conv)


def solution(mesh):
    return jax.shard_map(
        on_device,
        mesh=mesh,
        in_specs=(
            P(("groups", "rep"), "seq", None),
            P(("groups", "rep")),
            P(),
            P(),
            P(("groups", "rep"), "seq", None),
        ),
        out_specs=(
            P(("groups", "rep"), "seq", None),
            P(("groups", "rep"), "seq", None),
            P(("groups", "seq", "rep"), None),
            P("groups", None, None),
        ),
        check_vma=False,
    )
```

```python
import functools
import math

import jax
import jax.numpy as jnp
from jax import lax
from jax.sharding import PartitionSpec as P

GROUP_CHANNELS = 48
DILATION_STEP = 64


def with_halo(cells, sides, width):
    for axis, dim in sides:
        count = lax.axis_size(axis)
        ends = count - 1
        head = lax.slice_in_dim(cells, 0, width, axis=dim)
        tail = lax.slice_in_dim(cells, cells.shape[dim] - width, cells.shape[dim], axis=dim)
        cells = jnp.concatenate(
            [
                lax.ppermute(tail, axis, [(i, (i + 1) % count) for i in range(ends)]),
                cells,
                lax.ppermute(head, axis, [((i + 1) % count, i) for i in range(ends)]),
            ],
            axis=dim,
        )
    return cells


def gelu_pair(pre):
    cdf = 0.5 * (1.0 + jax.scipy.special.erf(pre * 0.7071067811865476))
    dens = jnp.exp(-0.5 * pre * pre) * 0.3989422804014327
    return (pre * cdf, cdf + pre * dens)


CHUNK = 384


def group_mask(rows, chans, dtype):
    row_group = lax.broadcasted_iota(jnp.int32, (rows, chans), 0) // GROUP_CHANNELS
    col_group = (lax.broadcasted_iota(jnp.int32, (rows, chans), 1) % CHUNK) // GROUP_CHANNELS
    return (row_group == col_group).astype(dtype)


def dense_weight(weight):
    taps, width, chans = weight.shape
    groups = CHUNK // width
    tiled = jnp.tile(weight, (1, groups, 1))
    return tiled * group_mask(CHUNK, chans, weight.dtype)[None]


def conv_taps(padded_input, dense, sequence_length, transpose=False):
    rows = padded_input[0]
    chunks = dense.shape[2] // CHUNK
    parts = []
    for c in range(chunks):
        cols = slice(c * CHUNK, (c + 1) * CHUNK)
        total = None
        for k in range(3):
            start = (2 - k if transpose else k) * DILATION_STEP
            window = rows[start : start + sequence_length, cols]
            dims = (((1,), (1,)), ((), ())) if transpose else (((1,), (0,)), ((), ()))
            term = lax.dot_general(
                window, dense[k, :, cols], dims, preferred_element_type=jnp.float32
            )
            total = term if total is None else total + term
        parts.append(total)
    return jnp.concatenate(parts, axis=1)[None]


def weight_taps(input_padded, output_gradient, sequence_length):
    rows = input_padded[0]
    grads = output_gradient[0]
    chans = grads.shape[1]
    chunks = chans // CHUNK
    groups = CHUNK // GROUP_CHANNELS
    mask = group_mask(CHUNK, CHUNK, jnp.float32).reshape(groups, GROUP_CHANNELS, CHUNK)
    taps = []
    for k in range(3):
        parts = []
        for c in range(chunks):
            cols = slice(c * CHUNK, (c + 1) * CHUNK)
            window = rows[k * DILATION_STEP : k * DILATION_STEP + sequence_length, cols]
            full = lax.dot_general(
                window, grads[:, cols], (((0,), (0,)), ((), ())),
                preferred_element_type=jnp.float32,
            ).reshape(groups, GROUP_CHANNELS, CHUNK)
            parts.append(jnp.sum(full * mask, axis=0))
        taps.append(jnp.concatenate(parts, axis=1))
    return jnp.stack(taps)


def swap(value, axis, distance):
    count = lax.axis_size(axis)
    return lax.ppermute(value, axis, [(i, i ^ distance) for i in range(count)])


def halving_plan(rows, cols, steps):
    plan = []
    for _ in range(steps):
        if cols % 256 == 0:
            plan.append(1)
            cols //= 2
        else:
            plan.append(0)
            rows //= 2
    return plan


def tree_sum(value):
    shape = value.shape
    cells = value.reshape(-1, shape[-1])
    stages = []
    for axis in ("rep", "seq"):
        distance = 1
        while distance < lax.axis_size(axis):
            stages.append((axis, distance))
            distance *= 2
    plan = halving_plan(cells.shape[0], cells.shape[1], len(stages))
    held = cells
    for (axis, distance), dim in zip(stages, plan):
        bit = (lax.axis_index(axis) // distance) % 2
        size = held.shape[dim] // 2
        keep = lax.dynamic_slice_in_dim(held, bit * size, size, axis=dim)
        give = lax.dynamic_slice_in_dim(held, (1 - bit) * size, size, axis=dim)
        held = keep + swap(give, axis, distance)
    for (axis, distance), dim in reversed(list(zip(stages, plan))):
        bit = (lax.axis_index(axis) // distance) % 2
        size = held.shape[dim]
        other = swap(held, axis, distance)
        full = jnp.concatenate([held, held], axis=dim)
        full = lax.dynamic_update_slice_in_dim(full, held, bit * size, axis=dim)
        held = lax.dynamic_update_slice_in_dim(full, other, (1 - bit) * size, axis=dim)
    return held.reshape(shape)


def ring_order(mesh):
    count = mesh.shape["seq"]
    names = mesh.axis_names
    index = [0] * len(names)
    cells = []
    for s in range(count):
        index[names.index("seq")] = s
        device = mesh.devices[tuple(index)]
        coords = getattr(device, "coords", None)
        if coords is None:
            return list(range(count))
        cells.append((tuple(coords), s))
    cells.sort(key=lambda cell: (cell[0][1], cell[0][2] if cell[0][1] % 2 == 0 else -cell[0][2]))
    return [s for _, s in cells]


def ring_reduce_scatter(blocks, ring):
    count = blocks.shape[0]
    if count == 1:
        return blocks[0]
    position = [0] * count
    for p, s in enumerate(ring):
        position[s] = p
    ring_table = jnp.array(ring, jnp.int32)
    here = jnp.array(position, jnp.int32)[lax.axis_index("seq")]
    half = blocks.shape[2] // 2
    forward = [(ring[i], ring[(i + 1) % count]) for i in range(count)]
    backward = [(ring[i], ring[(i - 1) % count]) for i in range(count)]

    def block(offset, low):
        owner = ring_table[(here + offset) % count]
        rows = lax.dynamic_index_in_dim(blocks, owner, axis=0, keepdims=False)
        return rows[:, :half] if low else rows[:, half:]

    ahead = block(-1, True)
    behind = block(1, False)
    for step in range(count - 1):
        ahead = lax.ppermute(ahead, "seq", forward) + block(-2 - step, True)
        behind = lax.ppermute(behind, "seq", backward) + block(2 + step, False)
    return jnp.concatenate([ahead, behind], axis=1)


def point_gradient(act_rows, cot_rows, ring):
    chans = act_rows.shape[1]
    seq_count = lax.axis_size("seq")
    rep_count = lax.axis_size("rep")
    block = chans // (seq_count * rep_count)
    split = chans // 2
    product = lambda a, b: lax.dot_general(
        a, b, (((0,), (0,)), ((), ())), preferred_element_type=jnp.float32
    )
    offload = product(act_rows, cot_rows[:, :split])
    offload, cot_rows = lax.optimization_barrier((offload, cot_rows))
    first = lax.psum_scatter(offload, ("seq", "rep"), scatter_dimension=0, tiled=True)
    if rep_count != 2:
        rest = lax.psum_scatter(
            product(act_rows, cot_rows[:, split:]), ("seq", "rep"),
            scatter_dimension=0, tiled=True,
        )
        return jnp.concatenate([first, rest], axis=1), cot_rows
    blocks = act_rows.reshape(act_rows.shape[0], seq_count, rep_count, block)
    rep_index = lax.axis_index("rep")

    def rows_of(owner):
        cols = lax.dynamic_index_in_dim(blocks, owner, axis=2, keepdims=False)
        cols = cols.reshape(act_rows.shape[0], seq_count * block)
        return product(cols, cot_rows[:, split:]).reshape(seq_count, block, chans - split)

    mine = rows_of(rep_index) + swap(rows_of(1 - rep_index), "rep", 1)
    rest = ring_reduce_scatter(mine, ring)
    return jnp.concatenate([first, rest], axis=1), cot_rows


def on_device(ring, inputs, lengths, conv_weight, point_weight, cotangent):
    local_bins = inputs.shape[1]
    chans = inputs.shape[2]
    seq_count = lax.axis_size("seq")
    rep_count = lax.axis_size("rep")
    seq_index = lax.axis_index("seq")
    positions = seq_index * local_bins + jnp.arange(local_bins, dtype=jnp.int32)
    mask = (positions[None, :] < lengths[:, None]).astype(jnp.float32)
    mask3 = mask[:, :, None]
    masked_input = (inputs.astype(jnp.float32) * mask3).astype(jnp.bfloat16)
    scale = 1.0 / math.sqrt(rep_count * seq_count * local_bins)
    padded_input = with_halo(masked_input, (("seq", 1),), DILATION_STEP)
    dense = dense_weight(conv_weight)
    pre = conv_taps(padded_input, dense, local_bins)
    act_val, slope = gelu_pair(pre)
    act = (act_val * mask3).astype(jnp.bfloat16)
    act_rows = act.reshape(local_bins, chans)
    cot_rows = cotangent.reshape(local_bins, chans)
    proj = jnp.dot(act_rows, point_weight, preferred_element_type=jnp.float32).reshape(inputs.shape)
    output = (inputs.astype(jnp.float32) + proj).astype(jnp.bfloat16)
    grad_point, cot_rows = point_gradient(act_rows, cot_rows, ring)
    back = lax.dot_general(
        cot_rows, point_weight, (((1,), (1,)), ((), ())), preferred_element_type=jnp.float32
    )
    preactivation_gradient = (back.reshape(inputs.shape) * slope * mask3).astype(jnp.bfloat16)
    padded_gradient = with_halo(preactivation_gradient, (("seq", 1),), DILATION_STEP)
    spread = conv_taps(padded_gradient, dense, local_bins, transpose=True)
    conv_local = weight_taps(padded_input, preactivation_gradient, local_bins)
    grad_conv = tree_sum(conv_local) * scale
    grad_inputs = (cotangent.astype(jnp.float32) + mask3 * spread).astype(jnp.bfloat16)
    grad_point = grad_point * scale
    return (output, grad_inputs, grad_point, grad_conv)


def solution(mesh):
    return jax.shard_map(
        functools.partial(on_device, ring_order(mesh)),
        mesh=mesh,
        in_specs=(
            P(("groups", "rep"), "seq", None),
            P(("groups", "rep")),
            P(),
            P(),
            P(("groups", "rep"), "seq", None),
        ),
        out_specs=(
            P(("groups", "rep"), "seq", None),
            P(("groups", "rep"), "seq", None),
            P(("groups", "seq", "rep"), None),
            P("groups", None, None),
        ),
        check_vma=False,
    )
```

```python
import math

import jax
import jax.numpy as jnp
from jax import lax
from jax.sharding import PartitionSpec as P

GROUP_CHANNELS = 48
DILATION_STEP = 64


def with_halo(cells, sides, width):
    for axis, dim in sides:
        count = lax.axis_size(axis)
        ends = count - 1
        head = lax.slice_in_dim(cells, 0, width, axis=dim)
        tail = lax.slice_in_dim(cells, cells.shape[dim] - width, cells.shape[dim], axis=dim)
        cells = jnp.concatenate(
            [
                lax.ppermute(tail, axis, [(i, (i + 1) % count) for i in range(ends)]),
                cells,
                lax.ppermute(head, axis, [((i + 1) % count, i) for i in range(ends)]),
            ],
            axis=dim,
        )
    return cells


def gelu_pair(pre):
    cdf = 0.5 * (1.0 + jax.scipy.special.erf(pre * 0.7071067811865476))
    dens = jnp.exp(-0.5 * pre * pre) * 0.3989422804014327
    return (pre * cdf, cdf + pre * dens)


CHUNK = 384


def group_mask(rows, chans, dtype):
    row_group = lax.broadcasted_iota(jnp.int32, (rows, chans), 0) // GROUP_CHANNELS
    col_group = (lax.broadcasted_iota(jnp.int32, (rows, chans), 1) % CHUNK) // GROUP_CHANNELS
    return (row_group == col_group).astype(dtype)


def dense_weight(weight):
    taps, width, chans = weight.shape
    groups = CHUNK // width
    tiled = jnp.tile(weight, (1, groups, 1))
    return tiled * group_mask(CHUNK, chans, weight.dtype)[None]


def conv_taps(padded_input, dense, sequence_length, transpose=False):
    rows = padded_input[0]
    chunks = dense.shape[2] // CHUNK
    parts = []
    for c in range(chunks):
        cols = slice(c * CHUNK, (c + 1) * CHUNK)
        total = None
        for k in range(3):
            start = (2 - k if transpose else k) * DILATION_STEP
            window = rows[start : start + sequence_length, cols]
            dims = (((1,), (1,)), ((), ())) if transpose else (((1,), (0,)), ((), ()))
            term = lax.dot_general(
                window, dense[k, :, cols], dims, preferred_element_type=jnp.float32
            )
            total = term if total is None else total + term
        parts.append(total)
    return jnp.concatenate(parts, axis=1)[None]


def weight_taps(input_padded, output_gradient, sequence_length):
    rows = input_padded[0]
    grads = output_gradient[0]
    chans = grads.shape[1]
    chunks = chans // CHUNK
    groups = CHUNK // GROUP_CHANNELS
    mask = group_mask(CHUNK, CHUNK, jnp.float32).reshape(groups, GROUP_CHANNELS, CHUNK)
    taps = []
    for k in range(3):
        parts = []
        for c in range(chunks):
            cols = slice(c * CHUNK, (c + 1) * CHUNK)
            window = rows[k * DILATION_STEP : k * DILATION_STEP + sequence_length, cols]
            full = lax.dot_general(
                window, grads[:, cols], (((0,), (0,)), ((), ())),
                preferred_element_type=jnp.float32,
            ).reshape(groups, GROUP_CHANNELS, CHUNK)
            parts.append(jnp.sum(full * mask, axis=0))
        taps.append(jnp.concatenate(parts, axis=1))
    return jnp.stack(taps)


def swap(value, axis, distance):
    count = lax.axis_size(axis)
    return lax.ppermute(value, axis, [(i, i ^ distance) for i in range(count)])


def halving_plan(rows, cols, steps):
    plan = []
    for _ in range(steps):
        if cols % 256 == 0:
            plan.append(1)
            cols //= 2
        else:
            plan.append(0)
            rows //= 2
    return plan


def tree_sum(value):
    shape = value.shape
    cells = value.reshape(-1, shape[-1])
    stages = []
    for axis in ("rep", "seq"):
        distance = 1
        while distance < lax.axis_size(axis):
            stages.append((axis, distance))
            distance *= 2
    plan = halving_plan(cells.shape[0], cells.shape[1], len(stages))
    held = cells
    for (axis, distance), dim in zip(stages, plan):
        bit = (lax.axis_index(axis) // distance) % 2
        size = held.shape[dim] // 2
        keep = lax.dynamic_slice_in_dim(held, bit * size, size, axis=dim)
        give = lax.dynamic_slice_in_dim(held, (1 - bit) * size, size, axis=dim)
        held = keep + swap(give, axis, distance)
    for (axis, distance), dim in reversed(list(zip(stages, plan))):
        bit = (lax.axis_index(axis) // distance) % 2
        size = held.shape[dim]
        other = swap(held, axis, distance)
        full = jnp.concatenate([held, held], axis=dim)
        full = lax.dynamic_update_slice_in_dim(full, held, bit * size, axis=dim)
        held = lax.dynamic_update_slice_in_dim(full, other, (1 - bit) * size, axis=dim)
    return held.reshape(shape)


def point_gradient(act_rows, cot_rows):
    chans = act_rows.shape[1]
    seq_count = lax.axis_size("seq")
    rep_count = lax.axis_size("rep")
    product = lambda a, b: lax.dot_general(
        a, b, (((0,), (0,)), ((), ())), preferred_element_type=jnp.float32
    )
    if rep_count != 2:
        partial = product(act_rows, cot_rows)
        partial, cot_rows = lax.optimization_barrier((partial, cot_rows))
        total = lax.psum_scatter(partial, ("seq", "rep"), scatter_dimension=0, tiled=True)
        return total, cot_rows
    block = chans // (seq_count * rep_count)
    blocks = act_rows.reshape(act_rows.shape[0], seq_count, rep_count, block)
    rep_index = lax.axis_index("rep")

    def rows_of(owner):
        cols = lax.dynamic_index_in_dim(blocks, owner, axis=2, keepdims=False)
        return product(cols.reshape(act_rows.shape[0], seq_count * block), cot_rows)

    mine = rows_of(rep_index) + swap(rows_of(1 - rep_index), "rep", 1)
    mine, cot_rows = lax.optimization_barrier((mine, cot_rows))
    total = lax.psum_scatter(mine, "seq", scatter_dimension=0, tiled=True)
    return total, cot_rows


def on_device(inputs, lengths, conv_weight, point_weight, cotangent):
    local_bins = inputs.shape[1]
    chans = inputs.shape[2]
    seq_count = lax.axis_size("seq")
    rep_count = lax.axis_size("rep")
    seq_index = lax.axis_index("seq")
    positions = seq_index * local_bins + jnp.arange(local_bins, dtype=jnp.int32)
    mask = (positions[None, :] < lengths[:, None]).astype(jnp.float32)
    mask3 = mask[:, :, None]
    masked_input = (inputs.astype(jnp.float32) * mask3).astype(jnp.bfloat16)
    scale = 1.0 / math.sqrt(rep_count * seq_count * local_bins)
    padded_input = with_halo(masked_input, (("seq", 1),), DILATION_STEP)
    dense = dense_weight(conv_weight)
    pre = conv_taps(padded_input, dense, local_bins)
    act_val, slope = gelu_pair(pre)
    act = (act_val * mask3).astype(jnp.bfloat16)
    act_rows = act.reshape(local_bins, chans)
    cot_rows = cotangent.reshape(local_bins, chans)
    proj = jnp.dot(act_rows, point_weight, preferred_element_type=jnp.float32).reshape(inputs.shape)
    output = (inputs.astype(jnp.float32) + proj).astype(jnp.bfloat16)
    grad_point, cot_rows = point_gradient(act_rows, cot_rows)
    back = lax.dot_general(
        cot_rows, point_weight, (((1,), (1,)), ((), ())), preferred_element_type=jnp.float32
    )
    preactivation_gradient = (back.reshape(inputs.shape) * slope * mask3).astype(jnp.bfloat16)
    padded_gradient = with_halo(preactivation_gradient, (("seq", 1),), DILATION_STEP)
    spread = conv_taps(padded_gradient, dense, local_bins, transpose=True)
    conv_local = weight_taps(padded_input, preactivation_gradient, local_bins)
    grad_conv = tree_sum(conv_local) * scale
    grad_inputs = (cotangent.astype(jnp.float32) + mask3 * spread).astype(jnp.bfloat16)
    grad_point = grad_point * scale
    return (output, grad_inputs, grad_point, grad_conv)


def solution(mesh):
    return jax.shard_map(
        on_device,
        mesh=mesh,
        in_specs=(
            P(("groups", "rep"), "seq", None),
            P(("groups", "rep")),
            P(),
            P(),
            P(("groups", "rep"), "seq", None),
        ),
        out_specs=(
            P(("groups", "rep"), "seq", None),
            P(("groups", "rep"), "seq", None),
            P(("groups", "seq", "rep"), None),
            P("groups", None, None),
        ),
        check_vma=False,
    )
```

```python
import math

import jax
import jax.numpy as jnp
from jax import lax
from jax.sharding import PartitionSpec as P

GROUP_CHANNELS = 48
DILATION_STEP = 64


def with_halo(cells, sides, width):
    for axis, dim in sides:
        count = lax.axis_size(axis)
        ends = count - 1
        head = lax.slice_in_dim(cells, 0, width, axis=dim)
        tail = lax.slice_in_dim(cells, cells.shape[dim] - width, cells.shape[dim], axis=dim)
        cells = jnp.concatenate(
            [
                lax.ppermute(tail, axis, [(i, (i + 1) % count) for i in range(ends)]),
                cells,
                lax.ppermute(head, axis, [((i + 1) % count, i) for i in range(ends)]),
            ],
            axis=dim,
        )
    return cells


def halos(cells, axis, width):
    count = lax.axis_size(axis)
    ends = count - 1
    head = lax.slice_in_dim(cells, 0, width, axis=1)
    tail = lax.slice_in_dim(cells, cells.shape[1] - width, cells.shape[1], axis=1)
    left = lax.ppermute(tail, axis, [(i, (i + 1) % count) for i in range(ends)])
    right = lax.ppermute(head, axis, [((i + 1) % count, i) for i in range(ends)])
    return left, right


def edge_taps(left, right, dense, sequence_length):
    chunks = dense.shape[2] // CHUNK
    width = left.shape[1]

    def side(rows, k):
        return jnp.concatenate(
            [
                jnp.dot(
                    rows[0, :, c * CHUNK : (c + 1) * CHUNK],
                    dense[k, :, c * CHUNK : (c + 1) * CHUNK],
                    preferred_element_type=jnp.float32,
                )
                for c in range(chunks)
            ],
            axis=1,
        )

    middle = jnp.zeros((sequence_length - 2 * width, dense.shape[2]), jnp.float32)
    return jnp.concatenate([side(left, 0), middle, side(right, 2)], axis=0)[None]


def gelu_pair(pre):
    cdf = 0.5 * (1.0 + jax.scipy.special.erf(pre * 0.7071067811865476))
    dens = jnp.exp(-0.5 * pre * pre) * 0.3989422804014327
    return (pre * cdf, cdf + pre * dens)


CHUNK = 384


def group_mask(rows, chans, dtype):
    row_group = lax.broadcasted_iota(jnp.int32, (rows, chans), 0) // GROUP_CHANNELS
    col_group = (lax.broadcasted_iota(jnp.int32, (rows, chans), 1) % CHUNK) // GROUP_CHANNELS
    return (row_group == col_group).astype(dtype)


def dense_weight(weight):
    taps, width, chans = weight.shape
    groups = CHUNK // width
    tiled = jnp.tile(weight, (1, groups, 1))
    return tiled * group_mask(CHUNK, chans, weight.dtype)[None]


def conv_taps(padded_input, dense, sequence_length, transpose=False):
    rows = padded_input[0]
    chunks = dense.shape[2] // CHUNK
    parts = []
    for c in range(chunks):
        cols = slice(c * CHUNK, (c + 1) * CHUNK)
        total = None
        for k in range(3):
            start = (2 - k if transpose else k) * DILATION_STEP
            window = rows[start : start + sequence_length, cols]
            dims = (((1,), (1,)), ((), ())) if transpose else (((1,), (0,)), ((), ()))
            term = lax.dot_general(
                window, dense[k, :, cols], dims, preferred_element_type=jnp.float32
            )
            total = term if total is None else total + term
        parts.append(total)
    return jnp.concatenate(parts, axis=1)[None]


def weight_taps(input_padded, output_gradient, sequence_length):
    rows = input_padded[0]
    grads = output_gradient[0]
    chans = grads.shape[1]
    chunks = chans // CHUNK
    groups = CHUNK // GROUP_CHANNELS
    mask = group_mask(CHUNK, CHUNK, jnp.float32).reshape(groups, GROUP_CHANNELS, CHUNK)
    taps = []
    for k in range(3):
        parts = []
        for c in range(chunks):
            cols = slice(c * CHUNK, (c + 1) * CHUNK)
            window = rows[k * DILATION_STEP : k * DILATION_STEP + sequence_length, cols]
            full = lax.dot_general(
                window, grads[:, cols], (((0,), (0,)), ((), ())),
                preferred_element_type=jnp.float32,
            ).reshape(groups, GROUP_CHANNELS, CHUNK)
            parts.append(jnp.sum(full * mask, axis=0))
        taps.append(jnp.concatenate(parts, axis=1))
    return jnp.stack(taps)


def swap(value, axis, distance):
    count = lax.axis_size(axis)
    return lax.ppermute(value, axis, [(i, i ^ distance) for i in range(count)])


def halving_plan(rows, cols, steps):
    plan = []
    for _ in range(steps):
        if cols % 256 == 0:
            plan.append(1)
            cols //= 2
        else:
            plan.append(0)
            rows //= 2
    return plan


def tree_sum(value):
    shape = value.shape
    cells = value.reshape(-1, shape[-1])
    stages = []
    for axis in ("rep", "seq"):
        distance = 1
        while distance < lax.axis_size(axis):
            stages.append((axis, distance))
            distance *= 2
    plan = halving_plan(cells.shape[0], cells.shape[1], len(stages))
    held = cells
    for (axis, distance), dim in zip(stages, plan):
        bit = (lax.axis_index(axis) // distance) % 2
        size = held.shape[dim] // 2
        keep = lax.dynamic_slice_in_dim(held, bit * size, size, axis=dim)
        give = lax.dynamic_slice_in_dim(held, (1 - bit) * size, size, axis=dim)
        held = keep + swap(give, axis, distance)
    for (axis, distance), dim in reversed(list(zip(stages, plan))):
        bit = (lax.axis_index(axis) // distance) % 2
        size = held.shape[dim]
        other = swap(held, axis, distance)
        full = jnp.concatenate([held, held], axis=dim)
        full = lax.dynamic_update_slice_in_dim(full, held, bit * size, axis=dim)
        held = lax.dynamic_update_slice_in_dim(full, other, (1 - bit) * size, axis=dim)
    return held.reshape(shape)


def point_gradient(act_rows, cot_rows):
    return lax.dot_general(
        act_rows, cot_rows, (((0,), (0,)), ((), ())), preferred_element_type=jnp.float32
    )


def on_device(inputs, lengths, conv_weight, point_weight, cotangent):
    local_bins = inputs.shape[1]
    chans = inputs.shape[2]
    seq_count = lax.axis_size("seq")
    rep_count = lax.axis_size("rep")
    seq_index = lax.axis_index("seq")
    positions = seq_index * local_bins + jnp.arange(local_bins, dtype=jnp.int32)
    mask = (positions[None, :] < lengths[:, None]).astype(jnp.float32)
    mask3 = mask[:, :, None]
    masked_input = (inputs.astype(jnp.float32) * mask3).astype(jnp.bfloat16)
    scale = 1.0 / math.sqrt(rep_count * seq_count * local_bins)
    left, right = halos(masked_input, "seq", DILATION_STEP)
    dense = dense_weight(conv_weight)
    zero_padded = jnp.pad(masked_input, ((0, 0), (DILATION_STEP, DILATION_STEP), (0, 0)))
    pre = conv_taps(zero_padded, dense, local_bins) + edge_taps(left, right, dense, local_bins)
    padded_input = jnp.concatenate([left, masked_input, right], axis=1)
    act_val, slope = gelu_pair(pre)
    act = (act_val * mask3).astype(jnp.bfloat16)
    act_rows = act.reshape(local_bins, chans)
    cot_rows = cotangent.reshape(local_bins, chans)
    proj = jnp.dot(act_rows, point_weight, preferred_element_type=jnp.float32).reshape(inputs.shape)
    output = (inputs.astype(jnp.float32) + proj).astype(jnp.bfloat16)
    point_partial = point_gradient(act_rows, cot_rows) * scale
    point_partial, cot_rows = lax.optimization_barrier((point_partial, cot_rows))
    grad_point = lax.psum_scatter(
        point_partial, ("seq", "rep"), scatter_dimension=0, tiled=True
    )
    back = lax.dot_general(
        cot_rows, point_weight, (((1,), (1,)), ((), ())), preferred_element_type=jnp.float32
    )
    preactivation_gradient = (back.reshape(inputs.shape) * slope * mask3).astype(jnp.bfloat16)
    padded_gradient = with_halo(preactivation_gradient, (("seq", 1),), DILATION_STEP)
    spread = conv_taps(padded_gradient, dense, local_bins, transpose=True)
    conv_local = weight_taps(padded_input, preactivation_gradient, local_bins)
    grad_conv = tree_sum(conv_local) * scale
    grad_inputs = (cotangent.astype(jnp.float32) + mask3 * spread).astype(jnp.bfloat16)
    return (output, grad_inputs, grad_point, grad_conv)


def solution(mesh):
    return jax.shard_map(
        on_device,
        mesh=mesh,
        in_specs=(
            P(("groups", "rep"), "seq", None),
            P(("groups", "rep")),
            P(),
            P(),
            P(("groups", "rep"), "seq", None),
        ),
        out_specs=(
            P(("groups", "rep"), "seq", None),
            P(("groups", "rep"), "seq", None),
            P(("groups", "seq", "rep"), None),
            P("groups", None, None),
        ),
        check_vma=False,
    )
```

```python
import math

import jax
import jax.numpy as jnp
from jax import lax
from jax.sharding import PartitionSpec as P

GROUP_CHANNELS = 48
DILATION_STEP = 64


def with_halo(cells, sides, width):
    for axis, dim in sides:
        count = lax.axis_size(axis)
        ends = count - 1
        head = lax.slice_in_dim(cells, 0, width, axis=dim)
        tail = lax.slice_in_dim(cells, cells.shape[dim] - width, cells.shape[dim], axis=dim)
        cells = jnp.concatenate(
            [
                lax.ppermute(tail, axis, [(i, (i + 1) % count) for i in range(ends)]),
                cells,
                lax.ppermute(head, axis, [((i + 1) % count, i) for i in range(ends)]),
            ],
            axis=dim,
        )
    return cells


def gelu_pair(pre):
    cdf = 0.5 * (1.0 + jax.scipy.special.erf(pre * 0.7071067811865476))
    dens = jnp.exp(-0.5 * pre * pre) * 0.3989422804014327
    return (pre * cdf, cdf + pre * dens)


CHUNK = 384


def group_mask(rows, chans, dtype):
    row_group = lax.broadcasted_iota(jnp.int32, (rows, chans), 0) // GROUP_CHANNELS
    col_group = (lax.broadcasted_iota(jnp.int32, (rows, chans), 1) % CHUNK) // GROUP_CHANNELS
    return (row_group == col_group).astype(dtype)


def dense_weight(weight):
    taps, width, chans = weight.shape
    groups = CHUNK // width
    tiled = jnp.tile(weight, (1, groups, 1))
    return tiled * group_mask(CHUNK, chans, weight.dtype)[None]


def conv_taps(padded_input, dense, sequence_length, transpose=False):
    rows = padded_input[0]
    chunks = dense.shape[2] // CHUNK
    parts = []
    for c in range(chunks):
        cols = slice(c * CHUNK, (c + 1) * CHUNK)
        total = None
        for k in range(3):
            start = (2 - k if transpose else k) * DILATION_STEP
            window = rows[start : start + sequence_length, cols]
            dims = (((1,), (1,)), ((), ())) if transpose else (((1,), (0,)), ((), ()))
            term = lax.dot_general(
                window, dense[k, :, cols], dims, preferred_element_type=jnp.float32
            )
            total = term if total is None else total + term
        parts.append(total)
    return jnp.concatenate(parts, axis=1)[None]


def weight_taps(input_padded, output_gradient, sequence_length):
    rows = input_padded[0]
    grads = output_gradient[0]
    chans = grads.shape[1]
    chunks = chans // CHUNK
    groups = CHUNK // GROUP_CHANNELS
    mask = group_mask(CHUNK, CHUNK, jnp.float32).reshape(groups, GROUP_CHANNELS, CHUNK)
    taps = []
    for k in range(3):
        parts = []
        for c in range(chunks):
            cols = slice(c * CHUNK, (c + 1) * CHUNK)
            window = rows[k * DILATION_STEP : k * DILATION_STEP + sequence_length, cols]
            full = lax.dot_general(
                window, grads[:, cols], (((0,), (0,)), ((), ())),
                preferred_element_type=jnp.float32,
            ).reshape(groups, GROUP_CHANNELS, CHUNK)
            parts.append(jnp.sum(full * mask, axis=0))
        taps.append(jnp.concatenate(parts, axis=1))
    return jnp.stack(taps)


def swap(value, axis, distance):
    count = lax.axis_size(axis)
    return lax.ppermute(value, axis, [(i, i ^ distance) for i in range(count)])


def halving_plan(rows, cols, steps):
    plan = []
    for _ in range(steps):
        if cols % 256 == 0:
            plan.append(1)
            cols //= 2
        else:
            plan.append(0)
            rows //= 2
    return plan


def tree_sum(value):
    shape = value.shape
    cells = value.reshape(-1, shape[-1])
    stages = []
    for axis in ("rep", "seq"):
        distance = 1
        while distance < lax.axis_size(axis):
            stages.append((axis, distance))
            distance *= 2
    plan = halving_plan(cells.shape[0], cells.shape[1], len(stages))
    held = cells
    for (axis, distance), dim in zip(stages, plan):
        bit = (lax.axis_index(axis) // distance) % 2
        size = held.shape[dim] // 2
        keep = lax.dynamic_slice_in_dim(held, bit * size, size, axis=dim)
        give = lax.dynamic_slice_in_dim(held, (1 - bit) * size, size, axis=dim)
        held = keep + swap(give, axis, distance)
    for (axis, distance), dim in reversed(list(zip(stages, plan))):
        bit = (lax.axis_index(axis) // distance) % 2
        size = held.shape[dim]
        other = swap(held, axis, distance)
        full = jnp.concatenate([held, held], axis=dim)
        full = lax.dynamic_update_slice_in_dim(full, held, bit * size, axis=dim)
        held = lax.dynamic_update_slice_in_dim(full, other, (1 - bit) * size, axis=dim)
    return held.reshape(shape)


def point_gradient(act_rows, cot_rows):
    return lax.dot_general(
        act_rows, cot_rows, (((0,), (0,)), ((), ())), preferred_element_type=jnp.float32
    )


def on_device(inputs, lengths, conv_weight, point_weight, cotangent):
    local_bins = inputs.shape[1]
    chans = inputs.shape[2]
    seq_count = lax.axis_size("seq")
    rep_count = lax.axis_size("rep")
    seq_index = lax.axis_index("seq")
    positions = seq_index * local_bins + jnp.arange(local_bins, dtype=jnp.int32)
    mask = (positions[None, :] < lengths[:, None]).astype(jnp.float32)
    mask3 = mask[:, :, None]
    masked_input = (inputs.astype(jnp.float32) * mask3).astype(jnp.bfloat16)
    scale = 1.0 / math.sqrt(rep_count * seq_count * local_bins)
    padded_input = with_halo(masked_input, (("seq", 1),), DILATION_STEP)
    dense = dense_weight(conv_weight)
    pre = conv_taps(padded_input, dense, local_bins)
    act_val, slope = gelu_pair(pre)
    act = (act_val * mask3).astype(jnp.bfloat16)
    act_rows = act.reshape(local_bins, chans)
    cot_rows = cotangent.reshape(local_bins, chans)
    proj = jnp.dot(act_rows, point_weight, preferred_element_type=jnp.float32).reshape(inputs.shape)
    output = (inputs.astype(jnp.float32) + proj).astype(jnp.bfloat16)
    point_partial = point_gradient(act_rows, cot_rows) * scale
    point_partial, cot_rows = lax.optimization_barrier((point_partial, cot_rows))
    grad_point = lax.psum_scatter(
        point_partial, ("seq", "rep"), scatter_dimension=0, tiled=True
    )
    back = lax.dot_general(
        cot_rows, point_weight, (((1,), (1,)), ((), ())), preferred_element_type=jnp.float32
    )
    preactivation_gradient = (back.reshape(inputs.shape) * slope * mask3).astype(jnp.bfloat16)
    padded_gradient = with_halo(preactivation_gradient, (("seq", 1),), DILATION_STEP)
    spread = conv_taps(padded_gradient, dense, local_bins, transpose=True)
    conv_local = weight_taps(padded_input, preactivation_gradient, local_bins)
    grad_conv = tree_sum(conv_local) * scale
    grad_inputs = (cotangent.astype(jnp.float32) + mask3 * spread).astype(jnp.bfloat16)
    return (output, grad_inputs, grad_point, grad_conv)


def solution(mesh):
    return jax.shard_map(
        on_device,
        mesh=mesh,
        in_specs=(
            P(("groups", "rep"), "seq", None),
            P(("groups", "rep")),
            P(),
            P(),
            P(("groups", "rep"), "seq", None),
        ),
        out_specs=(
            P(("groups", "rep"), "seq", None),
            P(("groups", "rep"), "seq", None),
            P(("groups", "seq", "rep"), None),
            P("groups", None, None),
        ),
        check_vma=False,
    )
```

```python
import functools
import math

import jax
import jax.numpy as jnp
from jax import lax
from jax.sharding import PartitionSpec as P

GROUP_CHANNELS = 48
DILATION_STEP = 64


def with_halo(cells, sides, width):
    for axis, dim in sides:
        count = lax.axis_size(axis)
        ends = count - 1
        head = lax.slice_in_dim(cells, 0, width, axis=dim)
        tail = lax.slice_in_dim(cells, cells.shape[dim] - width, cells.shape[dim], axis=dim)
        cells = jnp.concatenate(
            [
                lax.ppermute(tail, axis, [(i, (i + 1) % count) for i in range(ends)]),
                cells,
                lax.ppermute(head, axis, [((i + 1) % count, i) for i in range(ends)]),
            ],
            axis=dim,
        )
    return cells


def gelu_pair(pre):
    cdf = 0.5 * (1.0 + jax.scipy.special.erf(pre * 0.7071067811865476))
    dens = jnp.exp(-0.5 * pre * pre) * 0.3989422804014327
    return (pre * cdf, cdf + pre * dens)


CHUNK = 384


def group_mask(rows, chans, dtype):
    row_group = lax.broadcasted_iota(jnp.int32, (rows, chans), 0) // GROUP_CHANNELS
    col_group = (lax.broadcasted_iota(jnp.int32, (rows, chans), 1) % CHUNK) // GROUP_CHANNELS
    return (row_group == col_group).astype(dtype)


def dense_weight(weight):
    taps, width, chans = weight.shape
    groups = CHUNK // width
    tiled = jnp.tile(weight, (1, groups, 1))
    return tiled * group_mask(CHUNK, chans, weight.dtype)[None]


def conv_taps(padded_input, dense, sequence_length, transpose=False):
    rows = padded_input[0]
    chunks = dense.shape[2] // CHUNK
    parts = []
    for c in range(chunks):
        cols = slice(c * CHUNK, (c + 1) * CHUNK)
        total = None
        for k in range(3):
            start = (2 - k if transpose else k) * DILATION_STEP
            window = rows[start : start + sequence_length, cols]
            dims = (((1,), (1,)), ((), ())) if transpose else (((1,), (0,)), ((), ()))
            term = lax.dot_general(
                window, dense[k, :, cols], dims, preferred_element_type=jnp.float32
            )
            total = term if total is None else total + term
        parts.append(total)
    return jnp.concatenate(parts, axis=1)[None]


def weight_taps(input_padded, output_gradient, sequence_length):
    rows = input_padded[0]
    grads = output_gradient[0]
    chans = grads.shape[1]
    chunks = chans // CHUNK
    groups = CHUNK // GROUP_CHANNELS
    mask = group_mask(CHUNK, CHUNK, jnp.float32).reshape(groups, GROUP_CHANNELS, CHUNK)
    taps = []
    for k in range(3):
        parts = []
        for c in range(chunks):
            cols = slice(c * CHUNK, (c + 1) * CHUNK)
            window = rows[k * DILATION_STEP : k * DILATION_STEP + sequence_length, cols]
            full = lax.dot_general(
                window, grads[:, cols], (((0,), (0,)), ((), ())),
                preferred_element_type=jnp.float32,
            ).reshape(groups, GROUP_CHANNELS, CHUNK)
            parts.append(jnp.sum(full * mask, axis=0))
        taps.append(jnp.concatenate(parts, axis=1))
    return jnp.stack(taps)


def swap(value, axis, distance):
    count = lax.axis_size(axis)
    return lax.ppermute(value, axis, [(i, i ^ distance) for i in range(count)])


def halving_plan(rows, cols, steps):
    plan = []
    for _ in range(steps):
        if cols % 256 == 0:
            plan.append(1)
            cols //= 2
        else:
            plan.append(0)
            rows //= 2
    return plan


def tree_sum(value):
    shape = value.shape
    cells = value.reshape(-1, shape[-1])
    stages = []
    for axis in ("rep", "seq"):
        distance = 1
        while distance < lax.axis_size(axis):
            stages.append((axis, distance))
            distance *= 2
    plan = halving_plan(cells.shape[0], cells.shape[1], len(stages))
    held = cells
    for (axis, distance), dim in zip(stages, plan):
        bit = (lax.axis_index(axis) // distance) % 2
        size = held.shape[dim] // 2
        keep = lax.dynamic_slice_in_dim(held, bit * size, size, axis=dim)
        give = lax.dynamic_slice_in_dim(held, (1 - bit) * size, size, axis=dim)
        held = keep + swap(give, axis, distance)
    for (axis, distance), dim in reversed(list(zip(stages, plan))):
        bit = (lax.axis_index(axis) // distance) % 2
        size = held.shape[dim]
        other = swap(held, axis, distance)
        full = jnp.concatenate([held, held], axis=dim)
        full = lax.dynamic_update_slice_in_dim(full, held, bit * size, axis=dim)
        held = lax.dynamic_update_slice_in_dim(full, other, (1 - bit) * size, axis=dim)
    return held.reshape(shape)


def ring_order(mesh):
    count = mesh.shape["seq"]
    names = mesh.axis_names
    index = [0] * len(names)
    cells = []
    for s in range(count):
        index[names.index("seq")] = s
        coords = getattr(mesh.devices[tuple(index)], "coords", None)
        if coords is None:
            return False
        cells.append((tuple(coords), s))
    cells.sort(key=lambda cell: (cell[0][1], cell[0][2] if cell[0][1] % 2 == 0 else -cell[0][2]))
    half = count // 2
    snake = [2 * p if p < half else 2 * (count - 1 - p) + 1 for p in range(count)]
    return count % 2 == 0 and [s for _, s in cells] == snake


def ring_reduce_scatter(blocks, snake):
    count = blocks.shape[0]
    half_count = count // 2
    if snake:
        ring = [2 * p if p < half_count else 2 * (count - 1 - p) + 1 for p in range(count)]
    else:
        ring = list(range(count))
    seq_index = lax.axis_index("seq")
    if snake:
        here = jnp.where(seq_index % 2 == 0, seq_index // 2, count - 1 - seq_index // 2)
    else:
        here = seq_index
    cols = blocks.shape[2] // 2
    forward = [(ring[i], ring[(i + 1) % count]) for i in range(count)]
    backward = [(ring[i], ring[(i - 1) % count]) for i in range(count)]

    def block(offset, low):
        spot = (here + offset + count) % count
        if snake:
            owner = jnp.where(spot < half_count, 2 * spot, 2 * (count - 1 - spot) + 1)
        else:
            owner = spot
        rows = lax.dynamic_index_in_dim(blocks, owner, axis=0, keepdims=False)
        return rows[:, :cols] if low else rows[:, cols:]

    ahead = block(-1, True)
    behind = block(1, False)
    for step in range(count - 1):
        ahead = lax.ppermute(ahead, "seq", forward) + block(-2 - step, True)
        behind = lax.ppermute(behind, "seq", backward) + block(2 + step, False)
    return jnp.concatenate([ahead, behind], axis=1)


def point_gradient(act_rows, cot_rows, scale, snake):
    chans = act_rows.shape[1]
    seq_count = lax.axis_size("seq")
    rep_count = lax.axis_size("rep")
    product = lambda a, b: lax.dot_general(
        a, b, (((0,), (0,)), ((), ())), preferred_element_type=jnp.float32
    ) * scale
    if rep_count != 2:
        partial = product(act_rows, cot_rows)
        partial, cot_rows = lax.optimization_barrier((partial, cot_rows))
        total = lax.psum_scatter(partial, ("seq", "rep"), scatter_dimension=0, tiled=True)
        return total, cot_rows
    block = chans // (seq_count * rep_count)
    blocks = act_rows.reshape(act_rows.shape[0], seq_count, rep_count, block)
    rep_index = lax.axis_index("rep")

    def rows_of(owner):
        cols = lax.dynamic_index_in_dim(blocks, owner, axis=2, keepdims=False)
        cols = cols.reshape(act_rows.shape[0], seq_count * block)
        return product(cols, cot_rows).reshape(seq_count, block, chans)

    mine = rows_of(rep_index) + swap(rows_of(1 - rep_index), "rep", 1)
    mine, cot_rows = lax.optimization_barrier((mine, cot_rows))
    return ring_reduce_scatter(mine, snake), cot_rows


def on_device(snake, inputs, lengths, conv_weight, point_weight, cotangent):
    local_bins = inputs.shape[1]
    chans = inputs.shape[2]
    seq_count = lax.axis_size("seq")
    rep_count = lax.axis_size("rep")
    seq_index = lax.axis_index("seq")
    positions = seq_index * local_bins + jnp.arange(local_bins, dtype=jnp.int32)
    mask = (positions[None, :] < lengths[:, None]).astype(jnp.float32)
    mask3 = mask[:, :, None]
    masked_input = (inputs.astype(jnp.float32) * mask3).astype(jnp.bfloat16)
    scale = 1.0 / math.sqrt(rep_count * seq_count * local_bins)
    padded_input = with_halo(masked_input, (("seq", 1),), DILATION_STEP)
    dense = dense_weight(conv_weight)
    pre = conv_taps(padded_input, dense, local_bins)
    act_val, slope = gelu_pair(pre)
    act = (act_val * mask3).astype(jnp.bfloat16)
    act_rows = act.reshape(local_bins, chans)
    cot_rows = cotangent.reshape(local_bins, chans)
    proj = jnp.dot(act_rows, point_weight, preferred_element_type=jnp.float32).reshape(inputs.shape)
    output = (inputs.astype(jnp.float32) + proj).astype(jnp.bfloat16)
    grad_point, cot_rows = point_gradient(act_rows, cot_rows, scale, snake)
    back = lax.dot_general(
        cot_rows, point_weight, (((1,), (1,)), ((), ())), preferred_element_type=jnp.float32
    )
    preactivation_gradient = (back.reshape(inputs.shape) * slope * mask3).astype(jnp.bfloat16)
    padded_gradient = with_halo(preactivation_gradient, (("seq", 1),), DILATION_STEP)
    spread = conv_taps(padded_gradient, dense, local_bins, transpose=True)
    conv_local = weight_taps(padded_input, preactivation_gradient, local_bins)
    grad_conv = tree_sum(conv_local) * scale
    grad_inputs = (cotangent.astype(jnp.float32) + mask3 * spread).astype(jnp.bfloat16)
    return (output, grad_inputs, grad_point, grad_conv)


def solution(mesh):
    return jax.shard_map(
        functools.partial(on_device, ring_order(mesh)),
        mesh=mesh,
        in_specs=(
            P(("groups", "rep"), "seq", None),
            P(("groups", "rep")),
            P(),
            P(),
            P(("groups", "rep"), "seq", None),
        ),
        out_specs=(
            P(("groups", "rep"), "seq", None),
            P(("groups", "rep"), "seq", None),
            P(("groups", "seq", "rep"), None),
            P("groups", None, None),
        ),
        check_vma=False,
    )
```

```python
import functools
import math

import jax
import jax.numpy as jnp
from jax import lax
from jax.sharding import PartitionSpec as P

GROUP_CHANNELS = 48
DILATION_STEP = 64


def with_halo(cells, sides, width):
    for axis, dim in sides:
        count = lax.axis_size(axis)
        ends = count - 1
        head = lax.slice_in_dim(cells, 0, width, axis=dim)
        tail = lax.slice_in_dim(cells, cells.shape[dim] - width, cells.shape[dim], axis=dim)
        cells = jnp.concatenate(
            [
                lax.ppermute(tail, axis, [(i, (i + 1) % count) for i in range(ends)]),
                cells,
                lax.ppermute(head, axis, [((i + 1) % count, i) for i in range(ends)]),
            ],
            axis=dim,
        )
    return cells


def gelu_pair(pre):
    cdf = 0.5 * (1.0 + jax.scipy.special.erf(pre * 0.7071067811865476))
    dens = jnp.exp(-0.5 * pre * pre) * 0.3989422804014327
    return (pre * cdf, cdf + pre * dens)


CHUNK = 384


def group_mask(rows, chans, dtype):
    row_group = lax.broadcasted_iota(jnp.int32, (rows, chans), 0) // GROUP_CHANNELS
    col_group = (lax.broadcasted_iota(jnp.int32, (rows, chans), 1) % CHUNK) // GROUP_CHANNELS
    return (row_group == col_group).astype(dtype)


def dense_weight(weight):
    taps, width, chans = weight.shape
    groups = CHUNK // width
    tiled = jnp.tile(weight, (1, groups, 1))
    return tiled * group_mask(CHUNK, chans, weight.dtype)[None]


def conv_taps(padded_input, dense, sequence_length, transpose=False):
    rows = padded_input[0]
    chunks = dense.shape[2] // CHUNK
    parts = []
    for c in range(chunks):
        cols = slice(c * CHUNK, (c + 1) * CHUNK)
        total = None
        for k in range(3):
            start = (2 - k if transpose else k) * DILATION_STEP
            window = rows[start : start + sequence_length, cols]
            dims = (((1,), (1,)), ((), ())) if transpose else (((1,), (0,)), ((), ()))
            term = lax.dot_general(
                window, dense[k, :, cols], dims, preferred_element_type=jnp.float32
            )
            total = term if total is None else total + term
        parts.append(total)
    return jnp.concatenate(parts, axis=1)[None]


def weight_taps(input_padded, output_gradient, sequence_length):
    rows = input_padded[0]
    grads = output_gradient[0]
    chans = grads.shape[1]
    chunks = chans // CHUNK
    groups = CHUNK // GROUP_CHANNELS
    mask = group_mask(CHUNK, CHUNK, jnp.float32).reshape(groups, GROUP_CHANNELS, CHUNK)
    taps = []
    for k in range(3):
        parts = []
        for c in range(chunks):
            cols = slice(c * CHUNK, (c + 1) * CHUNK)
            window = rows[k * DILATION_STEP : k * DILATION_STEP + sequence_length, cols]
            full = lax.dot_general(
                window, grads[:, cols], (((0,), (0,)), ((), ())),
                preferred_element_type=jnp.float32,
            ).reshape(groups, GROUP_CHANNELS, CHUNK)
            parts.append(jnp.sum(full * mask, axis=0))
        taps.append(jnp.concatenate(parts, axis=1))
    return jnp.stack(taps)


def swap(value, axis, distance):
    count = lax.axis_size(axis)
    return lax.ppermute(value, axis, [(i, i ^ distance) for i in range(count)])


def halving_plan(rows, cols, steps):
    plan = []
    for _ in range(steps):
        if cols % 256 == 0:
            plan.append(1)
            cols //= 2
        else:
            plan.append(0)
            rows //= 2
    return plan


def tree_sum(value):
    shape = value.shape
    cells = value.reshape(-1, shape[-1])
    stages = []
    for axis in ("rep", "seq"):
        distance = 1
        while distance < lax.axis_size(axis):
            stages.append((axis, distance))
            distance *= 2
    plan = halving_plan(cells.shape[0], cells.shape[1], len(stages))
    held = cells
    for (axis, distance), dim in zip(stages, plan):
        bit = (lax.axis_index(axis) // distance) % 2
        size = held.shape[dim] // 2
        keep = lax.dynamic_slice_in_dim(held, bit * size, size, axis=dim)
        give = lax.dynamic_slice_in_dim(held, (1 - bit) * size, size, axis=dim)
        held = keep + swap(give, axis, distance)
    for (axis, distance), dim in reversed(list(zip(stages, plan))):
        bit = (lax.axis_index(axis) // distance) % 2
        size = held.shape[dim]
        other = swap(held, axis, distance)
        full = jnp.concatenate([held, held], axis=dim)
        full = lax.dynamic_update_slice_in_dim(full, held, bit * size, axis=dim)
        held = lax.dynamic_update_slice_in_dim(full, other, (1 - bit) * size, axis=dim)
    return held.reshape(shape)


def ring_order(mesh):
    count = mesh.shape["seq"]
    names = mesh.axis_names
    index = [0] * len(names)
    cells = []
    for s in range(count):
        index[names.index("seq")] = s
        coords = getattr(mesh.devices[tuple(index)], "coords", None)
        if coords is None:
            return False
        cells.append((tuple(coords), s))
    cells.sort(key=lambda cell: (cell[0][1], cell[0][2] if cell[0][1] % 2 == 0 else -cell[0][2]))
    half = count // 2
    snake = [2 * p if p < half else 2 * (count - 1 - p) + 1 for p in range(count)]
    return count % 2 == 0 and [s for _, s in cells] == snake


def ring_reduce_scatter(blocks, snake, hold):
    count = blocks.shape[0]
    half_count = count // 2
    if snake:
        ring = [2 * p if p < half_count else 2 * (count - 1 - p) + 1 for p in range(count)]
    else:
        ring = list(range(count))
    seq_index = lax.axis_index("seq")
    if snake:
        here = jnp.where(seq_index % 2 == 0, seq_index // 2, count - 1 - seq_index // 2)
    else:
        here = seq_index
    cols = blocks.shape[2] // 2
    forward = [(ring[i], ring[(i + 1) % count]) for i in range(count)]
    backward = [(ring[i], ring[(i - 1) % count]) for i in range(count)]

    def block(offset, low):
        spot = (here + offset + count) % count
        if snake:
            owner = jnp.where(spot < half_count, 2 * spot, 2 * (count - 1 - spot) + 1)
        else:
            owner = spot
        rows = lax.dynamic_index_in_dim(blocks, owner, axis=0, keepdims=False)
        return rows[:, :cols] if low else rows[:, cols:]

    ahead = block(-1, True)
    behind = block(1, False)
    for step in range(count - 1):
        ahead = lax.ppermute(ahead, "seq", forward) + block(-2 - step, True)
        behind = lax.ppermute(behind, "seq", backward) + block(2 + step, False)
        if step == 0:
            ahead, behind, hold = lax.optimization_barrier((ahead, behind, hold))
    return jnp.concatenate([ahead, behind], axis=1), hold


def point_gradient(act_rows, cot_rows, scale, snake, hold):
    chans = act_rows.shape[1]
    seq_count = lax.axis_size("seq")
    rep_count = lax.axis_size("rep")
    product = lambda a, b: lax.dot_general(
        a, b, (((0,), (0,)), ((), ())), preferred_element_type=jnp.float32
    ) * scale
    if rep_count != 2:
        partial = product(act_rows, cot_rows)
        partial, hold = lax.optimization_barrier((partial, hold))
        total = lax.psum_scatter(partial, ("seq", "rep"), scatter_dimension=0, tiled=True)
        return total, hold
    block = chans // (seq_count * rep_count)
    blocks = act_rows.reshape(act_rows.shape[0], seq_count, rep_count, block)
    rep_index = lax.axis_index("rep")

    def rows_of(owner):
        cols = lax.dynamic_index_in_dim(blocks, owner, axis=2, keepdims=False)
        cols = cols.reshape(act_rows.shape[0], seq_count * block)
        return product(cols, cot_rows).reshape(seq_count, block, chans)

    mine = rows_of(rep_index) + swap(rows_of(1 - rep_index), "rep", 1)
    return ring_reduce_scatter(mine, snake, hold)


def on_device(snake, inputs, lengths, conv_weight, point_weight, cotangent):
    local_bins = inputs.shape[1]
    chans = inputs.shape[2]
    seq_count = lax.axis_size("seq")
    rep_count = lax.axis_size("rep")
    seq_index = lax.axis_index("seq")
    positions = seq_index * local_bins + jnp.arange(local_bins, dtype=jnp.int32)
    mask = (positions[None, :] < lengths[:, None]).astype(jnp.float32)
    mask3 = mask[:, :, None]
    masked_input = (inputs.astype(jnp.float32) * mask3).astype(jnp.bfloat16)
    scale = 1.0 / math.sqrt(rep_count * seq_count * local_bins)
    padded_input = with_halo(masked_input, (("seq", 1),), DILATION_STEP)
    dense = dense_weight(conv_weight)
    pre = conv_taps(padded_input, dense, local_bins)
    act_val, slope = gelu_pair(pre)
    act = (act_val * mask3).astype(jnp.bfloat16)
    act_rows = act.reshape(local_bins, chans)
    cot_rows = cotangent.reshape(local_bins, chans)
    proj = jnp.dot(act_rows, point_weight, preferred_element_type=jnp.float32).reshape(inputs.shape)
    output = (inputs.astype(jnp.float32) + proj).astype(jnp.bfloat16)
    back = lax.dot_general(
        cot_rows, point_weight, (((1,), (1,)), ((), ())), preferred_element_type=jnp.float32
    )
    grad_point, back = point_gradient(act_rows, cot_rows, scale, snake, back)
    preactivation_gradient = (back.reshape(inputs.shape) * slope * mask3).astype(jnp.bfloat16)
    padded_gradient = with_halo(preactivation_gradient, (("seq", 1),), DILATION_STEP)
    spread = conv_taps(padded_gradient, dense, local_bins, transpose=True)
    conv_local = weight_taps(padded_input, preactivation_gradient, local_bins)
    grad_conv = tree_sum(conv_local) * scale
    grad_inputs = (cotangent.astype(jnp.float32) + mask3 * spread).astype(jnp.bfloat16)
    return (output, grad_inputs, grad_point, grad_conv)


def solution(mesh):
    return jax.shard_map(
        functools.partial(on_device, ring_order(mesh)),
        mesh=mesh,
        in_specs=(
            P(("groups", "rep"), "seq", None),
            P(("groups", "rep")),
            P(),
            P(),
            P(("groups", "rep"), "seq", None),
        ),
        out_specs=(
            P(("groups", "rep"), "seq", None),
            P(("groups", "rep"), "seq", None),
            P(("groups", "seq", "rep"), None),
            P("groups", None, None),
        ),
        check_vma=False,
    )
```

```python
import functools
import math

import jax
import jax.numpy as jnp
from jax import lax
from jax.sharding import PartitionSpec as P

GROUP_CHANNELS = 48
DILATION_STEP = 64


def with_halo(cells, sides, width):
    for axis, dim in sides:
        count = lax.axis_size(axis)
        ends = count - 1
        head = lax.slice_in_dim(cells, 0, width, axis=dim)
        tail = lax.slice_in_dim(cells, cells.shape[dim] - width, cells.shape[dim], axis=dim)
        cells = jnp.concatenate(
            [
                lax.ppermute(tail, axis, [(i, (i + 1) % count) for i in range(ends)]),
                cells,
                lax.ppermute(head, axis, [((i + 1) % count, i) for i in range(ends)]),
            ],
            axis=dim,
        )
    return cells


def gelu_pair(pre):
    cdf = 0.5 * (1.0 + jax.scipy.special.erf(pre * 0.7071067811865476))
    dens = jnp.exp(-0.5 * pre * pre) * 0.3989422804014327
    return (pre * cdf, cdf + pre * dens)


CHUNK = 384


def group_mask(rows, chans, dtype):
    row_group = lax.broadcasted_iota(jnp.int32, (rows, chans), 0) // GROUP_CHANNELS
    col_group = (lax.broadcasted_iota(jnp.int32, (rows, chans), 1) % CHUNK) // GROUP_CHANNELS
    return (row_group == col_group).astype(dtype)


def dense_weight(weight):
    taps, width, chans = weight.shape
    groups = CHUNK // width
    tiled = jnp.tile(weight, (1, groups, 1))
    return tiled * group_mask(CHUNK, chans, weight.dtype)[None]


def conv_taps(padded_input, dense, sequence_length, transpose=False):
    rows = padded_input[0]
    chunks = dense.shape[2] // CHUNK
    parts = []
    for c in range(chunks):
        cols = slice(c * CHUNK, (c + 1) * CHUNK)
        total = None
        for k in range(3):
            start = (2 - k if transpose else k) * DILATION_STEP
            window = rows[start : start + sequence_length, cols]
            dims = (((1,), (1,)), ((), ())) if transpose else (((1,), (0,)), ((), ()))
            term = lax.dot_general(
                window, dense[k, :, cols], dims, preferred_element_type=jnp.float32
            )
            total = term if total is None else total + term
        parts.append(total)
    return jnp.concatenate(parts, axis=1)[None]


def weight_taps(input_padded, output_gradient, sequence_length):
    rows = input_padded[0]
    grads = output_gradient[0]
    chans = grads.shape[1]
    chunks = chans // CHUNK
    groups = CHUNK // GROUP_CHANNELS
    mask = group_mask(CHUNK, CHUNK, jnp.float32).reshape(groups, GROUP_CHANNELS, CHUNK)
    taps = []
    for k in range(3):
        parts = []
        for c in range(chunks):
            cols = slice(c * CHUNK, (c + 1) * CHUNK)
            window = rows[k * DILATION_STEP : k * DILATION_STEP + sequence_length, cols]
            full = lax.dot_general(
                window, grads[:, cols], (((0,), (0,)), ((), ())),
                preferred_element_type=jnp.float32,
            ).reshape(groups, GROUP_CHANNELS, CHUNK)
            parts.append(jnp.sum(full * mask, axis=0))
        taps.append(jnp.concatenate(parts, axis=1))
    return jnp.stack(taps)


def swap(value, axis, distance):
    count = lax.axis_size(axis)
    return lax.ppermute(value, axis, [(i, i ^ distance) for i in range(count)])


def halving_plan(rows, cols, steps):
    plan = []
    for _ in range(steps):
        if cols % 256 == 0:
            plan.append(1)
            cols //= 2
        else:
            plan.append(0)
            rows //= 2
    return plan


def tree_sum(value):
    shape = value.shape
    cells = value.reshape(-1, shape[-1])
    stages = []
    for axis in ("rep", "seq"):
        distance = 1
        while distance < lax.axis_size(axis):
            stages.append((axis, distance))
            distance *= 2
    plan = halving_plan(cells.shape[0], cells.shape[1], len(stages))
    held = cells
    for (axis, distance), dim in zip(stages, plan):
        bit = (lax.axis_index(axis) // distance) % 2
        size = held.shape[dim] // 2
        keep = lax.dynamic_slice_in_dim(held, bit * size, size, axis=dim)
        give = lax.dynamic_slice_in_dim(held, (1 - bit) * size, size, axis=dim)
        held = keep + swap(give, axis, distance)
    for (axis, distance), dim in reversed(list(zip(stages, plan))):
        bit = (lax.axis_index(axis) // distance) % 2
        size = held.shape[dim]
        other = swap(held, axis, distance)
        full = jnp.concatenate([held, held], axis=dim)
        full = lax.dynamic_update_slice_in_dim(full, held, bit * size, axis=dim)
        held = lax.dynamic_update_slice_in_dim(full, other, (1 - bit) * size, axis=dim)
    return held.reshape(shape)


def ring_order(mesh):
    count = mesh.shape["seq"]
    names = mesh.axis_names
    index = [0] * len(names)
    cells = []
    for s in range(count):
        index[names.index("seq")] = s
        coords = getattr(mesh.devices[tuple(index)], "coords", None)
        if coords is None:
            return False
        cells.append((tuple(coords), s))
    cells.sort(key=lambda cell: (cell[0][1], cell[0][2] if cell[0][1] % 2 == 0 else -cell[0][2]))
    half = count // 2
    snake = [2 * p if p < half else 2 * (count - 1 - p) + 1 for p in range(count)]
    return count % 2 == 0 and [s for _, s in cells] == snake


def ring_reduce_scatter(blocks, snake):
    count = blocks.shape[0]
    half_count = count // 2
    if snake:
        ring = [2 * p if p < half_count else 2 * (count - 1 - p) + 1 for p in range(count)]
    else:
        ring = list(range(count))
    seq_index = lax.axis_index("seq")
    if snake:
        here = jnp.where(seq_index % 2 == 0, seq_index // 2, count - 1 - seq_index // 2)
    else:
        here = seq_index
    cols = blocks.shape[2] // 2
    forward = [(ring[i], ring[(i + 1) % count]) for i in range(count)]
    backward = [(ring[i], ring[(i - 1) % count]) for i in range(count)]

    def block(offset, low):
        spot = (here + offset + count) % count
        if snake:
            owner = jnp.where(spot < half_count, 2 * spot, 2 * (count - 1 - spot) + 1)
        else:
            owner = spot
        rows = lax.dynamic_index_in_dim(blocks, owner, axis=0, keepdims=False)
        return rows[:, :cols] if low else rows[:, cols:]

    ahead = block(-1, True)
    behind = block(1, False)
    for step in range(count - 1):
        ahead = lax.ppermute(ahead, "seq", forward) + block(-2 - step, True)
        behind = lax.ppermute(behind, "seq", backward) + block(2 + step, False)
    return jnp.concatenate([ahead, behind], axis=1)


def point_gradient(act_rows, cot_rows, scale, snake):
    chans = act_rows.shape[1]
    seq_count = lax.axis_size("seq")
    rep_count = lax.axis_size("rep")
    product = lambda a, b: lax.dot_general(
        a, b, (((0,), (0,)), ((), ())), preferred_element_type=jnp.float32
    ) * scale
    if rep_count != 2:
        partial = product(act_rows, cot_rows)
        partial, cot_rows = lax.optimization_barrier((partial, cot_rows))
        total = lax.psum_scatter(partial, ("seq", "rep"), scatter_dimension=0, tiled=True)
        return total, cot_rows
    block = chans // (seq_count * rep_count)
    blocks = act_rows.reshape(act_rows.shape[0], seq_count, rep_count, block)
    rep_index = lax.axis_index("rep")

    def rows_of(owner):
        cols = lax.dynamic_index_in_dim(blocks, owner, axis=2, keepdims=False)
        cols = cols.reshape(act_rows.shape[0], seq_count * block)
        return product(cols, cot_rows).reshape(seq_count, block, chans)

    mine = rows_of(rep_index) + swap(rows_of(1 - rep_index), "rep", 1)
    mine, cot_rows = lax.optimization_barrier((mine, cot_rows))
    return ring_reduce_scatter(mine, snake), cot_rows


def on_device(snake, inputs, lengths, conv_weight, point_weight, cotangent):
    local_bins = inputs.shape[1]
    chans = inputs.shape[2]
    seq_count = lax.axis_size("seq")
    rep_count = lax.axis_size("rep")
    seq_index = lax.axis_index("seq")
    positions = seq_index * local_bins + jnp.arange(local_bins, dtype=jnp.int32)
    mask = (positions[None, :] < lengths[:, None]).astype(jnp.float32)
    mask3 = mask[:, :, None]
    masked_input = (inputs.astype(jnp.float32) * mask3).astype(jnp.bfloat16)
    scale = 1.0 / math.sqrt(rep_count * seq_count * local_bins)
    padded_input = with_halo(masked_input, (("seq", 1),), DILATION_STEP)
    dense = dense_weight(conv_weight)
    pre = conv_taps(padded_input, dense, local_bins)
    act_val, slope = gelu_pair(pre)
    act = (act_val * mask3).astype(jnp.bfloat16)
    act_rows = act.reshape(local_bins, chans)
    cot_rows = cotangent.reshape(local_bins, chans)
    proj = jnp.dot(act_rows, point_weight, preferred_element_type=jnp.float32).reshape(inputs.shape)
    output = (inputs.astype(jnp.float32) + proj).astype(jnp.bfloat16)
    grad_point, cot_rows = point_gradient(act_rows, cot_rows, scale, snake)
    back = lax.dot_general(
        cot_rows, point_weight, (((1,), (1,)), ((), ())), preferred_element_type=jnp.float32
    )
    preactivation_gradient = (back.reshape(inputs.shape) * slope * mask3).astype(jnp.bfloat16)
    padded_gradient = with_halo(preactivation_gradient, (("seq", 1),), DILATION_STEP)
    spread = conv_taps(padded_gradient, dense, local_bins, transpose=True)
    conv_local = weight_taps(padded_input, preactivation_gradient, local_bins)
    grad_point, conv_local = lax.optimization_barrier((grad_point, conv_local))
    grad_conv = tree_sum(conv_local) * scale
    grad_inputs = (cotangent.astype(jnp.float32) + mask3 * spread).astype(jnp.bfloat16)
    return (output, grad_inputs, grad_point, grad_conv)


def solution(mesh):
    return jax.shard_map(
        functools.partial(on_device, ring_order(mesh)),
        mesh=mesh,
        in_specs=(
            P(("groups", "rep"), "seq", None),
            P(("groups", "rep")),
            P(),
            P(),
            P(("groups", "rep"), "seq", None),
        ),
        out_specs=(
            P(("groups", "rep"), "seq", None),
            P(("groups", "rep"), "seq", None),
            P(("groups", "seq", "rep"), None),
            P("groups", None, None),
        ),
        check_vma=False,
    )
```

```python
import functools
import math

import jax
import jax.numpy as jnp
from jax import lax
from jax.sharding import PartitionSpec as P

GROUP_CHANNELS = 48
DILATION_STEP = 64


def with_halo(cells, sides, width):
    for axis, dim in sides:
        count = lax.axis_size(axis)
        ends = count - 1
        head = lax.slice_in_dim(cells, 0, width, axis=dim)
        tail = lax.slice_in_dim(cells, cells.shape[dim] - width, cells.shape[dim], axis=dim)
        cells = jnp.concatenate(
            [
                lax.ppermute(tail, axis, [(i, (i + 1) % count) for i in range(ends)]),
                cells,
                lax.ppermute(head, axis, [((i + 1) % count, i) for i in range(ends)]),
            ],
            axis=dim,
        )
    return cells


def gelu_pair(pre):
    cdf = 0.5 * (1.0 + jax.scipy.special.erf(pre * 0.7071067811865476))
    dens = jnp.exp(-0.5 * pre * pre) * 0.3989422804014327
    return (pre * cdf, cdf + pre * dens)


CHUNK = 384


def group_mask(rows, chans, dtype):
    row_group = lax.broadcasted_iota(jnp.int32, (rows, chans), 0) // GROUP_CHANNELS
    col_group = (lax.broadcasted_iota(jnp.int32, (rows, chans), 1) % CHUNK) // GROUP_CHANNELS
    return (row_group == col_group).astype(dtype)


def dense_weight(weight):
    taps, width, chans = weight.shape
    groups = CHUNK // width
    tiled = jnp.tile(weight, (1, groups, 1))
    return tiled * group_mask(CHUNK, chans, weight.dtype)[None]


def conv_taps(padded_input, dense, sequence_length, transpose=False):
    rows = padded_input[0]
    chunks = dense.shape[2] // CHUNK
    parts = []
    for c in range(chunks):
        cols = slice(c * CHUNK, (c + 1) * CHUNK)
        total = None
        for k in range(3):
            start = (2 - k if transpose else k) * DILATION_STEP
            window = rows[start : start + sequence_length, cols]
            dims = (((1,), (1,)), ((), ())) if transpose else (((1,), (0,)), ((), ()))
            term = lax.dot_general(
                window, dense[k, :, cols], dims, preferred_element_type=jnp.float32
            )
            total = term if total is None else total + term
        parts.append(total)
    return jnp.concatenate(parts, axis=1)[None]


def weight_taps(input_padded, output_gradient, sequence_length):
    rows = input_padded[0]
    grads = output_gradient[0]
    chans = grads.shape[1]
    chunks = chans // CHUNK
    groups = CHUNK // GROUP_CHANNELS
    mask = group_mask(CHUNK, CHUNK, jnp.float32).reshape(groups, GROUP_CHANNELS, CHUNK)
    taps = []
    for k in range(3):
        parts = []
        for c in range(chunks):
            cols = slice(c * CHUNK, (c + 1) * CHUNK)
            window = rows[k * DILATION_STEP : k * DILATION_STEP + sequence_length, cols]
            full = lax.dot_general(
                window, grads[:, cols], (((0,), (0,)), ((), ())),
                preferred_element_type=jnp.float32,
            ).reshape(groups, GROUP_CHANNELS, CHUNK)
            parts.append(jnp.sum(full * mask, axis=0))
        taps.append(jnp.concatenate(parts, axis=1))
    return jnp.stack(taps)


def swap(value, axis, distance):
    count = lax.axis_size(axis)
    return lax.ppermute(value, axis, [(i, i ^ distance) for i in range(count)])


def halving_plan(rows, cols, steps):
    plan = []
    for _ in range(steps):
        if cols % 256 == 0:
            plan.append(1)
            cols //= 2
        else:
            plan.append(0)
            rows //= 2
    return plan


def tree_sum(value):
    shape = value.shape
    cells = value.reshape(-1, shape[-1])
    stages = []
    for axis in ("rep", "seq"):
        distance = 1
        while distance < lax.axis_size(axis):
            stages.append((axis, distance))
            distance *= 2
    plan = halving_plan(cells.shape[0], cells.shape[1], len(stages))
    held = cells
    for (axis, distance), dim in zip(stages, plan):
        bit = (lax.axis_index(axis) // distance) % 2
        size = held.shape[dim] // 2
        keep = lax.dynamic_slice_in_dim(held, bit * size, size, axis=dim)
        give = lax.dynamic_slice_in_dim(held, (1 - bit) * size, size, axis=dim)
        held = keep + swap(give, axis, distance)
    for (axis, distance), dim in reversed(list(zip(stages, plan))):
        bit = (lax.axis_index(axis) // distance) % 2
        size = held.shape[dim]
        other = swap(held, axis, distance)
        full = jnp.concatenate([held, held], axis=dim)
        full = lax.dynamic_update_slice_in_dim(full, held, bit * size, axis=dim)
        held = lax.dynamic_update_slice_in_dim(full, other, (1 - bit) * size, axis=dim)
    return held.reshape(shape)


def ring_order(mesh):
    count = mesh.shape["seq"]
    names = mesh.axis_names
    index = [0] * len(names)
    cells = []
    for s in range(count):
        index[names.index("seq")] = s
        coords = getattr(mesh.devices[tuple(index)], "coords", None)
        if coords is None:
            return False
        cells.append((tuple(coords), s))
    cells.sort(key=lambda cell: (cell[0][1], cell[0][2] if cell[0][1] % 2 == 0 else -cell[0][2]))
    half = count // 2
    snake = [2 * p if p < half else 2 * (count - 1 - p) + 1 for p in range(count)]
    return count % 2 == 0 and [s for _, s in cells] == snake


def ring_reduce_scatter(blocks, snake):
    count = blocks.shape[0]
    half_count = count // 2
    if snake:
        ring = [2 * p if p < half_count else 2 * (count - 1 - p) + 1 for p in range(count)]
    else:
        ring = list(range(count))
    seq_index = lax.axis_index("seq")
    if snake:
        here = jnp.where(seq_index % 2 == 0, seq_index // 2, count - 1 - seq_index // 2)
    else:
        here = seq_index
    cols = blocks.shape[2] // 2
    forward = [(ring[i], ring[(i + 1) % count]) for i in range(count)]
    backward = [(ring[i], ring[(i - 1) % count]) for i in range(count)]

    def block(offset, low):
        spot = (here + offset + count) % count
        if snake:
            owner = jnp.where(spot < half_count, 2 * spot, 2 * (count - 1 - spot) + 1)
        else:
            owner = spot
        rows = lax.dynamic_index_in_dim(blocks, owner, axis=0, keepdims=False)
        return rows[:, :cols] if low else rows[:, cols:]

    ahead = block(-1, True)
    behind = block(1, False)
    for step in range(count - 1):
        ahead = lax.ppermute(ahead, "seq", forward) + block(-2 - step, True)
        behind = lax.ppermute(behind, "seq", backward) + block(2 + step, False)
    return jnp.concatenate([ahead, behind], axis=1)


def gather_doubling(held):
    stages = [("rep", 1)]
    distance = 1
    while distance < lax.axis_size("seq"):
        stages.append(("seq", distance))
        distance *= 2
    for axis, distance in stages:
        if lax.axis_size(axis) == 1:
            continue
        bit = (lax.axis_index(axis) // distance) % 2
        size = held.shape[0]
        other = swap(held, axis, distance)
        full = jnp.concatenate([held, held], axis=0)
        full = lax.dynamic_update_slice_in_dim(full, held, bit * size, axis=0)
        held = lax.dynamic_update_slice_in_dim(full, other, (1 - bit) * size, axis=0)
    return held


def point_gradient(act_rows, cot_rows, conv_local, scale, snake):
    chans = act_rows.shape[1]
    seq_count = lax.axis_size("seq")
    rep_count = lax.axis_size("rep")
    product = lambda a, b: lax.dot_general(
        a, b, (((0,), (0,)), ((), ())), preferred_element_type=jnp.float32
    ) * scale
    if rep_count != 2:
        partial = product(act_rows, cot_rows)
        total = lax.psum_scatter(partial, ("seq", "rep"), scatter_dimension=0, tiled=True)
        conv = lax.psum(conv_local, ("seq", "rep")) * scale
        return total, conv
    devices = seq_count * rep_count
    block = chans // devices
    blocks = act_rows.reshape(act_rows.shape[0], seq_count, rep_count, block)
    conv_rows = conv_local.reshape(-1, chans) * scale
    conv_count = conv_rows.shape[0]
    share = -(-conv_count // devices)
    conv_rows = jnp.pad(conv_rows, ((0, share * devices - conv_count), (0, 0)))
    conv_cells = conv_rows.reshape(seq_count, rep_count, share, chans)
    rep_index = lax.axis_index("rep")

    def rows_of(owner):
        cols = lax.dynamic_index_in_dim(blocks, owner, axis=2, keepdims=False)
        cols = cols.reshape(act_rows.shape[0], seq_count * block)
        point = product(cols, cot_rows).reshape(seq_count, block, chans)
        conv = lax.dynamic_index_in_dim(conv_cells, owner, axis=1, keepdims=False)
        return jnp.concatenate([point, conv], axis=1)

    mine = rows_of(rep_index) + swap(rows_of(1 - rep_index), "rep", 1)
    summed = ring_reduce_scatter(mine, snake)
    conv = gather_doubling(summed[block:])
    return summed[:block], conv[:conv_count].reshape(conv_local.shape)


def on_device(snake, inputs, lengths, conv_weight, point_weight, cotangent):
    local_bins = inputs.shape[1]
    chans = inputs.shape[2]
    seq_count = lax.axis_size("seq")
    rep_count = lax.axis_size("rep")
    seq_index = lax.axis_index("seq")
    positions = seq_index * local_bins + jnp.arange(local_bins, dtype=jnp.int32)
    mask = (positions[None, :] < lengths[:, None]).astype(jnp.float32)
    mask3 = mask[:, :, None]
    masked_input = (inputs.astype(jnp.float32) * mask3).astype(jnp.bfloat16)
    scale = 1.0 / math.sqrt(rep_count * seq_count * local_bins)
    padded_input = with_halo(masked_input, (("seq", 1),), DILATION_STEP)
    dense = dense_weight(conv_weight)
    pre = conv_taps(padded_input, dense, local_bins)
    act_val, slope = gelu_pair(pre)
    act = (act_val * mask3).astype(jnp.bfloat16)
    act_rows = act.reshape(local_bins, chans)
    cot_rows = cotangent.reshape(local_bins, chans)
    proj = jnp.dot(act_rows, point_weight, preferred_element_type=jnp.float32).reshape(inputs.shape)
    output = (inputs.astype(jnp.float32) + proj).astype(jnp.bfloat16)
    back = lax.dot_general(
        cot_rows, point_weight, (((1,), (1,)), ((), ())), preferred_element_type=jnp.float32
    )
    preactivation_gradient = (back.reshape(inputs.shape) * slope * mask3).astype(jnp.bfloat16)
    padded_gradient = with_halo(preactivation_gradient, (("seq", 1),), DILATION_STEP)
    spread = conv_taps(padded_gradient, dense, local_bins, transpose=True)
    conv_local = weight_taps(padded_input, preactivation_gradient, local_bins)
    grad_point, grad_conv = point_gradient(act_rows, cot_rows, conv_local, scale, snake)
    grad_inputs = (cotangent.astype(jnp.float32) + mask3 * spread).astype(jnp.bfloat16)
    return (output, grad_inputs, grad_point, grad_conv)


def solution(mesh):
    return jax.shard_map(
        functools.partial(on_device, ring_order(mesh)),
        mesh=mesh,
        in_specs=(
            P(("groups", "rep"), "seq", None),
            P(("groups", "rep")),
            P(),
            P(),
            P(("groups", "rep"), "seq", None),
        ),
        out_specs=(
            P(("groups", "rep"), "seq", None),
            P(("groups", "rep"), "seq", None),
            P(("groups", "seq", "rep"), None),
            P("groups", None, None),
        ),
        check_vma=False,
    )
```

```python
import functools
import math

import jax
import jax.numpy as jnp
from jax import lax
from jax.sharding import PartitionSpec as P

GROUP_CHANNELS = 48
DILATION_STEP = 64


def with_halo(cells, sides, width):
    for axis, dim in sides:
        count = lax.axis_size(axis)
        ends = count - 1
        head = lax.slice_in_dim(cells, 0, width, axis=dim)
        tail = lax.slice_in_dim(cells, cells.shape[dim] - width, cells.shape[dim], axis=dim)
        cells = jnp.concatenate(
            [
                lax.ppermute(tail, axis, [(i, (i + 1) % count) for i in range(ends)]),
                cells,
                lax.ppermute(head, axis, [((i + 1) % count, i) for i in range(ends)]),
            ],
            axis=dim,
        )
    return cells


def gelu_pair(pre):
    cdf = 0.5 * (1.0 + jax.scipy.special.erf(pre * 0.7071067811865476))
    dens = jnp.exp(-0.5 * pre * pre) * 0.3989422804014327
    return (pre * cdf, cdf + pre * dens)


CHUNK = 384


def group_mask(rows, chans, dtype):
    row_group = lax.broadcasted_iota(jnp.int32, (rows, chans), 0) // GROUP_CHANNELS
    col_group = (lax.broadcasted_iota(jnp.int32, (rows, chans), 1) % CHUNK) // GROUP_CHANNELS
    return (row_group == col_group).astype(dtype)


def dense_weight(weight):
    taps, width, chans = weight.shape
    groups = CHUNK // width
    tiled = jnp.tile(weight, (1, groups, 1))
    return tiled * group_mask(CHUNK, chans, weight.dtype)[None]


def conv_taps(padded_input, dense, sequence_length, transpose=False):
    rows = padded_input[0]
    chunks = dense.shape[2] // CHUNK
    parts = []
    for c in range(chunks):
        cols = slice(c * CHUNK, (c + 1) * CHUNK)
        total = None
        for k in range(3):
            start = (2 - k if transpose else k) * DILATION_STEP
            window = rows[start : start + sequence_length, cols]
            dims = (((1,), (1,)), ((), ())) if transpose else (((1,), (0,)), ((), ()))
            term = lax.dot_general(
                window, dense[k, :, cols], dims, preferred_element_type=jnp.float32
            )
            total = term if total is None else total + term
        parts.append(total)
    return jnp.concatenate(parts, axis=1)[None]


def weight_taps(input_padded, output_gradient, sequence_length):
    rows = input_padded[0]
    grads = output_gradient[0]
    chans = grads.shape[1]
    chunks = chans // CHUNK
    groups = CHUNK // GROUP_CHANNELS
    mask = group_mask(CHUNK, CHUNK, jnp.float32).reshape(groups, GROUP_CHANNELS, CHUNK)
    taps = []
    for k in range(3):
        parts = []
        for c in range(chunks):
            cols = slice(c * CHUNK, (c + 1) * CHUNK)
            window = rows[k * DILATION_STEP : k * DILATION_STEP + sequence_length, cols]
            full = lax.dot_general(
                window, grads[:, cols], (((0,), (0,)), ((), ())),
                preferred_element_type=jnp.float32,
            ).reshape(groups, GROUP_CHANNELS, CHUNK)
            parts.append(jnp.sum(full * mask, axis=0))
        taps.append(jnp.concatenate(parts, axis=1))
    return jnp.stack(taps)


def swap(value, axis, distance):
    count = lax.axis_size(axis)
    return lax.ppermute(value, axis, [(i, i ^ distance) for i in range(count)])


def halving_plan(rows, cols, steps):
    plan = []
    for _ in range(steps):
        if cols % 256 == 0:
            plan.append(1)
            cols //= 2
        else:
            plan.append(0)
            rows //= 2
    return plan


def tree_sum(value):
    shape = value.shape
    cells = value.reshape(-1, shape[-1])
    stages = []
    for axis in ("rep", "seq"):
        distance = 1
        while distance < lax.axis_size(axis):
            stages.append((axis, distance))
            distance *= 2
    plan = halving_plan(cells.shape[0], cells.shape[1], len(stages))
    held = cells
    for (axis, distance), dim in zip(stages, plan):
        bit = (lax.axis_index(axis) // distance) % 2
        size = held.shape[dim] // 2
        keep = lax.dynamic_slice_in_dim(held, bit * size, size, axis=dim)
        give = lax.dynamic_slice_in_dim(held, (1 - bit) * size, size, axis=dim)
        held = keep + swap(give, axis, distance)
    for (axis, distance), dim in reversed(list(zip(stages, plan))):
        bit = (lax.axis_index(axis) // distance) % 2
        size = held.shape[dim]
        other = swap(held, axis, distance)
        full = jnp.concatenate([held, held], axis=dim)
        full = lax.dynamic_update_slice_in_dim(full, held, bit * size, axis=dim)
        held = lax.dynamic_update_slice_in_dim(full, other, (1 - bit) * size, axis=dim)
    return held.reshape(shape)


def ring_order(mesh):
    count = mesh.shape["seq"]
    names = mesh.axis_names
    index = [0] * len(names)
    cells = []
    for s in range(count):
        index[names.index("seq")] = s
        coords = getattr(mesh.devices[tuple(index)], "coords", None)
        if coords is None:
            return False
        cells.append((tuple(coords), s))
    cells.sort(key=lambda cell: (cell[0][1], cell[0][2] if cell[0][1] % 2 == 0 else -cell[0][2]))
    half = count // 2
    snake = [2 * p if p < half else 2 * (count - 1 - p) + 1 for p in range(count)]
    return count % 2 == 0 and [s for _, s in cells] == snake


def ring_reduce_scatter(blocks, snake, hold=None):
    count = blocks.shape[0]
    half_count = count // 2
    if snake:
        ring = [2 * p if p < half_count else 2 * (count - 1 - p) + 1 for p in range(count)]
    else:
        ring = list(range(count))
    seq_index = lax.axis_index("seq")
    if snake:
        here = jnp.where(seq_index % 2 == 0, seq_index // 2, count - 1 - seq_index // 2)
    else:
        here = seq_index
    cols = blocks.shape[2] // 2
    forward = [(ring[i], ring[(i + 1) % count]) for i in range(count)]
    backward = [(ring[i], ring[(i - 1) % count]) for i in range(count)]

    def block(offset, low):
        spot = (here + offset + count) % count
        if snake:
            owner = jnp.where(spot < half_count, 2 * spot, 2 * (count - 1 - spot) + 1)
        else:
            owner = spot
        rows = lax.dynamic_index_in_dim(blocks, owner, axis=0, keepdims=False)
        return rows[:, :cols] if low else rows[:, cols:]

    ahead = block(-1, True)
    behind = block(1, False)
    for step in range(count - 1):
        ahead = lax.ppermute(ahead, "seq", forward) + block(-2 - step, True)
        behind = lax.ppermute(behind, "seq", backward) + block(2 + step, False)
        if step == 0 and hold is not None:
            ahead, behind, hold = lax.optimization_barrier((ahead, behind, hold))
    return jnp.concatenate([ahead, behind], axis=1), hold


def point_gradient(act_rows, cot_rows, scale, snake, hold):
    chans = act_rows.shape[1]
    seq_count = lax.axis_size("seq")
    rep_count = lax.axis_size("rep")
    product = lambda a, b: lax.dot_general(
        a, b, (((0,), (0,)), ((), ())), preferred_element_type=jnp.float32
    ) * scale
    if rep_count != 2:
        partial = product(act_rows, cot_rows)
        total = lax.psum_scatter(partial, ("seq", "rep"), scatter_dimension=0, tiled=True)
        return total, hold
    block = chans // (seq_count * rep_count)
    blocks = act_rows.reshape(act_rows.shape[0], seq_count, rep_count, block)
    rep_index = lax.axis_index("rep")

    def rows_of(owner):
        cols = lax.dynamic_index_in_dim(blocks, owner, axis=2, keepdims=False)
        cols = cols.reshape(act_rows.shape[0], seq_count * block)
        return product(cols, cot_rows).reshape(seq_count, block, chans)

    mine = rows_of(rep_index) + swap(rows_of(1 - rep_index), "rep", 1)
    return ring_reduce_scatter(mine, snake, hold)


def on_device(snake, inputs, lengths, conv_weight, point_weight, cotangent):
    local_bins = inputs.shape[1]
    chans = inputs.shape[2]
    seq_count = lax.axis_size("seq")
    rep_count = lax.axis_size("rep")
    seq_index = lax.axis_index("seq")
    positions = seq_index * local_bins + jnp.arange(local_bins, dtype=jnp.int32)
    mask = (positions[None, :] < lengths[:, None]).astype(jnp.float32)
    mask3 = mask[:, :, None]
    masked_input = (inputs.astype(jnp.float32) * mask3).astype(jnp.bfloat16)
    scale = 1.0 / math.sqrt(rep_count * seq_count * local_bins)
    padded_input = with_halo(masked_input, (("seq", 1),), DILATION_STEP)
    dense = dense_weight(conv_weight)
    pre = conv_taps(padded_input, dense, local_bins)
    act_val, slope = gelu_pair(pre)
    act = (act_val * mask3).astype(jnp.bfloat16)
    act_rows = act.reshape(local_bins, chans)
    cot_rows = cotangent.reshape(local_bins, chans)
    proj = jnp.dot(act_rows, point_weight, preferred_element_type=jnp.float32).reshape(inputs.shape)
    output = (inputs.astype(jnp.float32) + proj).astype(jnp.bfloat16)
    back = lax.dot_general(
        cot_rows, point_weight, (((1,), (1,)), ((), ())), preferred_element_type=jnp.float32
    )
    preactivation_gradient = (back.reshape(inputs.shape) * slope * mask3).astype(jnp.bfloat16)
    grad_point, preactivation_gradient = point_gradient(
        act_rows, cot_rows, scale, snake, preactivation_gradient
    )
    padded_gradient = with_halo(preactivation_gradient, (("seq", 1),), DILATION_STEP)
    spread = conv_taps(padded_gradient, dense, local_bins, transpose=True)
    conv_local = weight_taps(padded_input, preactivation_gradient, local_bins)
    grad_conv = tree_sum(conv_local) * scale
    grad_inputs = (cotangent.astype(jnp.float32) + mask3 * spread).astype(jnp.bfloat16)
    return (output, grad_inputs, grad_point, grad_conv)


def solution(mesh):
    return jax.shard_map(
        functools.partial(on_device, ring_order(mesh)),
        mesh=mesh,
        in_specs=(
            P(("groups", "rep"), "seq", None),
            P(("groups", "rep")),
            P(),
            P(),
            P(("groups", "rep"), "seq", None),
        ),
        out_specs=(
            P(("groups", "rep"), "seq", None),
            P(("groups", "rep"), "seq", None),
            P(("groups", "seq", "rep"), None),
            P("groups", None, None),
        ),
        check_vma=False,
    )
```

```python
import functools
import math

import jax
import jax.numpy as jnp
from jax import lax
from jax.sharding import PartitionSpec as P

GROUP_CHANNELS = 48
DILATION_STEP = 64


def with_halo(cells, sides, width):
    for axis, dim in sides:
        count = lax.axis_size(axis)
        ends = count - 1
        head = lax.slice_in_dim(cells, 0, width, axis=dim)
        tail = lax.slice_in_dim(cells, cells.shape[dim] - width, cells.shape[dim], axis=dim)
        cells = jnp.concatenate(
            [
                lax.ppermute(tail, axis, [(i, (i + 1) % count) for i in range(ends)]),
                cells,
                lax.ppermute(head, axis, [((i + 1) % count, i) for i in range(ends)]),
            ],
            axis=dim,
        )
    return cells


def gelu_pair(pre):
    cdf = 0.5 * (1.0 + jax.scipy.special.erf(pre * 0.7071067811865476))
    dens = jnp.exp(-0.5 * pre * pre) * 0.3989422804014327
    return (pre * cdf, cdf + pre * dens)


CHUNK = 384


def group_mask(rows, chans, dtype):
    row_group = lax.broadcasted_iota(jnp.int32, (rows, chans), 0) // GROUP_CHANNELS
    col_group = (lax.broadcasted_iota(jnp.int32, (rows, chans), 1) % CHUNK) // GROUP_CHANNELS
    return (row_group == col_group).astype(dtype)


def dense_weight(weight):
    taps, width, chans = weight.shape
    groups = CHUNK // width
    tiled = jnp.tile(weight, (1, groups, 1))
    return tiled * group_mask(CHUNK, chans, weight.dtype)[None]


def conv_taps(padded_input, dense, sequence_length, transpose=False):
    rows = padded_input[0]
    chunks = dense.shape[2] // CHUNK
    parts = []
    for c in range(chunks):
        cols = slice(c * CHUNK, (c + 1) * CHUNK)
        total = None
        for k in range(3):
            start = (2 - k if transpose else k) * DILATION_STEP
            window = rows[start : start + sequence_length, cols]
            dims = (((1,), (1,)), ((), ())) if transpose else (((1,), (0,)), ((), ()))
            term = lax.dot_general(
                window, dense[k, :, cols], dims, preferred_element_type=jnp.float32
            )
            total = term if total is None else total + term
        parts.append(total)
    return jnp.concatenate(parts, axis=1)[None]


def weight_taps(input_padded, output_gradient, sequence_length):
    rows = input_padded[0]
    grads = output_gradient[0]
    chans = grads.shape[1]
    chunks = chans // CHUNK
    groups = CHUNK // GROUP_CHANNELS
    mask = group_mask(CHUNK, CHUNK, jnp.float32).reshape(groups, GROUP_CHANNELS, CHUNK)
    taps = []
    for k in range(3):
        parts = []
        for c in range(chunks):
            cols = slice(c * CHUNK, (c + 1) * CHUNK)
            window = rows[k * DILATION_STEP : k * DILATION_STEP + sequence_length, cols]
            full = lax.dot_general(
                window, grads[:, cols], (((0,), (0,)), ((), ())),
                preferred_element_type=jnp.float32,
            ).reshape(groups, GROUP_CHANNELS, CHUNK)
            parts.append(jnp.sum(full * mask, axis=0))
        taps.append(jnp.concatenate(parts, axis=1))
    return jnp.stack(taps)


def swap(value, axis, distance):
    count = lax.axis_size(axis)
    return lax.ppermute(value, axis, [(i, i ^ distance) for i in range(count)])


def tree_sum(value):
    shape = value.shape
    cells = value.reshape(-1, shape[-1])
    rows, chans = cells.shape
    rep_count = lax.axis_size("rep")
    seq_count = lax.axis_size("seq")
    if rep_count != 2 or chans % 2:
        return lax.psum(value, ("seq", "rep"))
    rep_bit = lax.axis_index("rep")
    half = chans // 2
    keep = lax.dynamic_slice_in_dim(cells, rep_bit * half, half, axis=1)
    give = lax.dynamic_slice_in_dim(cells, (1 - rep_bit) * half, half, axis=1)
    held = keep + swap(give, "rep", 1)
    share = -(-rows // seq_count)
    held = jnp.pad(held, ((0, share * seq_count - rows), (0, 0)))
    pieces = held.reshape(seq_count, share, half)
    here = lax.axis_index("seq")
    total = lax.dynamic_index_in_dim(pieces, here, axis=0, keepdims=False)
    for shift in range(1, seq_count):
        perm = [(i, (i + shift) % seq_count) for i in range(seq_count)]
        piece = lax.dynamic_index_in_dim(pieces, (here + shift) % seq_count, axis=0, keepdims=False)
        total = total + lax.ppermute(piece, "seq", perm)
    gathered = jnp.zeros_like(pieces)
    gathered = lax.dynamic_update_index_in_dim(gathered, total, here, axis=0)
    for shift in range(1, seq_count):
        perm = [(i, (i + shift) % seq_count) for i in range(seq_count)]
        source = (here - shift + seq_count) % seq_count
        gathered = lax.dynamic_update_index_in_dim(
            gathered, lax.ppermute(total, "seq", perm), source, axis=0
        )
    held = gathered.reshape(share * seq_count, half)[:rows]
    other = swap(held, "rep", 1)
    full = jnp.concatenate([held, held], axis=1)
    full = lax.dynamic_update_slice_in_dim(full, held, rep_bit * half, axis=1)
    full = lax.dynamic_update_slice_in_dim(full, other, (1 - rep_bit) * half, axis=1)
    return full.reshape(shape)


def ring_order(mesh):
    count = mesh.shape["seq"]
    names = mesh.axis_names
    index = [0] * len(names)
    cells = []
    for s in range(count):
        index[names.index("seq")] = s
        coords = getattr(mesh.devices[tuple(index)], "coords", None)
        if coords is None:
            return False
        cells.append((tuple(coords), s))
    cells.sort(key=lambda cell: (cell[0][1], cell[0][2] if cell[0][1] % 2 == 0 else -cell[0][2]))
    half = count // 2
    snake = [2 * p if p < half else 2 * (count - 1 - p) + 1 for p in range(count)]
    return count % 2 == 0 and [s for _, s in cells] == snake


def ring_reduce_scatter(blocks, snake):
    count = blocks.shape[0]
    half_count = count // 2
    if snake:
        ring = [2 * p if p < half_count else 2 * (count - 1 - p) + 1 for p in range(count)]
    else:
        ring = list(range(count))
    seq_index = lax.axis_index("seq")
    if snake:
        here = jnp.where(seq_index % 2 == 0, seq_index // 2, count - 1 - seq_index // 2)
    else:
        here = seq_index
    cols = blocks.shape[2] // 2
    forward = [(ring[i], ring[(i + 1) % count]) for i in range(count)]
    backward = [(ring[i], ring[(i - 1) % count]) for i in range(count)]

    def block(offset, low):
        spot = (here + offset + count) % count
        if snake:
            owner = jnp.where(spot < half_count, 2 * spot, 2 * (count - 1 - spot) + 1)
        else:
            owner = spot
        rows = lax.dynamic_index_in_dim(blocks, owner, axis=0, keepdims=False)
        return rows[:, :cols] if low else rows[:, cols:]

    ahead = block(-1, True)
    behind = block(1, False)
    for step in range(count - 1):
        ahead = lax.ppermute(ahead, "seq", forward) + block(-2 - step, True)
        behind = lax.ppermute(behind, "seq", backward) + block(2 + step, False)
    return jnp.concatenate([ahead, behind], axis=1)


def point_gradient(act_rows, cot_rows, scale, snake):
    chans = act_rows.shape[1]
    seq_count = lax.axis_size("seq")
    rep_count = lax.axis_size("rep")
    product = lambda a, b: lax.dot_general(
        a, b, (((0,), (0,)), ((), ())), preferred_element_type=jnp.float32
    ) * scale
    if rep_count != 2:
        partial = product(act_rows, cot_rows)
        partial, cot_rows = lax.optimization_barrier((partial, cot_rows))
        total = lax.psum_scatter(partial, ("seq", "rep"), scatter_dimension=0, tiled=True)
        return total, cot_rows
    block = chans // (seq_count * rep_count)
    blocks = act_rows.reshape(act_rows.shape[0], seq_count, rep_count, block)
    rep_index = lax.axis_index("rep")

    def rows_of(owner):
        cols = lax.dynamic_index_in_dim(blocks, owner, axis=2, keepdims=False)
        cols = cols.reshape(act_rows.shape[0], seq_count * block)
        return product(cols, cot_rows).reshape(seq_count, block, chans)

    mine = rows_of(rep_index) + swap(rows_of(1 - rep_index), "rep", 1)
    mine, cot_rows = lax.optimization_barrier((mine, cot_rows))
    return ring_reduce_scatter(mine, snake), cot_rows


def on_device(snake, inputs, lengths, conv_weight, point_weight, cotangent):
    local_bins = inputs.shape[1]
    chans = inputs.shape[2]
    seq_count = lax.axis_size("seq")
    rep_count = lax.axis_size("rep")
    seq_index = lax.axis_index("seq")
    positions = seq_index * local_bins + jnp.arange(local_bins, dtype=jnp.int32)
    mask = (positions[None, :] < lengths[:, None]).astype(jnp.float32)
    mask3 = mask[:, :, None]
    masked_input = (inputs.astype(jnp.float32) * mask3).astype(jnp.bfloat16)
    scale = 1.0 / math.sqrt(rep_count * seq_count * local_bins)
    padded_input = with_halo(masked_input, (("seq", 1),), DILATION_STEP)
    dense = dense_weight(conv_weight)
    pre = conv_taps(padded_input, dense, local_bins)
    act_val, slope = gelu_pair(pre)
    act = (act_val * mask3).astype(jnp.bfloat16)
    act_rows = act.reshape(local_bins, chans)
    cot_rows = cotangent.reshape(local_bins, chans)
    proj = jnp.dot(act_rows, point_weight, preferred_element_type=jnp.float32).reshape(inputs.shape)
    output = (inputs.astype(jnp.float32) + proj).astype(jnp.bfloat16)
    grad_point, cot_rows = point_gradient(act_rows, cot_rows, scale, snake)
    back = lax.dot_general(
        cot_rows, point_weight, (((1,), (1,)), ((), ())), preferred_element_type=jnp.float32
    )
    preactivation_gradient = (back.reshape(inputs.shape) * slope * mask3).astype(jnp.bfloat16)
    padded_gradient = with_halo(preactivation_gradient, (("seq", 1),), DILATION_STEP)
    spread = conv_taps(padded_gradient, dense, local_bins, transpose=True)
    conv_local = weight_taps(padded_input, preactivation_gradient, local_bins)
    grad_conv = tree_sum(conv_local) * scale
    grad_inputs = (cotangent.astype(jnp.float32) + mask3 * spread).astype(jnp.bfloat16)
    return (output, grad_inputs, grad_point, grad_conv)


def solution(mesh):
    return jax.shard_map(
        functools.partial(on_device, ring_order(mesh)),
        mesh=mesh,
        in_specs=(
            P(("groups", "rep"), "seq", None),
            P(("groups", "rep")),
            P(),
            P(),
            P(("groups", "rep"), "seq", None),
        ),
        out_specs=(
            P(("groups", "rep"), "seq", None),
            P(("groups", "rep"), "seq", None),
            P(("groups", "seq", "rep"), None),
            P("groups", None, None),
        ),
        check_vma=False,
    )
```

```python
import functools
import math

import jax
import jax.numpy as jnp
from jax import lax
from jax.sharding import PartitionSpec as P

GROUP_CHANNELS = 48
DILATION_STEP = 64


def with_halo(cells, sides, width):
    for axis, dim in sides:
        count = lax.axis_size(axis)
        ends = count - 1
        head = lax.slice_in_dim(cells, 0, width, axis=dim)
        tail = lax.slice_in_dim(cells, cells.shape[dim] - width, cells.shape[dim], axis=dim)
        cells = jnp.concatenate(
            [
                lax.ppermute(tail, axis, [(i, (i + 1) % count) for i in range(ends)]),
                cells,
                lax.ppermute(head, axis, [((i + 1) % count, i) for i in range(ends)]),
            ],
            axis=dim,
        )
    return cells


def gelu_pair(pre):
    cdf = 0.5 * (1.0 + jax.scipy.special.erf(pre * 0.7071067811865476))
    dens = jnp.exp(-0.5 * pre * pre) * 0.3989422804014327
    return (pre * cdf, cdf + pre * dens)


CHUNK = 384


def group_mask(rows, chans, dtype):
    row_group = lax.broadcasted_iota(jnp.int32, (rows, chans), 0) // GROUP_CHANNELS
    col_group = (lax.broadcasted_iota(jnp.int32, (rows, chans), 1) % CHUNK) // GROUP_CHANNELS
    return (row_group == col_group).astype(dtype)


def dense_weight(weight):
    taps, width, chans = weight.shape
    groups = CHUNK // width
    tiled = jnp.tile(weight, (1, groups, 1))
    return tiled * group_mask(CHUNK, chans, weight.dtype)[None]


def conv_taps(padded_input, dense, sequence_length, transpose=False):
    rows = padded_input[0]
    chunks = dense.shape[2] // CHUNK
    parts = []
    for c in range(chunks):
        cols = slice(c * CHUNK, (c + 1) * CHUNK)
        total = None
        for k in range(3):
            start = (2 - k if transpose else k) * DILATION_STEP
            window = rows[start : start + sequence_length, cols]
            dims = (((1,), (1,)), ((), ())) if transpose else (((1,), (0,)), ((), ()))
            term = lax.dot_general(
                window, dense[k, :, cols], dims, preferred_element_type=jnp.float32
            )
            total = term if total is None else total + term
        parts.append(total)
    return jnp.concatenate(parts, axis=1)[None]


def weight_taps(input_padded, output_gradient, sequence_length):
    rows = input_padded[0]
    grads = output_gradient[0]
    chans = grads.shape[1]
    chunks = chans // CHUNK
    groups = CHUNK // GROUP_CHANNELS
    mask = group_mask(CHUNK, CHUNK, jnp.float32).reshape(groups, GROUP_CHANNELS, CHUNK)
    taps = []
    for k in range(3):
        parts = []
        for c in range(chunks):
            cols = slice(c * CHUNK, (c + 1) * CHUNK)
            window = rows[k * DILATION_STEP : k * DILATION_STEP + sequence_length, cols]
            full = lax.dot_general(
                window, grads[:, cols], (((0,), (0,)), ((), ())),
                preferred_element_type=jnp.float32,
            ).reshape(groups, GROUP_CHANNELS, CHUNK)
            parts.append(jnp.sum(full * mask, axis=0))
        taps.append(jnp.concatenate(parts, axis=1))
    return jnp.stack(taps)


def swap(value, axis, distance):
    count = lax.axis_size(axis)
    return lax.ppermute(value, axis, [(i, i ^ distance) for i in range(count)])


def halving_plan(rows, cols, steps):
    plan = []
    for _ in range(steps):
        if cols % 256 == 0:
            plan.append(1)
            cols //= 2
        else:
            plan.append(0)
            rows //= 2
    return plan


def tree_sum(value):
    shape = value.shape
    cells = value.reshape(-1, shape[-1])
    stages = []
    for axis in ("rep", "seq"):
        distance = 1
        while distance < lax.axis_size(axis):
            stages.append((axis, distance))
            distance *= 2
    plan = halving_plan(cells.shape[0], cells.shape[1], len(stages))
    held = cells
    for (axis, distance), dim in zip(stages, plan):
        bit = (lax.axis_index(axis) // distance) % 2
        size = held.shape[dim] // 2
        keep = lax.dynamic_slice_in_dim(held, bit * size, size, axis=dim)
        give = lax.dynamic_slice_in_dim(held, (1 - bit) * size, size, axis=dim)
        held = keep + swap(give, axis, distance)
    for (axis, distance), dim in reversed(list(zip(stages, plan))):
        bit = (lax.axis_index(axis) // distance) % 2
        size = held.shape[dim]
        other = swap(held, axis, distance)
        full = jnp.concatenate([held, held], axis=dim)
        full = lax.dynamic_update_slice_in_dim(full, held, bit * size, axis=dim)
        held = lax.dynamic_update_slice_in_dim(full, other, (1 - bit) * size, axis=dim)
    return held.reshape(shape)


def ring_order(mesh):
    count = mesh.shape["seq"]
    names = mesh.axis_names
    index = [0] * len(names)
    cells = []
    for s in range(count):
        index[names.index("seq")] = s
        coords = getattr(mesh.devices[tuple(index)], "coords", None)
        if coords is None:
            return False
        cells.append((tuple(coords), s))
    cells.sort(key=lambda cell: (cell[0][1], cell[0][2] if cell[0][1] % 2 == 0 else -cell[0][2]))
    half = count // 2
    snake = [2 * p if p < half else 2 * (count - 1 - p) + 1 for p in range(count)]
    return count % 2 == 0 and [s for _, s in cells] == snake


def ring_reduce_scatter(blocks, snake, hold):
    count = blocks.shape[0]
    half_count = count // 2
    if snake:
        ring = [2 * p if p < half_count else 2 * (count - 1 - p) + 1 for p in range(count)]
    else:
        ring = list(range(count))
    seq_index = lax.axis_index("seq")
    if snake:
        here = jnp.where(seq_index % 2 == 0, seq_index // 2, count - 1 - seq_index // 2)
    else:
        here = seq_index
    cols = blocks.shape[2] // 2
    forward = [(ring[i], ring[(i + 1) % count]) for i in range(count)]
    backward = [(ring[i], ring[(i - 1) % count]) for i in range(count)]

    def block(offset, low):
        spot = (here + offset + count) % count
        if snake:
            owner = jnp.where(spot < half_count, 2 * spot, 2 * (count - 1 - spot) + 1)
        else:
            owner = spot
        rows = lax.dynamic_index_in_dim(blocks, owner, axis=0, keepdims=False)
        return rows[:, :cols] if low else rows[:, cols:]

    ahead = block(-1, True)
    behind = block(1, False)
    for step in range(count - 1):
        ahead = lax.ppermute(ahead, "seq", forward) + block(-2 - step, True)
        behind = lax.ppermute(behind, "seq", backward) + block(2 + step, False)
        if step == count // 2 - 1:
            ahead, behind, hold = lax.optimization_barrier((ahead, behind, hold))
    return jnp.concatenate([ahead, behind], axis=1), hold


def point_gradient(act_rows, cot_rows, scale):
    chans = act_rows.shape[1]
    seq_count = lax.axis_size("seq")
    rep_count = lax.axis_size("rep")
    product = lambda a, b: lax.dot_general(
        a, b, (((0,), (0,)), ((), ())), preferred_element_type=jnp.float32
    ) * scale
    if rep_count != 2:
        partial = product(act_rows, cot_rows)
        partial, cot_rows = lax.optimization_barrier((partial, cot_rows))
        total = lax.psum_scatter(partial, ("seq", "rep"), scatter_dimension=0, tiled=True)
        return total, cot_rows
    block = chans // (seq_count * rep_count)
    blocks = act_rows.reshape(act_rows.shape[0], seq_count, rep_count, block)
    rep_index = lax.axis_index("rep")

    def rows_of(owner):
        cols = lax.dynamic_index_in_dim(blocks, owner, axis=2, keepdims=False)
        cols = cols.reshape(act_rows.shape[0], seq_count * block)
        return product(cols, cot_rows).reshape(seq_count, block, chans)

    mine = rows_of(rep_index) + swap(rows_of(1 - rep_index), "rep", 1)
    mine, cot_rows = lax.optimization_barrier((mine, cot_rows))
    return mine, cot_rows


def on_device(snake, inputs, lengths, conv_weight, point_weight, cotangent):
    local_bins = inputs.shape[1]
    chans = inputs.shape[2]
    seq_count = lax.axis_size("seq")
    rep_count = lax.axis_size("rep")
    seq_index = lax.axis_index("seq")
    positions = seq_index * local_bins + jnp.arange(local_bins, dtype=jnp.int32)
    mask = (positions[None, :] < lengths[:, None]).astype(jnp.float32)
    mask3 = mask[:, :, None]
    masked_input = (inputs.astype(jnp.float32) * mask3).astype(jnp.bfloat16)
    scale = 1.0 / math.sqrt(rep_count * seq_count * local_bins)
    padded_input = with_halo(masked_input, (("seq", 1),), DILATION_STEP)
    dense = dense_weight(conv_weight)
    pre = conv_taps(padded_input, dense, local_bins)
    act_val, slope = gelu_pair(pre)
    act = (act_val * mask3).astype(jnp.bfloat16)
    act_rows = act.reshape(local_bins, chans)
    cot_rows = cotangent.reshape(local_bins, chans)
    proj = jnp.dot(act_rows, point_weight, preferred_element_type=jnp.float32).reshape(inputs.shape)
    output = (inputs.astype(jnp.float32) + proj).astype(jnp.bfloat16)
    mine, cot_rows = point_gradient(act_rows, cot_rows, scale)
    back = lax.dot_general(
        cot_rows, point_weight, (((1,), (1,)), ((), ())), preferred_element_type=jnp.float32
    )
    preactivation_gradient = (back.reshape(inputs.shape) * slope * mask3).astype(jnp.bfloat16)
    padded_gradient = with_halo(preactivation_gradient, (("seq", 1),), DILATION_STEP)
    spread = conv_taps(padded_gradient, dense, local_bins, transpose=True)
    conv_local = weight_taps(padded_input, preactivation_gradient, local_bins)
    if lax.axis_size("rep") == 2:
        grad_point, conv_local = ring_reduce_scatter(mine, snake, conv_local)
    else:
        grad_point = mine
    grad_conv = tree_sum(conv_local) * scale
    grad_inputs = (cotangent.astype(jnp.float32) + mask3 * spread).astype(jnp.bfloat16)
    return (output, grad_inputs, grad_point, grad_conv)


def solution(mesh):
    return jax.shard_map(
        functools.partial(on_device, ring_order(mesh)),
        mesh=mesh,
        in_specs=(
            P(("groups", "rep"), "seq", None),
            P(("groups", "rep")),
            P(),
            P(),
            P(("groups", "rep"), "seq", None),
        ),
        out_specs=(
            P(("groups", "rep"), "seq", None),
            P(("groups", "rep"), "seq", None),
            P(("groups", "seq", "rep"), None),
            P("groups", None, None),
        ),
        check_vma=False,
    )
```

```python
import functools
import math

import jax
import jax.numpy as jnp
from jax import lax
from jax.sharding import PartitionSpec as P

GROUP_CHANNELS = 48
DILATION_STEP = 64


def with_halo(cells, sides, width):
    for axis, dim in sides:
        count = lax.axis_size(axis)
        ends = count - 1
        head = lax.slice_in_dim(cells, 0, width, axis=dim)
        tail = lax.slice_in_dim(cells, cells.shape[dim] - width, cells.shape[dim], axis=dim)
        cells = jnp.concatenate(
            [
                lax.ppermute(tail, axis, [(i, (i + 1) % count) for i in range(ends)]),
                cells,
                lax.ppermute(head, axis, [((i + 1) % count, i) for i in range(ends)]),
            ],
            axis=dim,
        )
    return cells


def gelu_pair(pre):
    cdf = 0.5 * (1.0 + jax.scipy.special.erf(pre * 0.7071067811865476))
    dens = jnp.exp(-0.5 * pre * pre) * 0.3989422804014327
    return (pre * cdf, cdf + pre * dens)


CHUNK = 384


def group_mask(rows, chans, dtype):
    row_group = lax.broadcasted_iota(jnp.int32, (rows, chans), 0) // GROUP_CHANNELS
    col_group = (lax.broadcasted_iota(jnp.int32, (rows, chans), 1) % CHUNK) // GROUP_CHANNELS
    return (row_group == col_group).astype(dtype)


def dense_weight(weight):
    taps, width, chans = weight.shape
    groups = CHUNK // width
    tiled = jnp.tile(weight, (1, groups, 1))
    return tiled * group_mask(CHUNK, chans, weight.dtype)[None]


def conv_taps(padded_input, dense, sequence_length, transpose=False):
    rows = padded_input[0]
    chunks = dense.shape[2] // CHUNK
    parts = []
    for c in range(chunks):
        cols = slice(c * CHUNK, (c + 1) * CHUNK)
        total = None
        for k in range(3):
            start = (2 - k if transpose else k) * DILATION_STEP
            window = rows[start : start + sequence_length, cols]
            dims = (((1,), (1,)), ((), ())) if transpose else (((1,), (0,)), ((), ()))
            term = lax.dot_general(
                window, dense[k, :, cols], dims, preferred_element_type=jnp.float32
            )
            total = term if total is None else total + term
        parts.append(total)
    return jnp.concatenate(parts, axis=1)[None]


def weight_taps(input_padded, output_gradient, sequence_length):
    rows = input_padded[0]
    grads = output_gradient[0]
    chans = grads.shape[1]
    chunks = chans // CHUNK
    groups = CHUNK // GROUP_CHANNELS
    mask = group_mask(CHUNK, CHUNK, jnp.float32).reshape(groups, GROUP_CHANNELS, CHUNK)
    taps = []
    for k in range(3):
        parts = []
        for c in range(chunks):
            cols = slice(c * CHUNK, (c + 1) * CHUNK)
            window = rows[k * DILATION_STEP : k * DILATION_STEP + sequence_length, cols]
            full = lax.dot_general(
                window, grads[:, cols], (((0,), (0,)), ((), ())),
                preferred_element_type=jnp.float32,
            ).reshape(groups, GROUP_CHANNELS, CHUNK)
            parts.append(jnp.sum(full * mask, axis=0))
        taps.append(jnp.concatenate(parts, axis=1))
    return jnp.stack(taps)


def swap(value, axis, distance):
    count = lax.axis_size(axis)
    return lax.ppermute(value, axis, [(i, i ^ distance) for i in range(count)])


def halving_plan(rows, cols, steps):
    plan = []
    for _ in range(steps):
        if cols % 256 == 0:
            plan.append(1)
            cols //= 2
        else:
            plan.append(0)
            rows //= 2
    return plan


def tree_sum(value):
    shape = value.shape
    cells = value.reshape(-1, shape[-1])
    stages = []
    for axis in ("rep", "seq"):
        distance = 1
        while distance < lax.axis_size(axis):
            stages.append((axis, distance))
            distance *= 2
    plan = halving_plan(cells.shape[0], cells.shape[1], len(stages))
    held = cells
    for (axis, distance), dim in zip(stages, plan):
        bit = (lax.axis_index(axis) // distance) % 2
        size = held.shape[dim] // 2
        keep = lax.dynamic_slice_in_dim(held, bit * size, size, axis=dim)
        give = lax.dynamic_slice_in_dim(held, (1 - bit) * size, size, axis=dim)
        held = keep + swap(give, axis, distance)
    for (axis, distance), dim in reversed(list(zip(stages, plan))):
        bit = (lax.axis_index(axis) // distance) % 2
        size = held.shape[dim]
        other = swap(held, axis, distance)
        full = jnp.concatenate([held, held], axis=dim)
        full = lax.dynamic_update_slice_in_dim(full, held, bit * size, axis=dim)
        held = lax.dynamic_update_slice_in_dim(full, other, (1 - bit) * size, axis=dim)
    return held.reshape(shape)


def ring_order(mesh):
    count = mesh.shape["seq"]
    names = mesh.axis_names
    index = [0] * len(names)
    cells = []
    for s in range(count):
        index[names.index("seq")] = s
        coords = getattr(mesh.devices[tuple(index)], "coords", None)
        if coords is None:
            return False
        cells.append((tuple(coords), s))
    cells.sort(key=lambda cell: (cell[0][1], cell[0][2] if cell[0][1] % 2 == 0 else -cell[0][2]))
    half = count // 2
    snake = [2 * p if p < half else 2 * (count - 1 - p) + 1 for p in range(count)]
    return count % 2 == 0 and [s for _, s in cells] == snake


def ring_reduce_scatter(blocks, snake, hold):
    count = blocks.shape[0]
    half_count = count // 2
    if snake:
        ring = [2 * p if p < half_count else 2 * (count - 1 - p) + 1 for p in range(count)]
    else:
        ring = list(range(count))
    seq_index = lax.axis_index("seq")
    if snake:
        here = jnp.where(seq_index % 2 == 0, seq_index // 2, count - 1 - seq_index // 2)
    else:
        here = seq_index
    cols = blocks.shape[2] // 2
    forward = [(ring[i], ring[(i + 1) % count]) for i in range(count)]
    backward = [(ring[i], ring[(i - 1) % count]) for i in range(count)]

    def block(offset, low):
        spot = (here + offset + count) % count
        if snake:
            owner = jnp.where(spot < half_count, 2 * spot, 2 * (count - 1 - spot) + 1)
        else:
            owner = spot
        rows = lax.dynamic_index_in_dim(blocks, owner, axis=0, keepdims=False)
        return rows[:, :cols] if low else rows[:, cols:]

    ahead = block(-1, True)
    behind = block(1, False)
    for step in range(count - 1):
        ahead = lax.ppermute(ahead, "seq", forward) + block(-2 - step, True)
        behind = lax.ppermute(behind, "seq", backward) + block(2 + step, False)
        if step == 0:
            ahead, behind, hold = lax.optimization_barrier((ahead, behind, hold))
    return jnp.concatenate([ahead, behind], axis=1), hold


def point_gradient(act_rows, cot_rows, scale):
    chans = act_rows.shape[1]
    seq_count = lax.axis_size("seq")
    rep_count = lax.axis_size("rep")
    product = lambda a, b: lax.dot_general(
        a, b, (((0,), (0,)), ((), ())), preferred_element_type=jnp.float32
    ) * scale
    if rep_count != 2:
        partial = product(act_rows, cot_rows)
        partial, cot_rows = lax.optimization_barrier((partial, cot_rows))
        total = lax.psum_scatter(partial, ("seq", "rep"), scatter_dimension=0, tiled=True)
        return total, cot_rows
    block = chans // (seq_count * rep_count)
    blocks = act_rows.reshape(act_rows.shape[0], seq_count, rep_count, block)
    rep_index = lax.axis_index("rep")

    def rows_of(owner):
        cols = lax.dynamic_index_in_dim(blocks, owner, axis=2, keepdims=False)
        cols = cols.reshape(act_rows.shape[0], seq_count * block)
        return product(cols, cot_rows).reshape(seq_count, block, chans)

    mine = rows_of(rep_index) + swap(rows_of(1 - rep_index), "rep", 1)
    mine, cot_rows = lax.optimization_barrier((mine, cot_rows))
    return mine, cot_rows


def on_device(snake, inputs, lengths, conv_weight, point_weight, cotangent):
    local_bins = inputs.shape[1]
    chans = inputs.shape[2]
    seq_count = lax.axis_size("seq")
    rep_count = lax.axis_size("rep")
    seq_index = lax.axis_index("seq")
    positions = seq_index * local_bins + jnp.arange(local_bins, dtype=jnp.int32)
    mask = (positions[None, :] < lengths[:, None]).astype(jnp.float32)
    mask3 = mask[:, :, None]
    masked_input = (inputs.astype(jnp.float32) * mask3).astype(jnp.bfloat16)
    scale = 1.0 / math.sqrt(rep_count * seq_count * local_bins)
    padded_input = with_halo(masked_input, (("seq", 1),), DILATION_STEP)
    dense = dense_weight(conv_weight)
    pre = conv_taps(padded_input, dense, local_bins)
    act_val, slope = gelu_pair(pre)
    act = (act_val * mask3).astype(jnp.bfloat16)
    act_rows = act.reshape(local_bins, chans)
    cot_rows = cotangent.reshape(local_bins, chans)
    proj = jnp.dot(act_rows, point_weight, preferred_element_type=jnp.float32).reshape(inputs.shape)
    output = (inputs.astype(jnp.float32) + proj).astype(jnp.bfloat16)
    mine, cot_rows = point_gradient(act_rows, cot_rows, scale)
    back = lax.dot_general(
        cot_rows, point_weight, (((1,), (1,)), ((), ())), preferred_element_type=jnp.float32
    )
    preactivation_gradient = (back.reshape(inputs.shape) * slope * mask3).astype(jnp.bfloat16)
    if lax.axis_size("rep") == 2:
        grad_point, held_gradient = ring_reduce_scatter(mine, snake, preactivation_gradient)
    else:
        grad_point, held_gradient = mine, preactivation_gradient
    padded_gradient = with_halo(held_gradient, (("seq", 1),), DILATION_STEP)
    spread = conv_taps(padded_gradient, dense, local_bins, transpose=True)
    conv_local = weight_taps(padded_input, preactivation_gradient, local_bins)
    grad_conv = tree_sum(conv_local) * scale
    grad_inputs = (cotangent.astype(jnp.float32) + mask3 * spread).astype(jnp.bfloat16)
    return (output, grad_inputs, grad_point, grad_conv)


def solution(mesh):
    return jax.shard_map(
        functools.partial(on_device, ring_order(mesh)),
        mesh=mesh,
        in_specs=(
            P(("groups", "rep"), "seq", None),
            P(("groups", "rep")),
            P(),
            P(),
            P(("groups", "rep"), "seq", None),
        ),
        out_specs=(
            P(("groups", "rep"), "seq", None),
            P(("groups", "rep"), "seq", None),
            P(("groups", "seq", "rep"), None),
            P("groups", None, None),
        ),
        check_vma=False,
    )
```

```python
import functools
import math

import jax
import jax.numpy as jnp
from jax import lax
from jax.sharding import PartitionSpec as P

GROUP_CHANNELS = 48
DILATION_STEP = 64


def with_halo(cells, sides, width):
    for axis, dim in sides:
        count = lax.axis_size(axis)
        ends = count - 1
        head = lax.slice_in_dim(cells, 0, width, axis=dim)
        tail = lax.slice_in_dim(cells, cells.shape[dim] - width, cells.shape[dim], axis=dim)
        cells = jnp.concatenate(
            [
                lax.ppermute(tail, axis, [(i, (i + 1) % count) for i in range(ends)]),
                cells,
                lax.ppermute(head, axis, [((i + 1) % count, i) for i in range(ends)]),
            ],
            axis=dim,
        )
    return cells


def gelu_pair(pre):
    cdf = 0.5 * (1.0 + jax.scipy.special.erf(pre * 0.7071067811865476))
    dens = jnp.exp(-0.5 * pre * pre) * 0.3989422804014327
    return (pre * cdf, cdf + pre * dens)


CHUNK = 384


def group_mask(rows, chans, dtype):
    row_group = lax.broadcasted_iota(jnp.int32, (rows, chans), 0) // GROUP_CHANNELS
    col_group = (lax.broadcasted_iota(jnp.int32, (rows, chans), 1) % CHUNK) // GROUP_CHANNELS
    return (row_group == col_group).astype(dtype)


def dense_weight(weight):
    taps, width, chans = weight.shape
    groups = CHUNK // width
    tiled = jnp.tile(weight, (1, groups, 1))
    return tiled * group_mask(CHUNK, chans, weight.dtype)[None]


def conv_taps(padded_input, dense, sequence_length, transpose=False):
    rows = padded_input[0]
    chunks = dense.shape[2] // CHUNK
    parts = []
    for c in range(chunks):
        cols = slice(c * CHUNK, (c + 1) * CHUNK)
        total = None
        for k in range(3):
            start = (2 - k if transpose else k) * DILATION_STEP
            window = rows[start : start + sequence_length, cols]
            dims = (((1,), (1,)), ((), ())) if transpose else (((1,), (0,)), ((), ()))
            term = lax.dot_general(
                window, dense[k, :, cols], dims, preferred_element_type=jnp.float32
            )
            total = term if total is None else total + term
        parts.append(total)
    return jnp.concatenate(parts, axis=1)[None]


def weight_taps(input_padded, output_gradient, sequence_length):
    rows = input_padded[0]
    grads = output_gradient[0]
    chans = grads.shape[1]
    chunks = chans // CHUNK
    groups = CHUNK // GROUP_CHANNELS
    mask = group_mask(CHUNK, CHUNK, jnp.float32).reshape(groups, GROUP_CHANNELS, CHUNK)
    taps = []
    for k in range(3):
        parts = []
        for c in range(chunks):
            cols = slice(c * CHUNK, (c + 1) * CHUNK)
            window = rows[k * DILATION_STEP : k * DILATION_STEP + sequence_length, cols]
            full = lax.dot_general(
                window, grads[:, cols], (((0,), (0,)), ((), ())),
                preferred_element_type=jnp.float32,
            ).reshape(groups, GROUP_CHANNELS, CHUNK)
            parts.append(jnp.sum(full * mask, axis=0))
        taps.append(jnp.concatenate(parts, axis=1))
    return jnp.stack(taps)


def swap(value, axis, distance):
    count = lax.axis_size(axis)
    return lax.ppermute(value, axis, [(i, i ^ distance) for i in range(count)])


def halving_plan(rows, cols, steps):
    plan = []
    for _ in range(steps):
        if rows % 16 == 0 or cols % 256:
            plan.append(0)
            rows //= 2
        else:
            plan.append(1)
            cols //= 2
    return plan


def tree_sum(value):
    shape = value.shape
    cells = value.reshape(-1, shape[-1])
    stages = []
    for axis in ("rep", "seq"):
        distance = 1
        while distance < lax.axis_size(axis):
            stages.append((axis, distance))
            distance *= 2
    plan = halving_plan(cells.shape[0], cells.shape[1], len(stages))
    held = cells
    for (axis, distance), dim in zip(stages, plan):
        bit = (lax.axis_index(axis) // distance) % 2
        size = held.shape[dim] // 2
        keep = lax.dynamic_slice_in_dim(held, bit * size, size, axis=dim)
        give = lax.dynamic_slice_in_dim(held, (1 - bit) * size, size, axis=dim)
        held = keep + swap(give, axis, distance)
    for (axis, distance), dim in reversed(list(zip(stages, plan))):
        bit = (lax.axis_index(axis) // distance) % 2
        size = held.shape[dim]
        other = swap(held, axis, distance)
        full = jnp.concatenate([held, held], axis=dim)
        full = lax.dynamic_update_slice_in_dim(full, held, bit * size, axis=dim)
        held = lax.dynamic_update_slice_in_dim(full, other, (1 - bit) * size, axis=dim)
    return held.reshape(shape)


def ring_order(mesh):
    count = mesh.shape["seq"]
    names = mesh.axis_names
    index = [0] * len(names)
    cells = []
    for s in range(count):
        index[names.index("seq")] = s
        coords = getattr(mesh.devices[tuple(index)], "coords", None)
        if coords is None:
            return False
        cells.append((tuple(coords), s))
    cells.sort(key=lambda cell: (cell[0][1], cell[0][2] if cell[0][1] % 2 == 0 else -cell[0][2]))
    half = count // 2
    snake = [2 * p if p < half else 2 * (count - 1 - p) + 1 for p in range(count)]
    return count % 2 == 0 and [s for _, s in cells] == snake


def ring_reduce_scatter(blocks, snake):
    count = blocks.shape[0]
    half_count = count // 2
    if snake:
        ring = [2 * p if p < half_count else 2 * (count - 1 - p) + 1 for p in range(count)]
    else:
        ring = list(range(count))
    seq_index = lax.axis_index("seq")
    if snake:
        here = jnp.where(seq_index % 2 == 0, seq_index // 2, count - 1 - seq_index // 2)
    else:
        here = seq_index
    cols = blocks.shape[2] // 2
    forward = [(ring[i], ring[(i + 1) % count]) for i in range(count)]
    backward = [(ring[i], ring[(i - 1) % count]) for i in range(count)]

    def block(offset, low):
        spot = (here + offset + count) % count
        if snake:
            owner = jnp.where(spot < half_count, 2 * spot, 2 * (count - 1 - spot) + 1)
        else:
            owner = spot
        rows = lax.dynamic_index_in_dim(blocks, owner, axis=0, keepdims=False)
        return rows[:, :cols] if low else rows[:, cols:]

    ahead = block(-1, True)
    behind = block(1, False)
    for step in range(count - 1):
        ahead = lax.ppermute(ahead, "seq", forward) + block(-2 - step, True)
        behind = lax.ppermute(behind, "seq", backward) + block(2 + step, False)
    return jnp.concatenate([ahead, behind], axis=1)


def point_gradient(act_rows, cot_rows, scale, snake):
    chans = act_rows.shape[1]
    seq_count = lax.axis_size("seq")
    rep_count = lax.axis_size("rep")
    product = lambda a, b: lax.dot_general(
        a, b, (((0,), (0,)), ((), ())), preferred_element_type=jnp.float32
    ) * scale
    if rep_count != 2:
        partial = product(act_rows, cot_rows)
        partial, cot_rows = lax.optimization_barrier((partial, cot_rows))
        total = lax.psum_scatter(partial, ("seq", "rep"), scatter_dimension=0, tiled=True)
        return total, cot_rows
    block = chans // (seq_count * rep_count)
    blocks = act_rows.reshape(act_rows.shape[0], seq_count, rep_count, block)
    rep_index = lax.axis_index("rep")

    def rows_of(owner):
        cols = lax.dynamic_index_in_dim(blocks, owner, axis=2, keepdims=False)
        cols = cols.reshape(act_rows.shape[0], seq_count * block)
        return product(cols, cot_rows).reshape(seq_count, block, chans)

    mine = rows_of(rep_index) + swap(rows_of(1 - rep_index), "rep", 1)
    mine, cot_rows = lax.optimization_barrier((mine, cot_rows))
    return ring_reduce_scatter(mine, snake), cot_rows


def on_device(snake, inputs, lengths, conv_weight, point_weight, cotangent):
    local_bins = inputs.shape[1]
    chans = inputs.shape[2]
    seq_count = lax.axis_size("seq")
    rep_count = lax.axis_size("rep")
    seq_index = lax.axis_index("seq")
    positions = seq_index * local_bins + jnp.arange(local_bins, dtype=jnp.int32)
    mask = (positions[None, :] < lengths[:, None]).astype(jnp.float32)
    mask3 = mask[:, :, None]
    masked_input = (inputs.astype(jnp.float32) * mask3).astype(jnp.bfloat16)
    scale = 1.0 / math.sqrt(rep_count * seq_count * local_bins)
    padded_input = with_halo(masked_input, (("seq", 1),), DILATION_STEP)
    dense = dense_weight(conv_weight)
    pre = conv_taps(padded_input, dense, local_bins)
    act_val, slope = gelu_pair(pre)
    act = (act_val * mask3).astype(jnp.bfloat16)
    act_rows = act.reshape(local_bins, chans)
    cot_rows = cotangent.reshape(local_bins, chans)
    proj = jnp.dot(act_rows, point_weight, preferred_element_type=jnp.float32).reshape(inputs.shape)
    output = (inputs.astype(jnp.float32) + proj).astype(jnp.bfloat16)
    grad_point, cot_rows = point_gradient(act_rows, cot_rows, scale, snake)
    back = lax.dot_general(
        cot_rows, point_weight, (((1,), (1,)), ((), ())), preferred_element_type=jnp.float32
    )
    preactivation_gradient = (back.reshape(inputs.shape) * slope * mask3).astype(jnp.bfloat16)
    padded_gradient = with_halo(preactivation_gradient, (("seq", 1),), DILATION_STEP)
    spread = conv_taps(padded_gradient, dense, local_bins, transpose=True)
    conv_local = weight_taps(padded_input, preactivation_gradient, local_bins)
    grad_conv = tree_sum(conv_local) * scale
    grad_inputs = (cotangent.astype(jnp.float32) + mask3 * spread).astype(jnp.bfloat16)
    return (output, grad_inputs, grad_point, grad_conv)


def solution(mesh):
    return jax.shard_map(
        functools.partial(on_device, ring_order(mesh)),
        mesh=mesh,
        in_specs=(
            P(("groups", "rep"), "seq", None),
            P(("groups", "rep")),
            P(),
            P(),
            P(("groups", "rep"), "seq", None),
        ),
        out_specs=(
            P(("groups", "rep"), "seq", None),
            P(("groups", "rep"), "seq", None),
            P(("groups", "seq", "rep"), None),
            P("groups", None, None),
        ),
        check_vma=False,
    )
```

```python
import functools
import math

import jax
import jax.numpy as jnp
from jax import lax
from jax.sharding import PartitionSpec as P

GROUP_CHANNELS = 48
DILATION_STEP = 64


def with_halo(cells, sides, width):
    for axis, dim in sides:
        count = lax.axis_size(axis)
        ends = count - 1
        head = lax.slice_in_dim(cells, 0, width, axis=dim)
        tail = lax.slice_in_dim(cells, cells.shape[dim] - width, cells.shape[dim], axis=dim)
        cells = jnp.concatenate(
            [
                lax.ppermute(tail, axis, [(i, (i + 1) % count) for i in range(ends)]),
                cells,
                lax.ppermute(head, axis, [((i + 1) % count, i) for i in range(ends)]),
            ],
            axis=dim,
        )
    return cells


def gelu_pair(pre):
    cdf = 0.5 * (1.0 + jax.scipy.special.erf(pre * 0.7071067811865476))
    dens = jnp.exp(-0.5 * pre * pre) * 0.3989422804014327
    return (pre * cdf, cdf + pre * dens)


CHUNK = 384


def group_mask(rows, chans, dtype):
    row_group = lax.broadcasted_iota(jnp.int32, (rows, chans), 0) // GROUP_CHANNELS
    col_group = (lax.broadcasted_iota(jnp.int32, (rows, chans), 1) % CHUNK) // GROUP_CHANNELS
    return (row_group == col_group).astype(dtype)


def dense_weight(weight):
    taps, width, chans = weight.shape
    groups = CHUNK // width
    tiled = jnp.tile(weight, (1, groups, 1))
    return tiled * group_mask(CHUNK, chans, weight.dtype)[None]


def conv_taps(padded_input, dense, sequence_length, transpose=False):
    rows = padded_input[0]
    chunks = dense.shape[2] // CHUNK
    parts = []
    for c in range(chunks):
        cols = slice(c * CHUNK, (c + 1) * CHUNK)
        total = None
        for k in range(3):
            start = (2 - k if transpose else k) * DILATION_STEP
            window = rows[start : start + sequence_length, cols]
            dims = (((1,), (1,)), ((), ())) if transpose else (((1,), (0,)), ((), ()))
            term = lax.dot_general(
                window, dense[k, :, cols], dims, preferred_element_type=jnp.float32
            )
            total = term if total is None else total + term
        parts.append(total)
    return jnp.concatenate(parts, axis=1)[None]


def weight_taps(input_padded, output_gradient, sequence_length):
    rows = input_padded[0]
    grads = output_gradient[0]
    chans = grads.shape[1]
    chunks = chans // CHUNK
    groups = CHUNK // GROUP_CHANNELS
    mask = group_mask(CHUNK, CHUNK, jnp.float32).reshape(groups, GROUP_CHANNELS, CHUNK)
    taps = []
    for k in range(3):
        parts = []
        for c in range(chunks):
            cols = slice(c * CHUNK, (c + 1) * CHUNK)
            window = rows[k * DILATION_STEP : k * DILATION_STEP + sequence_length, cols]
            full = lax.dot_general(
                window, grads[:, cols], (((0,), (0,)), ((), ())),
                preferred_element_type=jnp.float32,
            ).reshape(groups, GROUP_CHANNELS, CHUNK)
            parts.append(jnp.sum(full * mask, axis=0))
        taps.append(jnp.concatenate(parts, axis=1))
    return jnp.stack(taps)


def swap(value, axis, distance):
    count = lax.axis_size(axis)
    return lax.ppermute(value, axis, [(i, i ^ distance) for i in range(count)])


def halving_plan(rows, cols, steps):
    plan = []
    for _ in range(steps):
        if rows % 16 == 0 or cols % 256:
            plan.append(0)
            rows //= 2
        else:
            plan.append(1)
            cols //= 2
    return plan


def tree_sum(value):
    shape = value.shape
    cells = value.reshape(-1, shape[-1])
    stages = []
    for axis in ("rep", "seq"):
        distance = 1
        while distance < lax.axis_size(axis):
            stages.append((axis, distance))
            distance *= 2
    plan = halving_plan(cells.shape[0], cells.shape[1], len(stages))
    held = cells
    for (axis, distance), dim in zip(stages, plan):
        bit = (lax.axis_index(axis) // distance) % 2
        size = held.shape[dim] // 2
        keep = lax.dynamic_slice_in_dim(held, bit * size, size, axis=dim)
        give = lax.dynamic_slice_in_dim(held, (1 - bit) * size, size, axis=dim)
        held = keep + swap(give, axis, distance)
    for (axis, distance), dim in reversed(list(zip(stages, plan))):
        bit = (lax.axis_index(axis) // distance) % 2
        size = held.shape[dim]
        other = swap(held, axis, distance)
        full = jnp.concatenate([held, held], axis=dim)
        full = lax.dynamic_update_slice_in_dim(full, held, bit * size, axis=dim)
        held = lax.dynamic_update_slice_in_dim(full, other, (1 - bit) * size, axis=dim)
    return held.reshape(shape)


def ring_order(mesh):
    count = mesh.shape["seq"]
    names = mesh.axis_names
    index = [0] * len(names)
    cells = []
    for s in range(count):
        index[names.index("seq")] = s
        coords = getattr(mesh.devices[tuple(index)], "coords", None)
        if coords is None:
            return False
        cells.append((tuple(coords), s))
    cells.sort(key=lambda cell: (cell[0][1], cell[0][2] if cell[0][1] % 2 == 0 else -cell[0][2]))
    half = count // 2
    snake = [2 * p if p < half else 2 * (count - 1 - p) + 1 for p in range(count)]
    return count % 2 == 0 and [s for _, s in cells] == snake


def ring_reduce_scatter(blocks, snake):
    count = blocks.shape[0]
    half_count = count // 2
    if snake:
        ring = [2 * p if p < half_count else 2 * (count - 1 - p) + 1 for p in range(count)]
    else:
        ring = list(range(count))
    seq_index = lax.axis_index("seq")
    if snake:
        here = jnp.where(seq_index % 2 == 0, seq_index // 2, count - 1 - seq_index // 2)
    else:
        here = seq_index
    cols = blocks.shape[2] // 2
    forward = [(ring[i], ring[(i + 1) % count]) for i in range(count)]
    backward = [(ring[i], ring[(i - 1) % count]) for i in range(count)]

    def block(offset, low):
        spot = (here + offset + count) % count
        if snake:
            owner = jnp.where(spot < half_count, 2 * spot, 2 * (count - 1 - spot) + 1)
        else:
            owner = spot
        rows = lax.dynamic_index_in_dim(blocks, owner, axis=0, keepdims=False)
        return rows[:, :cols] if low else rows[:, cols:]

    ahead = block(-1, True)
    behind = block(1, False)
    for step in range(count - 1):
        ahead = lax.ppermute(ahead, "seq", forward) + block(-2 - step, True)
        behind = lax.ppermute(behind, "seq", backward) + block(2 + step, False)
    return jnp.concatenate([ahead, behind], axis=1)


def point_gradient(act_rows, cot_rows, scale, snake, slope):
    chans = act_rows.shape[1]
    seq_count = lax.axis_size("seq")
    rep_count = lax.axis_size("rep")
    product = lambda a, b: lax.dot_general(
        a, b, (((0,), (0,)), ((), ())), preferred_element_type=jnp.float32
    ) * scale
    if rep_count != 2:
        partial = product(act_rows, cot_rows)
        partial, slope = lax.optimization_barrier((partial, slope))
        total = lax.psum_scatter(partial, ("seq", "rep"), scatter_dimension=0, tiled=True)
        return total, slope
    block = chans // (seq_count * rep_count)
    blocks = act_rows.reshape(act_rows.shape[0], seq_count, rep_count, block)
    rep_index = lax.axis_index("rep")

    def rows_of(owner):
        cols = lax.dynamic_index_in_dim(blocks, owner, axis=2, keepdims=False)
        cols = cols.reshape(act_rows.shape[0], seq_count * block)
        return product(cols, cot_rows).reshape(seq_count, block, chans)

    mine = rows_of(rep_index) + swap(rows_of(1 - rep_index), "rep", 1)
    mine, slope = lax.optimization_barrier((mine, slope))
    return ring_reduce_scatter(mine, snake), slope


def on_device(snake, inputs, lengths, conv_weight, point_weight, cotangent):
    local_bins = inputs.shape[1]
    chans = inputs.shape[2]
    seq_count = lax.axis_size("seq")
    rep_count = lax.axis_size("rep")
    seq_index = lax.axis_index("seq")
    positions = seq_index * local_bins + jnp.arange(local_bins, dtype=jnp.int32)
    mask = (positions[None, :] < lengths[:, None]).astype(jnp.float32)
    mask3 = mask[:, :, None]
    masked_input = (inputs.astype(jnp.float32) * mask3).astype(jnp.bfloat16)
    scale = 1.0 / math.sqrt(rep_count * seq_count * local_bins)
    padded_input = with_halo(masked_input, (("seq", 1),), DILATION_STEP)
    dense = dense_weight(conv_weight)
    pre = conv_taps(padded_input, dense, local_bins)
    act_val, slope = gelu_pair(pre)
    act = (act_val * mask3).astype(jnp.bfloat16)
    act_rows = act.reshape(local_bins, chans)
    cot_rows = cotangent.reshape(local_bins, chans)
    proj = jnp.dot(act_rows, point_weight, preferred_element_type=jnp.float32).reshape(inputs.shape)
    output = (inputs.astype(jnp.float32) + proj).astype(jnp.bfloat16)
    grad_point, slope = point_gradient(act_rows, cot_rows, scale, snake, slope)
    back = lax.dot_general(
        cot_rows, point_weight, (((1,), (1,)), ((), ())), preferred_element_type=jnp.float32
    )
    preactivation_gradient = (back.reshape(inputs.shape) * slope * mask3).astype(jnp.bfloat16)
    padded_gradient = with_halo(preactivation_gradient, (("seq", 1),), DILATION_STEP)
    spread = conv_taps(padded_gradient, dense, local_bins, transpose=True)
    conv_local = weight_taps(padded_input, preactivation_gradient, local_bins)
    grad_conv = tree_sum(conv_local) * scale
    grad_inputs = (cotangent.astype(jnp.float32) + mask3 * spread).astype(jnp.bfloat16)
    return (output, grad_inputs, grad_point, grad_conv)


def solution(mesh):
    return jax.shard_map(
        functools.partial(on_device, ring_order(mesh)),
        mesh=mesh,
        in_specs=(
            P(("groups", "rep"), "seq", None),
            P(("groups", "rep")),
            P(),
            P(),
            P(("groups", "rep"), "seq", None),
        ),
        out_specs=(
            P(("groups", "rep"), "seq", None),
            P(("groups", "rep"), "seq", None),
            P(("groups", "seq", "rep"), None),
            P("groups", None, None),
        ),
        check_vma=False,
    )
```

```python
import functools
import math

import jax
import jax.numpy as jnp
from jax import lax
from jax.sharding import PartitionSpec as P

GROUP_CHANNELS = 48
DILATION_STEP = 64


def with_halo(cells, sides, width):
    for axis, dim in sides:
        count = lax.axis_size(axis)
        ends = count - 1
        head = lax.slice_in_dim(cells, 0, width, axis=dim)
        tail = lax.slice_in_dim(cells, cells.shape[dim] - width, cells.shape[dim], axis=dim)
        cells = jnp.concatenate(
            [
                lax.ppermute(tail, axis, [(i, (i + 1) % count) for i in range(ends)]),
                cells,
                lax.ppermute(head, axis, [((i + 1) % count, i) for i in range(ends)]),
            ],
            axis=dim,
        )
    return cells


def gelu_pair(pre):
    cdf = 0.5 * (1.0 + jax.scipy.special.erf(pre * 0.7071067811865476))
    dens = jnp.exp(-0.5 * pre * pre) * 0.3989422804014327
    return (pre * cdf, cdf + pre * dens)


CHUNK = 384


def group_mask(rows, chans, dtype):
    row_group = lax.broadcasted_iota(jnp.int32, (rows, chans), 0) // GROUP_CHANNELS
    col_group = (lax.broadcasted_iota(jnp.int32, (rows, chans), 1) % CHUNK) // GROUP_CHANNELS
    return (row_group == col_group).astype(dtype)


def dense_weight(weight):
    taps, width, chans = weight.shape
    groups = CHUNK // width
    tiled = jnp.tile(weight, (1, groups, 1))
    return tiled * group_mask(CHUNK, chans, weight.dtype)[None]


def conv_taps(padded_input, dense, sequence_length, transpose=False):
    rows = padded_input[0]
    chunks = dense.shape[2] // CHUNK
    parts = []
    for c in range(chunks):
        cols = slice(c * CHUNK, (c + 1) * CHUNK)
        total = None
        for k in range(3):
            start = (2 - k if transpose else k) * DILATION_STEP
            window = rows[start : start + sequence_length, cols]
            dims = (((1,), (1,)), ((), ())) if transpose else (((1,), (0,)), ((), ()))
            term = lax.dot_general(
                window, dense[k, :, cols], dims, preferred_element_type=jnp.float32
            )
            total = term if total is None else total + term
        parts.append(total)
    return jnp.concatenate(parts, axis=1)[None]


def weight_taps(input_padded, output_gradient, sequence_length):
    rows = input_padded[0]
    grads = output_gradient[0]
    chans = grads.shape[1]
    chunks = chans // CHUNK
    groups = CHUNK // GROUP_CHANNELS
    mask = group_mask(CHUNK, CHUNK, jnp.float32).reshape(groups, GROUP_CHANNELS, CHUNK)
    taps = []
    for k in range(3):
        parts = []
        for c in range(chunks):
            cols = slice(c * CHUNK, (c + 1) * CHUNK)
            window = rows[k * DILATION_STEP : k * DILATION_STEP + sequence_length, cols]
            full = lax.dot_general(
                window, grads[:, cols], (((0,), (0,)), ((), ())),
                preferred_element_type=jnp.float32,
            ).reshape(groups, GROUP_CHANNELS, CHUNK)
            parts.append(jnp.sum(full * mask, axis=0))
        taps.append(jnp.concatenate(parts, axis=1))
    return jnp.stack(taps)


def swap(value, axis, distance):
    count = lax.axis_size(axis)
    return lax.ppermute(value, axis, [(i, i ^ distance) for i in range(count)])


def halving_plan(rows, cols, steps):
    plan = []
    for _ in range(steps):
        if rows % 16 == 0 or cols % 256:
            plan.append(0)
            rows //= 2
        else:
            plan.append(1)
            cols //= 2
    return plan


def tree_sum(value):
    shape = value.shape
    cells = value.reshape(-1, shape[-1])
    stages = []
    for axis in ("rep", "seq"):
        distance = 1
        while distance < lax.axis_size(axis):
            stages.append((axis, distance))
            distance *= 2
    plan = halving_plan(cells.shape[0], cells.shape[1], len(stages))
    held = cells
    for (axis, distance), dim in zip(stages, plan):
        bit = (lax.axis_index(axis) // distance) % 2
        size = held.shape[dim] // 2
        keep = lax.dynamic_slice_in_dim(held, bit * size, size, axis=dim)
        give = lax.dynamic_slice_in_dim(held, (1 - bit) * size, size, axis=dim)
        held = keep + swap(give, axis, distance)
    for (axis, distance), dim in reversed(list(zip(stages, plan))):
        bit = (lax.axis_index(axis) // distance) % 2
        size = held.shape[dim]
        other = swap(held, axis, distance)
        full = jnp.concatenate([held, held], axis=dim)
        full = lax.dynamic_update_slice_in_dim(full, held, bit * size, axis=dim)
        held = lax.dynamic_update_slice_in_dim(full, other, (1 - bit) * size, axis=dim)
    return held.reshape(shape)


def ring_order(mesh):
    count = mesh.shape["seq"]
    names = mesh.axis_names
    index = [0] * len(names)
    cells = []
    for s in range(count):
        index[names.index("seq")] = s
        coords = getattr(mesh.devices[tuple(index)], "coords", None)
        if coords is None:
            return False
        cells.append((tuple(coords), s))
    cells.sort(key=lambda cell: (cell[0][1], cell[0][2] if cell[0][1] % 2 == 0 else -cell[0][2]))
    half = count // 2
    snake = [2 * p if p < half else 2 * (count - 1 - p) + 1 for p in range(count)]
    return count % 2 == 0 and [s for _, s in cells] == snake


def ring_reduce_scatter(blocks, snake):
    count = blocks.shape[0]
    half_count = count // 2
    if snake:
        ring = [2 * p if p < half_count else 2 * (count - 1 - p) + 1 for p in range(count)]
    else:
        ring = list(range(count))
    seq_index = lax.axis_index("seq")
    if snake:
        here = jnp.where(seq_index % 2 == 0, seq_index // 2, count - 1 - seq_index // 2)
    else:
        here = seq_index
    cols = blocks.shape[2] // 2
    forward = [(ring[i], ring[(i + 1) % count]) for i in range(count)]
    backward = [(ring[i], ring[(i - 1) % count]) for i in range(count)]

    def block(offset, low):
        spot = (here + offset + count) % count
        if snake:
            owner = jnp.where(spot < half_count, 2 * spot, 2 * (count - 1 - spot) + 1)
        else:
            owner = spot
        rows = lax.dynamic_index_in_dim(blocks, owner, axis=0, keepdims=False)
        return rows[:, :cols] if low else rows[:, cols:]

    ahead = block(-1, True)
    behind = block(1, False)
    for step in range(count - 1):
        ahead = lax.ppermute(ahead, "seq", forward) + block(-2 - step, True)
        behind = lax.ppermute(behind, "seq", backward) + block(2 + step, False)
    return jnp.concatenate([ahead, behind], axis=1)


def point_gradient(act_rows, cot_rows, scale, snake):
    chans = act_rows.shape[1]
    seq_count = lax.axis_size("seq")
    rep_count = lax.axis_size("rep")
    product = lambda a, b: lax.dot_general(
        a, b, (((0,), (0,)), ((), ())), preferred_element_type=jnp.float32
    ) * scale
    if rep_count != 2:
        partial = product(act_rows, cot_rows)
        partial, cot_rows = lax.optimization_barrier((partial, cot_rows))
        total = lax.psum_scatter(partial, ("seq", "rep"), scatter_dimension=0, tiled=True)
        return total, cot_rows
    block = chans // (seq_count * rep_count)
    blocks = act_rows.reshape(act_rows.shape[0], seq_count, rep_count, block)
    rep_index = lax.axis_index("rep")

    def rows_of(owner):
        cols = lax.dynamic_index_in_dim(blocks, owner, axis=2, keepdims=False)
        cols = cols.reshape(act_rows.shape[0], seq_count * block)
        return product(cols, cot_rows).reshape(seq_count, block, chans)

    mine = rows_of(rep_index) + swap(rows_of(1 - rep_index), "rep", 1)
    mine, cot_rows = lax.optimization_barrier((mine, cot_rows))
    return ring_reduce_scatter(mine, snake), cot_rows


def on_device(snake, inputs, lengths, conv_weight, point_weight, cotangent):
    local_bins = inputs.shape[1]
    chans = inputs.shape[2]
    seq_count = lax.axis_size("seq")
    rep_count = lax.axis_size("rep")
    seq_index = lax.axis_index("seq")
    positions = seq_index * local_bins + jnp.arange(local_bins, dtype=jnp.int32)
    mask = (positions[None, :] < lengths[:, None]).astype(jnp.float32)
    mask3 = mask[:, :, None]
    scale = 1.0 / math.sqrt(rep_count * seq_count * local_bins)
    spots = seq_index * local_bins - DILATION_STEP + jnp.arange(
        local_bins + 2 * DILATION_STEP, dtype=jnp.int32
    )
    pad_mask = (spots[None, :] < lengths[:, None]).astype(jnp.float32)[:, :, None]
    padded_input = with_halo(inputs, (("seq", 1),), DILATION_STEP)
    padded_input = (padded_input.astype(jnp.float32) * pad_mask).astype(jnp.bfloat16)
    dense = dense_weight(conv_weight)
    pre = conv_taps(padded_input, dense, local_bins)
    act_val, slope = gelu_pair(pre)
    act = (act_val * mask3).astype(jnp.bfloat16)
    act_rows = act.reshape(local_bins, chans)
    cot_rows = cotangent.reshape(local_bins, chans)
    proj = jnp.dot(act_rows, point_weight, preferred_element_type=jnp.float32).reshape(inputs.shape)
    output = (inputs.astype(jnp.float32) + proj).astype(jnp.bfloat16)
    grad_point, cot_rows = point_gradient(act_rows, cot_rows, scale, snake)
    back = lax.dot_general(
        cot_rows, point_weight, (((1,), (1,)), ((), ())), preferred_element_type=jnp.float32
    )
    preactivation_gradient = (back.reshape(inputs.shape) * slope * mask3).astype(jnp.bfloat16)
    padded_gradient = with_halo(preactivation_gradient, (("seq", 1),), DILATION_STEP)
    spread = conv_taps(padded_gradient, dense, local_bins, transpose=True)
    conv_local = weight_taps(padded_input, preactivation_gradient, local_bins)
    grad_conv = tree_sum(conv_local) * scale
    grad_inputs = (cotangent.astype(jnp.float32) + mask3 * spread).astype(jnp.bfloat16)
    return (output, grad_inputs, grad_point, grad_conv)


def solution(mesh):
    return jax.shard_map(
        functools.partial(on_device, ring_order(mesh)),
        mesh=mesh,
        in_specs=(
            P(("groups", "rep"), "seq", None),
            P(("groups", "rep")),
            P(),
            P(),
            P(("groups", "rep"), "seq", None),
        ),
        out_specs=(
            P(("groups", "rep"), "seq", None),
            P(("groups", "rep"), "seq", None),
            P(("groups", "seq", "rep"), None),
            P("groups", None, None),
        ),
        check_vma=False,
    )
```
